32 devices in a mesh: groups: 2 (over y), corr: 4 (over z), filt: 2 (over x), pair: 2 (over core).
Axes of the slice: x: 2, y: 2, z: 4, core: 2. Of those that a mesh axis runs over, the one named last changes fastest.
Arguments:
- raw_rows: bfloat16 [4, 32, 3, 16384], P(('groups', 'pair'), 'filt', None, 'corr'), parts along dimension 0, may hold values from -6 to 6
- valid_counts: int32 [4, 32], P(('groups', 'pair'), 'filt'), parts along dimension 0, may hold values from 4096 to 16384
- taps: bfloat16 [64], replicated, may hold values from -0.75 to 0.75
- templates: bfloat16 [128, 225], P('corr'), may hold values from -6 to 6
- masks: int32 [128, 3, 32], replicated, may hold values 0 or 1
Outputs:
- stack: float32 [4, 128, 4096], P(('groups', 'pair'), 'corr', 'filt'), parts along dimension 0
The draws below stay inside these ranges and needn't reach their ends.
There are 2 independent parts, one for each index of `groups`. The reference program is written for one: setup_inputs(seed, part) draws one part's arguments, and reference() takes and returns one part's arrays. A program takes and returns all parts, laid end to end along the dimension named above; an argument that names none is the same for every part. Nothing has to cross between parts.
All inputs are finite; a program needn't handle non-finite values.
Results may differ from the reference program's by a relative error of at most 0.0051.
Values may be sent and summed in bfloat16 or wider, within the bound.
No kernel may reach another device: no remote copies, remote signals or barrier semaphores. Data moves between devices by JAX's collectives and lax.ppermute only.
A program may use at most 192 MiB of HBM per device.

```python
import jax
import jax.numpy as jnp
from jax import lax

S = 32
K = 128
L = 75
TAPS = 64
DEC = 4
TDH = 4096
TRH = 16384
WINDOWS = 2


def draw_valid_counts(key, part):
    drawn = jax.random.randint(key, (WINDOWS, S), TRH // 4, 2 * TRH, dtype=jnp.int32)
    return jnp.minimum(drawn, TRH).astype(jnp.int32)


def with_ends(array, own_key, smallest, top_value):
    dims = array.shape
    place = [jax.random.randint(jax.random.fold_in(own_key, axis), (), 0, dims[axis]) for axis in range(len(dims))]
    array = array.at[tuple(place)].set(smallest)
    longest = dims.index(max(dims))
    place[longest] = (place[longest] + 1) % dims[longest]
    return array.at[tuple(place)].set(top_value)


def levels(stream_key, dims, cuts, smallest, top_value):
    def one(axis_at, blocks):
        draws = jax.random.uniform(jax.random.fold_in(jax.random.fold_in(stream_key, 6), axis_at), (blocks,), jnp.float32, smallest / len(cuts), top_value / len(cuts))
        return jnp.repeat(jnp.exp(draws), dims[axis_at] // blocks).reshape((-1,) + (1,) * (len(dims) - axis_at - 1))

    gain = one(*cuts[0])
    for cut in cuts[1:]:
        gain = gain * one(*cut)
    return gain


def noise(key, extent, deviation, bound, pieces=(), kind=jnp.bfloat16):
    values = jax.random.normal(key, extent, jnp.float32) * deviation
    if len(pieces) > 0:
        values = levels(key, extent, pieces, -0.22, 0.18) * values
    return jnp.clip(values, min=-bound, max=bound).astype(kind)


def setup_inputs(seed: int = 0, part: int = 0) -> dict:
    keys = jax.random.split(jax.random.key(seed), 6)
    part_keys = jax.random.split(jax.random.fold_in(keys[5], part), 6)
    return {
        "raw_rows": noise(part_keys[0], (WINDOWS, S, 3, TRH), 1.0, 6.0, ((0, 2), (1, 2), (3, 4))),
        "valid_counts": draw_valid_counts(jax.random.fold_in(jax.random.fold_in(keys[5], part), 71), part),
        "taps": noise(keys[2], (TAPS,), TAPS ** -0.5, 0.75),
        "templates": noise(keys[3], (K, 3 * L), 1.0, 6.0, ((0, 4),)),
        "masks": with_ends((jax.random.randint(keys[4], (K, 3, S), 0, 2) < 1).astype(jnp.int32), jax.random.fold_in(keys[4], 1), 0, 1),
    }


def one_window(raw_window, counts_window, base, mask_by_station, tap_values):
    phases = TAPS // DEC
    time_index = jnp.arange(TRH, dtype=jnp.int32)

    def station(accum, inputs):
        samples, count, station_mask = inputs
        live = jnp.where(time_index[None, :] < count, samples, jnp.zeros_like(samples))
        extended = jnp.concatenate([jnp.zeros((3, TAPS - 1), samples.dtype), live], axis=1)
        blocks = extended[:, :DEC * (TDH + phases - 1)].reshape(3, TDH + phases - 1, DEC)
        blocks = jnp.transpose(blocks, (0, 2, 1))
        frames = jnp.stack([blocks[:, DEC - 1 - tap % DEC, phases - 1 - tap // DEC:phases - 1 - tap // DEC + TDH] for tap in range(TAPS)], axis=1)
        filtered = jnp.einsum('cid,i->cd', frames.astype(jnp.float32), tap_values).astype(jnp.bfloat16)
        padded = jnp.concatenate([filtered, jnp.zeros((3, L - 1), filtered.dtype)], axis=1)
        slices = jnp.stack([padded[:, lag:lag + TDH] for lag in range(L)], axis=1).astype(jnp.float32)
        energy = lax.optimization_barrier(jnp.sum(slices * slices, axis=1))
        scaled = (slices / jnp.sqrt(jnp.maximum(energy, 1.0))[:, None, :]).astype(jnp.bfloat16)
        weights = (base * station_mask[:, :, None]).astype(jnp.bfloat16)
        accum = accum + jnp.einsum('kn,nt->kt', weights.reshape(K, 3 * L).astype(jnp.float32), scaled.reshape(3 * L, TDH).astype(jnp.float32))
        return (accum, None)
    start = jnp.zeros((K, TDH), jnp.float32)
    result, unused = lax.scan(station, start, (raw_window, counts_window, mask_by_station))
    return result

def reference(raw_rows, valid_counts, taps, templates, masks):
    shaped = templates.astype(jnp.float32).reshape(K, 3, L)
    norms = jnp.sqrt(lax.optimization_barrier(jnp.sum(shaped * shaped, axis=2)) + 1e-06)
    base = shaped / norms[:, :, None]
    mask_by_station = jnp.transpose(masks.astype(jnp.float32), (2, 0, 1))
    tap_values = taps.astype(jnp.float32)
    outputs = [one_window(raw_rows[window], valid_counts[window], base, mask_by_station, tap_values) for window in range(WINDOWS)]
    return jnp.stack(outputs, axis=0)
```

```python
import functools

import jax
import jax.numpy as jnp
from jax import lax
from jax.experimental import pallas as pl
from jax.experimental.pallas import tpu as pltpu
from jax.sharding import PartitionSpec as P

L = 75
TAPS = 64
DEC = 4
JP = 76
TT = 512
RSUB = 16


def from_behind(block, axis, distance):
    devices = range(lax.axis_size(axis))
    route = [(i - distance, i) for i in devices if i - distance in devices]
    return lax.ppermute(block, axis, route)


def window_energy(rows, width):
    p1 = rows * rows
    p2 = p1[:, :-1] + p1[:, 1:]
    p4 = p2[:, :-2] + p2[:, 2:]
    p8 = p4[:, :-4] + p4[:, 4:]
    p16 = p8[:, :-8] + p8[:, 8:]
    p32 = p16[:, :-16] + p16[:, 16:]
    p64 = p32[:, :-32] + p32[:, 32:]
    return (
        p64[:, :width]
        + p8[:, 64 : 64 + width]
        + p2[:, 72 : 72 + width]
        + p1[:, 74 : 74 + width]
    )


def corr_kernel(f_ref, inv_ref, w_ref, o_ref, s_ref, *, row_block):
    q = pl.program_id(1)
    span = TT + 128

    def fill(sub, carry):
        r0 = pl.multiple_of(sub * RSUB, RSUB)
        seg = f_ref[0, pl.ds(r0, RSUB), :].astype(jnp.float32)
        inv = inv_ref[pl.ds(r0, RSUB), :]
        for j in range(JP):
            moved = seg if j == 0 else pltpu.roll(seg, span - j, 1)
            piece = (moved[:, :TT] * inv).astype(jnp.bfloat16)
            s_ref[pl.ds(pl.multiple_of(j * row_block + r0, RSUB), RSUB), :] = piece
        return carry

    lax.fori_loop(0, row_block // RSUB, fill, 0)
    part = jnp.dot(w_ref[...], s_ref[...], preferred_element_type=jnp.float32)

    @pl.when(q == 0)
    def _():
        o_ref[...] = part

    @pl.when(q > 0)
    def _():
        o_ref[...] += part


def correlate(windows, inv, weights, row_block):
    tiles, rows, span = windows.shape
    count = weights.shape[0]
    width = inv.shape[1]
    chunks = rows // row_block
    return pl.pallas_call(
        functools.partial(corr_kernel, row_block=row_block),
        grid=(tiles, chunks),
        in_specs=[
            pl.BlockSpec((1, row_block, span), lambda i, q: (i, q, 0)),
            pl.BlockSpec((row_block, TT), lambda i, q: (q, i)),
            pl.BlockSpec((count, JP * row_block), lambda i, q: (0, q)),
        ],
        out_specs=pl.BlockSpec((count, TT), lambda i, q: (0, i)),
        out_shape=jax.ShapeDtypeStruct((count, width), jnp.float32),
        scratch_shapes=[pltpu.VMEM((JP * row_block, TT), jnp.bfloat16)],
        compiler_params=pltpu.CompilerParams(
            dimension_semantics=("parallel", "arbitrary"),
            vmem_limit_bytes=48 * 1024 * 1024,
        ),
    )(windows, inv, weights)


def body(raw_rows, valid_counts, taps, templates, masks):
    samples = raw_rows[0]
    counts = valid_counts[0]
    local_stations = samples.shape[0]
    raw_width = samples.shape[2]
    corr_place = lax.axis_index("corr")
    filt_place = lax.axis_index("filt")
    filt_count = lax.axis_size("filt")
    sample_times = corr_place * raw_width + lax.iota(jnp.int32, raw_width)
    live = jnp.where(
        sample_times[None, None, :] < counts[:, None, None], samples, jnp.zeros_like(samples)
    )
    history = from_behind(live[:, :, raw_width - (TAPS - 1) :], "corr", 1)
    extended = jnp.concatenate([history, live], axis=2).reshape(
        local_stations * 3, 1, raw_width + TAPS - 1
    )
    kernel = taps[::-1].reshape(1, 1, TAPS)
    filtered = lax.conv_general_dilated(
        extended,
        kernel,
        (DEC,),
        "VALID",
        dimension_numbers=("NCH", "OIH", "NCH"),
        preferred_element_type=jnp.float32,
    )
    decimated = raw_width // DEC
    filtered = filtered.astype(jnp.bfloat16).reshape(local_stations * 3, decimated)
    whole = lax.all_gather(filtered, "corr", axis=1, tiled=True)
    total_width = whole.shape[1]
    block = total_width // filt_count
    span = block + 128
    padded = jnp.concatenate(
        [whole, jnp.zeros((whole.shape[0], 128), whole.dtype)], axis=1
    )
    pieces = jnp.stack(
        [padded[:, g * block : g * block + span] for g in range(filt_count)], axis=0
    )
    gathered = lax.all_to_all(pieces, "filt", 0, 0, tiled=True)
    rows = gathered.reshape(filt_count * local_stations * 3, span)
    energy = window_energy(rows.astype(jnp.float32), block)
    inv = lax.rsqrt(jnp.maximum(energy, 1.0))
    tiles = block // TT
    windows = jnp.stack([rows[:, i * TT : i * TT + TT + 128] for i in range(tiles)], axis=0)

    count = templates.shape[0]
    stations = masks.shape[2]
    shaped = templates.astype(jnp.float32).reshape(count, 3, L)
    norms = jnp.sqrt(jnp.sum(shaped * shaped, axis=2) + 1e-06)
    base = shaped / norms[:, :, None]
    mine = lax.dynamic_slice_in_dim(masks, corr_place * count, count, 0).astype(jnp.float32)
    full = jnp.transpose(base, (0, 2, 1))[:, :, None, :] * jnp.transpose(mine, (0, 2, 1))[:, None, :, :]
    full = full.astype(jnp.bfloat16).reshape(count, L, stations * 3)
    full = jnp.concatenate([full, jnp.zeros((count, JP - L, stations * 3), full.dtype)], axis=1)
    total_rows = stations * 3
    row_block = 96 if total_rows % 96 == 0 else total_rows
    chunks = total_rows // row_block
    weights = (
        full.reshape(count, JP, chunks, row_block)
        .transpose(0, 2, 1, 3)
        .reshape(count, chunks * JP * row_block)
    )
    stacked = correlate(windows, inv, weights, row_block)
    return stacked[None]


def solution(mesh):
    return jax.shard_map(
        body,
        mesh=mesh,
        in_specs=(
            P(("groups", "pair"), "filt", None, "corr"),
            P(("groups", "pair"), "filt"),
            P(),
            P("corr", None),
            P(),
        ),
        out_specs=P(("groups", "pair"), "corr", "filt"),
        check_vma=False,
    )
```

```python
import functools

import jax
import jax.numpy as jnp
from jax import lax
from jax.experimental import pallas as pl
from jax.experimental.pallas import tpu as pltpu
from jax.sharding import PartitionSpec as P

L = 75
TAPS = 64
DEC = 4
JP = 76
TT = 512
RSUB = 16


def from_behind(block, axis, distance):
    devices = range(lax.axis_size(axis))
    route = [(i - distance, i) for i in devices if i - distance in devices]
    return lax.ppermute(block, axis, route)


def window_energy(rows, width):
    p1 = rows * rows
    p2 = p1[:, :-1] + p1[:, 1:]
    p4 = p2[:, :-2] + p2[:, 2:]
    p8 = p4[:, :-4] + p4[:, 4:]
    p16 = p8[:, :-8] + p8[:, 8:]
    p32 = p16[:, :-16] + p16[:, 16:]
    p64 = p32[:, :-32] + p32[:, 32:]
    return (
        p64[:, :width]
        + p8[:, 64 : 64 + width]
        + p2[:, 72 : 72 + width]
        + p1[:, 74 : 74 + width]
    )


def corr_kernel(f_ref, inv_ref, w_ref, o_ref, s_ref, *, row_block):
    q = pl.program_id(1)
    span = TT + 128

    def fill(sub, carry):
        r0 = pl.multiple_of(sub * RSUB, RSUB)
        seg = f_ref[0, pl.ds(r0, RSUB), :].astype(jnp.float32)
        inv = inv_ref[pl.ds(r0, RSUB), :]
        for j in range(JP):
            moved = seg if j == 0 else pltpu.roll(seg, span - j, 1)
            piece = (moved[:, :TT] * inv).astype(jnp.bfloat16)
            s_ref[pl.ds(pl.multiple_of(j * row_block + r0, RSUB), RSUB), :] = piece
        return carry

    lax.fori_loop(0, row_block // RSUB, fill, 0)
    part = jnp.dot(w_ref[...], s_ref[...], preferred_element_type=jnp.float32)

    @pl.when(q == 0)
    def _():
        o_ref[...] = part

    @pl.when(q > 0)
    def _():
        o_ref[...] += part


def correlate(windows, inv, weights, row_block):
    tiles, rows, span = windows.shape
    count = weights.shape[0]
    width = inv.shape[1]
    chunks = rows // row_block
    return pl.pallas_call(
        functools.partial(corr_kernel, row_block=row_block),
        grid=(tiles, chunks),
        in_specs=[
            pl.BlockSpec((1, row_block, span), lambda i, q: (i, q, 0)),
            pl.BlockSpec((row_block, TT), lambda i, q: (q, i)),
            pl.BlockSpec((count, JP * row_block), lambda i, q: (0, q)),
        ],
        out_specs=pl.BlockSpec((count, TT), lambda i, q: (0, i)),
        out_shape=jax.ShapeDtypeStruct((count, width), jnp.float32),
        scratch_shapes=[pltpu.VMEM((JP * row_block, TT), jnp.bfloat16)],
        compiler_params=pltpu.CompilerParams(
            dimension_semantics=("parallel", "arbitrary"),
            vmem_limit_bytes=48 * 1024 * 1024,
        ),
    )(windows, inv, weights)


def body(raw_rows, valid_counts, taps, templates, masks):
    samples = raw_rows[0]
    counts = valid_counts[0]
    local_stations = samples.shape[0]
    raw_width = samples.shape[2]
    corr_place = lax.axis_index("corr")
    filt_place = lax.axis_index("filt")
    filt_count = lax.axis_size("filt")
    sample_times = corr_place * raw_width + lax.iota(jnp.int32, raw_width)
    live = jnp.where(
        sample_times[None, None, :] < counts[:, None, None], samples, jnp.zeros_like(samples)
    )
    history = from_behind(live[:, :, raw_width - 128 :], "corr", 1)
    extended = jnp.concatenate([history, live], axis=2).reshape(local_stations * 3, raw_width + 128)
    decimated = raw_width // DEC
    blocks = decimated // 128
    frames = jnp.stack(
        [extended[:, 512 * a : 512 * a + 640] for a in range(blocks)], axis=1
    ).reshape(local_stations * 3 * blocks, 640)
    ring = jnp.concatenate(
        [jnp.zeros((65,), taps.dtype), taps[::-1], jnp.zeros((644 - 129,), taps.dtype)]
    )
    bank = jnp.tile(ring, 128)[: 128 * 640].reshape(128, 640)
    filtered = lax.dot_general(
        frames, bank, (((1,), (1,)), ((), ())), preferred_element_type=jnp.float32
    )
    filtered = filtered.astype(jnp.bfloat16).reshape(local_stations * 3, decimated)
    corr_count = lax.axis_size("corr")
    copies = jnp.broadcast_to(filtered[None], (corr_count,) + filtered.shape)
    whole = lax.all_to_all(copies, "corr", 0, 0, tiled=True)
    whole = jnp.transpose(whole, (1, 0, 2)).reshape(filtered.shape[0], -1)
    total_width = whole.shape[1]
    block = total_width // filt_count
    span = block + 128
    padded = jnp.concatenate(
        [whole, jnp.zeros((whole.shape[0], 128), whole.dtype)], axis=1
    )
    pieces = jnp.stack(
        [padded[:, g * block : g * block + span] for g in range(filt_count)], axis=0
    )
    gathered = lax.all_to_all(pieces, "filt", 0, 0, tiled=True)
    rows = gathered.reshape(filt_count * local_stations * 3, span)
    energy = window_energy(rows.astype(jnp.float32), block)
    inv = lax.rsqrt(jnp.maximum(energy, 1.0))
    tiles = block // TT
    windows = jnp.stack([rows[:, i * TT : i * TT + TT + 128] for i in range(tiles)], axis=0)

    count = templates.shape[0]
    stations = masks.shape[2]
    shaped = templates.astype(jnp.float32).reshape(count, 3, L)
    norms = jnp.sqrt(jnp.sum(shaped * shaped, axis=2) + 1e-06)
    base = shaped / norms[:, :, None]
    mine = lax.dynamic_slice_in_dim(masks, corr_place * count, count, 0).astype(jnp.float32)
    full = jnp.transpose(base, (0, 2, 1))[:, :, None, :] * jnp.transpose(mine, (0, 2, 1))[:, None, :, :]
    full = full.astype(jnp.bfloat16).reshape(count, L, stations * 3)
    full = jnp.concatenate([full, jnp.zeros((count, JP - L, stations * 3), full.dtype)], axis=1)
    total_rows = stations * 3
    row_block = 96 if total_rows % 96 == 0 else total_rows
    chunks = total_rows // row_block
    weights = (
        full.reshape(count, JP, chunks, row_block)
        .transpose(0, 2, 1, 3)
        .reshape(count, chunks * JP * row_block)
    )
    stacked = correlate(windows, inv, weights, row_block)
    return stacked[None]


def solution(mesh):
    return jax.shard_map(
        body,
        mesh=mesh,
        in_specs=(
            P(("groups", "pair"), "filt", None, "corr"),
            P(("groups", "pair"), "filt"),
            P(),
            P("corr", None),
            P(),
        ),
        out_specs=P(("groups", "pair"), "corr", "filt"),
        check_vma=False,
    )
```

```python
import functools

import jax
import jax.numpy as jnp
from jax import lax
from jax.experimental import pallas as pl
from jax.experimental.pallas import tpu as pltpu
from jax.sharding import PartitionSpec as P

L = 75
TAPS = 64
DEC = 4
JP = 76
TT = 512
RSUB = 16


def from_behind(block, axis, distance):
    devices = range(lax.axis_size(axis))
    route = [(i - distance, i) for i in devices if i - distance in devices]
    return lax.ppermute(block, axis, route)


def window_energy(rows, width):
    p1 = rows * rows
    p2 = p1[:, :-1] + p1[:, 1:]
    p4 = p2[:, :-2] + p2[:, 2:]
    p8 = p4[:, :-4] + p4[:, 4:]
    p16 = p8[:, :-8] + p8[:, 8:]
    p32 = p16[:, :-16] + p16[:, 16:]
    p64 = p32[:, :-32] + p32[:, 32:]
    return (
        p64[:, :width]
        + p8[:, 64 : 64 + width]
        + p2[:, 72 : 72 + width]
        + p1[:, 74 : 74 + width]
    )


def corr_kernel(f_ref, inv_ref, w_ref, o_ref, s_ref, *, row_block):
    q = pl.program_id(1)
    span = TT + 128

    def fill(sub, carry):
        r0 = pl.multiple_of(sub * RSUB, RSUB)
        seg = f_ref[0, pl.ds(r0, RSUB), :].astype(jnp.float32)
        inv = inv_ref[pl.ds(r0, RSUB), :]
        for j in range(JP):
            moved = seg if j == 0 else pltpu.roll(seg, span - j, 1)
            piece = (moved[:, :TT] * inv).astype(jnp.bfloat16)
            s_ref[pl.ds(pl.multiple_of(j * row_block + r0, RSUB), RSUB), :] = piece
        return carry

    lax.fori_loop(0, row_block // RSUB, fill, 0)
    part = jnp.dot(w_ref[...], s_ref[...], preferred_element_type=jnp.float32)

    @pl.when(q == 0)
    def _():
        o_ref[...] = part

    @pl.when(q > 0)
    def _():
        o_ref[...] += part


def correlate(windows, inv, weights, row_block):
    tiles, rows, span = windows.shape
    count = weights.shape[0]
    width = inv.shape[1]
    chunks = rows // row_block
    return pl.pallas_call(
        functools.partial(corr_kernel, row_block=row_block),
        grid=(tiles, chunks),
        in_specs=[
            pl.BlockSpec((1, row_block, span), lambda i, q: (i, q, 0)),
            pl.BlockSpec((row_block, TT), lambda i, q: (q, i)),
            pl.BlockSpec((count, JP * row_block), lambda i, q: (0, q)),
        ],
        out_specs=pl.BlockSpec((count, TT), lambda i, q: (0, i)),
        out_shape=jax.ShapeDtypeStruct((count, width), jnp.float32),
        scratch_shapes=[pltpu.VMEM((JP * row_block, TT), jnp.bfloat16)],
        compiler_params=pltpu.CompilerParams(
            dimension_semantics=("parallel", "arbitrary"),
            vmem_limit_bytes=48 * 1024 * 1024,
        ),
    )(windows, inv, weights)


def body(raw_rows, valid_counts, taps, templates, masks):
    samples = raw_rows[0]
    counts = valid_counts[0]
    local_stations = samples.shape[0]
    raw_width = samples.shape[2]
    corr_place = lax.axis_index("corr")
    filt_place = lax.axis_index("filt")
    filt_count = lax.axis_size("filt")
    sample_times = corr_place * raw_width + lax.iota(jnp.int32, raw_width)
    live = jnp.where(
        sample_times[None, None, :] < counts[:, None, None], samples, jnp.zeros_like(samples)
    )
    history = from_behind(live[:, :, raw_width - 128 :], "corr", 1)
    extended = jnp.concatenate([history, live], axis=2).reshape(local_stations * 3, raw_width + 128)
    decimated = raw_width // DEC
    blocks = decimated // 128
    frames = jnp.stack(
        [extended[:, 512 * a : 512 * a + 640] for a in range(blocks)], axis=1
    ).reshape(local_stations * 3 * blocks, 640)
    ring = jnp.concatenate(
        [jnp.zeros((65,), taps.dtype), taps[::-1], jnp.zeros((644 - 129,), taps.dtype)]
    )
    bank = jnp.tile(ring, 128)[: 128 * 640].reshape(128, 640)
    filtered = lax.dot_general(
        frames, bank, (((1,), (1,)), ((), ())), preferred_element_type=jnp.float32
    )
    filtered = filtered.astype(jnp.bfloat16).reshape(local_stations * 3, decimated)
    corr_count = lax.axis_size("corr")
    group = corr_count * filt_count
    copies = jnp.broadcast_to(filtered[None], (group,) + filtered.shape)
    everything = lax.all_to_all(copies, ("corr", "filt"), 0, 0, tiled=True)
    everything = everything.reshape(corr_count, filt_count, filtered.shape[0], decimated)
    everything = jnp.concatenate(
        [everything, jnp.zeros((1,) + everything.shape[1:], everything.dtype)], axis=0
    )
    per_block = corr_count // filt_count
    block = per_block * decimated
    span = block + 128
    mine = lax.dynamic_slice_in_dim(everything, filt_place * per_block, per_block + 1, 0)
    rows = jnp.transpose(mine, (1, 2, 0, 3)).reshape(
        filt_count * filtered.shape[0], (per_block + 1) * decimated
    )[:, :span]
    energy = window_energy(rows.astype(jnp.float32), block)
    inv = lax.rsqrt(jnp.maximum(energy, 1.0))
    tiles = block // TT
    windows = jnp.stack([rows[:, i * TT : i * TT + TT + 128] for i in range(tiles)], axis=0)

    count = templates.shape[0]
    stations = masks.shape[2]
    shaped = templates.astype(jnp.float32).reshape(count, 3, L)
    norms = jnp.sqrt(jnp.sum(shaped * shaped, axis=2) + 1e-06)
    base = shaped / norms[:, :, None]
    chosen = lax.dynamic_slice_in_dim(masks, corr_place * count, count, 0).astype(jnp.float32)
    full = jnp.transpose(base, (0, 2, 1))[:, :, None, :] * jnp.transpose(chosen, (0, 2, 1))[:, None, :, :]
    full = full.astype(jnp.bfloat16).reshape(count, L, stations * 3)
    full = jnp.concatenate([full, jnp.zeros((count, JP - L, stations * 3), full.dtype)], axis=1)
    total_rows = stations * 3
    row_block = 96 if total_rows % 96 == 0 else total_rows
    chunks = total_rows // row_block
    weights = (
        full.reshape(count, JP, chunks, row_block)
        .transpose(0, 2, 1, 3)
        .reshape(count, chunks * JP * row_block)
    )
    stacked = correlate(windows, inv, weights, row_block)
    return stacked[None]


def solution(mesh):
    return jax.shard_map(
        body,
        mesh=mesh,
        in_specs=(
            P(("groups", "pair"), "filt", None, "corr"),
            P(("groups", "pair"), "filt"),
            P(),
            P("corr", None),
            P(),
        ),
        out_specs=P(("groups", "pair"), "corr", "filt"),
        check_vma=False,
    )
```

```python
import functools

import jax
import jax.numpy as jnp
from jax import lax
from jax.experimental import pallas as pl
from jax.experimental.pallas import tpu as pltpu
from jax.sharding import PartitionSpec as P

L = 75
TAPS = 64
DEC = 4
JP = 76
TT = 512
RSUB = 16


def from_behind(block, axis, distance):
    devices = range(lax.axis_size(axis))
    route = [(i - distance, i) for i in devices if i - distance in devices]
    return lax.ppermute(block, axis, route)


def window_energy(rows, width):
    p1 = rows * rows
    p2 = p1[:, :-1] + p1[:, 1:]
    p4 = p2[:, :-2] + p2[:, 2:]
    p8 = p4[:, :-4] + p4[:, 4:]
    p16 = p8[:, :-8] + p8[:, 8:]
    p32 = p16[:, :-16] + p16[:, 16:]
    p64 = p32[:, :-32] + p32[:, 32:]
    return (
        p64[:, :width]
        + p8[:, 64 : 64 + width]
        + p2[:, 72 : 72 + width]
        + p1[:, 74 : 74 + width]
    )


def corr_kernel(f_ref, inv_ref, w_ref, o_ref, s_ref, *, row_block):
    q = pl.program_id(1)
    span = TT + 128

    def fill(sub, carry):
        r0 = pl.multiple_of(sub * RSUB, RSUB)
        seg = f_ref[0, pl.ds(r0, RSUB), :].astype(jnp.float32)
        inv = inv_ref[pl.ds(r0, RSUB), :]
        for j in range(JP):
            moved = seg if j == 0 else pltpu.roll(seg, span - j, 1)
            piece = (moved[:, :TT] * inv).astype(jnp.bfloat16)
            s_ref[pl.ds(pl.multiple_of(j * row_block + r0, RSUB), RSUB), :] = piece
        return carry

    lax.fori_loop(0, row_block // RSUB, fill, 0)
    part = jnp.dot(w_ref[...], s_ref[...], preferred_element_type=jnp.float32)

    @pl.when(q == 0)
    def _():
        o_ref[...] = part

    @pl.when(q > 0)
    def _():
        o_ref[...] += part


def correlate(windows, inv, weights, row_block):
    tiles, rows, span = windows.shape
    count = weights.shape[0]
    width = inv.shape[1]
    chunks = rows // row_block
    return pl.pallas_call(
        functools.partial(corr_kernel, row_block=row_block),
        grid=(tiles, chunks),
        in_specs=[
            pl.BlockSpec((1, row_block, span), lambda i, q: (i, q, 0)),
            pl.BlockSpec((row_block, TT), lambda i, q: (q, i)),
            pl.BlockSpec((count, JP * row_block), lambda i, q: (0, q)),
        ],
        out_specs=pl.BlockSpec((count, TT), lambda i, q: (0, i)),
        out_shape=jax.ShapeDtypeStruct((count, width), jnp.float32),
        scratch_shapes=[pltpu.VMEM((JP * row_block, TT), jnp.bfloat16)],
        compiler_params=pltpu.CompilerParams(
            dimension_semantics=("parallel", "arbitrary"),
            vmem_limit_bytes=48 * 1024 * 1024,
        ),
    )(windows, inv, weights)


def body(raw_rows, valid_counts, taps, templates, masks):
    samples = raw_rows[0]
    counts = valid_counts[0]
    local_stations = samples.shape[0]
    raw_width = samples.shape[2]
    corr_place = lax.axis_index("corr")
    filt_place = lax.axis_index("filt")
    filt_count = lax.axis_size("filt")
    sample_times = corr_place * raw_width + lax.iota(jnp.int32, raw_width)
    live = jnp.where(
        sample_times[None, None, :] < counts[:, None, None], samples, jnp.zeros_like(samples)
    )
    history = from_behind(live[:, :, raw_width - 128 :], "corr", 1)
    corr_count = lax.axis_size("corr")
    ahead = from_behind(live[:, :, :512], "corr", -1)
    extended = jnp.concatenate([history, live, ahead], axis=2).reshape(
        local_stations * 3, raw_width + 640
    )
    decimated = raw_width // DEC
    blocks = decimated // 128 + 1
    frames = jnp.stack(
        [extended[:, 512 * a : 512 * a + 640] for a in range(blocks)], axis=1
    ).reshape(local_stations * 3 * blocks, 640)
    ring = jnp.concatenate(
        [jnp.zeros((65,), taps.dtype), taps[::-1], jnp.zeros((644 - 129,), taps.dtype)]
    )
    bank = jnp.tile(ring, 128)[: 128 * 640].reshape(128, 640)
    filtered = lax.dot_general(
        frames, bank, (((1,), (1,)), ((), ())), preferred_element_type=jnp.float32
    )
    filtered = filtered.astype(jnp.bfloat16).reshape(local_stations * 3, decimated + 128)
    past_end = (corr_place == corr_count - 1) & (lax.iota(jnp.int32, decimated + 128) >= decimated)
    filtered = jnp.where(past_end[None, :], jnp.zeros_like(filtered), filtered)
    per_block = corr_count // filt_count
    block = per_block * decimated
    span = block + 128
    sender = (corr_place % per_block) * filt_count + filt_place
    target_filt = corr_place // per_block
    received = []
    for k in range(corr_count):
        route = []
        for c in range(corr_count):
            for f in range(filt_count):
                s_id = (c % per_block) * filt_count + f
                dest = ((s_id + k) % corr_count) * filt_count + c // per_block
                route.append((c * filt_count + f, dest))
        received.append(lax.ppermute(filtered, ("corr", "filt"), route))
    received = jnp.stack(received, axis=0)
    order = (corr_place - lax.iota(jnp.int32, corr_count)) % corr_count
    ordered = jnp.take(received, order, axis=0)
    ordered = ordered.reshape(per_block, filt_count, filtered.shape[0], decimated + 128)
    heads = jnp.transpose(ordered[:, :, :, :decimated], (1, 2, 0, 3)).reshape(
        filt_count, filtered.shape[0], block
    )
    tail = ordered[per_block - 1, :, :, decimated:]
    rows = jnp.concatenate([heads, tail], axis=2).reshape(filt_count * filtered.shape[0], span)
    energy = window_energy(rows.astype(jnp.float32), block)
    inv = lax.rsqrt(jnp.maximum(energy, 1.0))
    tiles = block // TT
    windows = jnp.stack([rows[:, i * TT : i * TT + TT + 128] for i in range(tiles)], axis=0)

    count = templates.shape[0]
    stations = masks.shape[2]
    shaped = templates.astype(jnp.float32).reshape(count, 3, L)
    norms = jnp.sqrt(jnp.sum(shaped * shaped, axis=2) + 1e-06)
    base = shaped / norms[:, :, None]
    chosen = lax.dynamic_slice_in_dim(masks, corr_place * count, count, 0).astype(jnp.float32)
    full = jnp.transpose(base, (0, 2, 1))[:, :, None, :] * jnp.transpose(chosen, (0, 2, 1))[:, None, :, :]
    full = full.astype(jnp.bfloat16).reshape(count, L, stations * 3)
    full = jnp.concatenate([full, jnp.zeros((count, JP - L, stations * 3), full.dtype)], axis=1)
    total_rows = stations * 3
    row_block = 96 if total_rows % 96 == 0 else total_rows
    chunks = total_rows // row_block
    weights = (
        full.reshape(count, JP, chunks, row_block)
        .transpose(0, 2, 1, 3)
        .reshape(count, chunks * JP * row_block)
    )
    stacked = correlate(windows, inv, weights, row_block)
    return stacked[None]


def solution(mesh):
    return jax.shard_map(
        body,
        mesh=mesh,
        in_specs=(
            P(("groups", "pair"), "filt", None, "corr"),
            P(("groups", "pair"), "filt"),
            P(),
            P("corr", None),
            P(),
        ),
        out_specs=P(("groups", "pair"), "corr", "filt"),
        check_vma=False,
    )
```

```python
import functools

import jax
import jax.numpy as jnp
from jax import lax
from jax.experimental import pallas as pl
from jax.experimental.pallas import tpu as pltpu
from jax.sharding import PartitionSpec as P

L = 75
TAPS = 64
DEC = 4
JP = 76
TT = 512
RSUB = 16


def from_behind(block, axis, distance):
    devices = range(lax.axis_size(axis))
    route = [(i - distance, i) for i in devices if i - distance in devices]
    return lax.ppermute(block, axis, route)


def window_energy(rows, width):
    p1 = rows * rows
    p2 = p1[:, :-1] + p1[:, 1:]
    p4 = p2[:, :-2] + p2[:, 2:]
    p8 = p4[:, :-4] + p4[:, 4:]
    p16 = p8[:, :-8] + p8[:, 8:]
    p32 = p16[:, :-16] + p16[:, 16:]
    p64 = p32[:, :-32] + p32[:, 32:]
    return (
        p64[:, :width]
        + p8[:, 64 : 64 + width]
        + p2[:, 72 : 72 + width]
        + p1[:, 74 : 74 + width]
    )


def corr_kernel(f_ref, inv_ref, w_ref, o_ref, s_ref, *, row_block, tile):
    q = pl.program_id(1)
    span = tile + 128

    def fill(sub, carry):
        r0 = pl.multiple_of(sub * RSUB, RSUB)
        seg = f_ref[0, pl.ds(r0, RSUB), :].astype(jnp.float32)
        inv = inv_ref[pl.ds(r0, RSUB), :]
        for j in range(JP):
            moved = seg if j == 0 else pltpu.roll(seg, span - j, 1)
            piece = (moved[:, :tile] * inv).astype(jnp.bfloat16)
            s_ref[pl.ds(pl.multiple_of(j * row_block + r0, RSUB), RSUB), :] = piece
        return carry

    lax.fori_loop(0, row_block // RSUB, fill, 0)
    part = jnp.dot(w_ref[...], s_ref[...], preferred_element_type=jnp.float32)

    @pl.when(q == 0)
    def _():
        o_ref[...] = part

    @pl.when(q > 0)
    def _():
        o_ref[...] += part


def correlate(windows, inv, weights, row_block):
    tiles, rows, span = windows.shape
    count = weights.shape[0]
    width = inv.shape[1]
    tile = width // tiles
    chunks = rows // row_block
    return pl.pallas_call(
        functools.partial(corr_kernel, row_block=row_block, tile=tile),
        grid=(tiles, chunks),
        in_specs=[
            pl.BlockSpec((1, row_block, span), lambda i, q: (i, q, 0)),
            pl.BlockSpec((row_block, tile), lambda i, q: (q, i)),
            pl.BlockSpec((count, JP * row_block), lambda i, q: (0, q)),
        ],
        out_specs=pl.BlockSpec((count, tile), lambda i, q: (0, i)),
        out_shape=jax.ShapeDtypeStruct((count, width), jnp.float32),
        scratch_shapes=[pltpu.VMEM((JP * row_block, tile), jnp.bfloat16)],
        compiler_params=pltpu.CompilerParams(
            dimension_semantics=("parallel", "arbitrary"),
            vmem_limit_bytes=48 * 1024 * 1024,
        ),
    )(windows, inv, weights)


def body(raw_rows, valid_counts, taps, templates, masks):
    samples = raw_rows[0]
    counts = valid_counts[0]
    local_stations = samples.shape[0]
    raw_width = samples.shape[2]
    corr_place = lax.axis_index("corr")
    filt_place = lax.axis_index("filt")
    filt_count = lax.axis_size("filt")
    sample_times = corr_place * raw_width + lax.iota(jnp.int32, raw_width)
    live = jnp.where(
        sample_times[None, None, :] < counts[:, None, None], samples, jnp.zeros_like(samples)
    )
    history = from_behind(live[:, :, raw_width - 128 :], "corr", 1)
    corr_count = lax.axis_size("corr")
    ahead = from_behind(live[:, :, :512], "corr", -1)
    extended = jnp.concatenate([history, live, ahead], axis=2).reshape(
        local_stations * 3, raw_width + 640
    )
    decimated = raw_width // DEC
    blocks = decimated // 128 + 1
    frames = jnp.stack(
        [extended[:, 512 * a : 512 * a + 640] for a in range(blocks)], axis=1
    ).reshape(local_stations * 3 * blocks, 640)
    ring = jnp.concatenate(
        [jnp.zeros((65,), taps.dtype), taps[::-1], jnp.zeros((644 - 129,), taps.dtype)]
    )
    bank = jnp.tile(ring, 128)[: 128 * 640].reshape(128, 640)
    filtered = lax.dot_general(
        frames, bank, (((1,), (1,)), ((), ())), preferred_element_type=jnp.float32
    )
    filtered = filtered.astype(jnp.bfloat16).reshape(local_stations * 3, decimated + 128)
    past_end = (corr_place == corr_count - 1) & (lax.iota(jnp.int32, decimated + 128) >= decimated)
    filtered = jnp.where(past_end[None, :], jnp.zeros_like(filtered), filtered)
    per_block = corr_count // filt_count
    block = per_block * decimated
    width = block // corr_count
    span = width + 128
    received = []
    for k in range(filt_count):
        piece = (filt_place + k) % filt_count
        part = lax.dynamic_slice_in_dim(filtered, piece * width, span, 1)
        route = []
        for c in range(corr_count):
            for f in range(filt_count):
                dest = ((c % per_block) * filt_count + (f + k) % filt_count) * filt_count + c // per_block
                route.append((c * filt_count + f, dest))
        received.append(lax.ppermute(part, ("corr", "filt"), route))
    received = jnp.stack(received, axis=0)
    order = (corr_place - lax.iota(jnp.int32, filt_count)) % filt_count
    rows = jnp.take(received, order, axis=0).reshape(filt_count * filtered.shape[0], span)
    energy = window_energy(rows.astype(jnp.float32), width)
    inv = lax.rsqrt(jnp.maximum(energy, 1.0))
    tile = min(TT, width)
    tiles = width // tile
    windows = jnp.stack([rows[:, i * tile : i * tile + tile + 128] for i in range(tiles)], axis=0)

    local_count = templates.shape[0]
    copies = jnp.broadcast_to(templates[None], (corr_count,) + templates.shape)
    templates = lax.all_to_all(copies, "corr", 0, 0, tiled=True).reshape(
        corr_count * local_count, templates.shape[1]
    )
    count = templates.shape[0]
    stations = masks.shape[2]
    shaped = templates.astype(jnp.float32).reshape(count, 3, L)
    norms = jnp.sqrt(jnp.sum(shaped * shaped, axis=2) + 1e-06)
    base = shaped / norms[:, :, None]
    chosen = masks.astype(jnp.float32)
    full = jnp.transpose(base, (0, 2, 1))[:, :, None, :] * jnp.transpose(chosen, (0, 2, 1))[:, None, :, :]
    full = full.astype(jnp.bfloat16).reshape(count, L, stations * 3)
    full = jnp.concatenate([full, jnp.zeros((count, JP - L, stations * 3), full.dtype)], axis=1)
    total_rows = stations * 3
    row_block = 96 if total_rows % 96 == 0 else total_rows
    chunks = total_rows // row_block
    weights = (
        full.reshape(count, JP, chunks, row_block)
        .transpose(0, 2, 1, 3)
        .reshape(count, chunks * JP * row_block)
    )
    stacked = correlate(windows, inv, weights, row_block)
    stacked = lax.all_to_all(stacked, "corr", 0, 1, tiled=True)
    return stacked[None]


def solution(mesh):
    return jax.shard_map(
        body,
        mesh=mesh,
        in_specs=(
            P(("groups", "pair"), "filt", None, "corr"),
            P(("groups", "pair"), "filt"),
            P(),
            P("corr", None),
            P(),
        ),
        out_specs=P(("groups", "pair"), "corr", "filt"),
        check_vma=False,
    )
```

```python
import functools

import jax
import jax.numpy as jnp
from jax import lax
from jax.experimental import pallas as pl
from jax.experimental.pallas import tpu as pltpu
from jax.sharding import PartitionSpec as P

L = 75
TAPS = 64
DEC = 4
JP = 76
TT = 512
RSUB = 16


def from_behind(block, axis, distance):
    devices = range(lax.axis_size(axis))
    route = [(i - distance, i) for i in devices if i - distance in devices]
    return lax.ppermute(block, axis, route)


def window_energy(rows, width):
    p1 = rows * rows
    p2 = p1[:, :-1] + p1[:, 1:]
    p4 = p2[:, :-2] + p2[:, 2:]
    p8 = p4[:, :-4] + p4[:, 4:]
    p16 = p8[:, :-8] + p8[:, 8:]
    p32 = p16[:, :-16] + p16[:, 16:]
    p64 = p32[:, :-32] + p32[:, 32:]
    return (
        p64[:, :width]
        + p8[:, 64 : 64 + width]
        + p2[:, 72 : 72 + width]
        + p1[:, 74 : 74 + width]
    )


def corr_kernel(f_ref, inv_ref, w_ref, o_ref, s_ref, *, row_block, tile):
    q = pl.program_id(1)
    span = tile + 128

    def fill(sub, carry):
        r0 = pl.multiple_of(sub * RSUB, RSUB)
        seg = f_ref[0, pl.ds(r0, RSUB), :].astype(jnp.float32)
        inv = inv_ref[pl.ds(r0, RSUB), :]
        for j in range(JP):
            moved = seg if j == 0 else pltpu.roll(seg, span - j, 1)
            piece = (moved[:, :tile] * inv).astype(jnp.bfloat16)
            s_ref[pl.ds(pl.multiple_of(j * row_block + r0, RSUB), RSUB), :] = piece
        return carry

    lax.fori_loop(0, row_block // RSUB, fill, 0)
    part = jnp.dot(w_ref[...], s_ref[...], preferred_element_type=jnp.float32)

    @pl.when(q == 0)
    def _():
        o_ref[...] = part

    @pl.when(q > 0)
    def _():
        o_ref[...] += part


def correlate(windows, inv, weights, row_block):
    tiles, rows, span = windows.shape
    count = weights.shape[0]
    width = inv.shape[1]
    tile = width // tiles
    chunks = rows // row_block
    return pl.pallas_call(
        functools.partial(corr_kernel, row_block=row_block, tile=tile),
        grid=(tiles, chunks),
        in_specs=[
            pl.BlockSpec((1, row_block, span), lambda i, q: (i, q, 0)),
            pl.BlockSpec((row_block, tile), lambda i, q: (q, i)),
            pl.BlockSpec((count, JP * row_block), lambda i, q: (0, q)),
        ],
        out_specs=pl.BlockSpec((count, tile), lambda i, q: (0, i)),
        out_shape=jax.ShapeDtypeStruct((count, width), jnp.float32),
        scratch_shapes=[pltpu.VMEM((JP * row_block, tile), jnp.bfloat16)],
        compiler_params=pltpu.CompilerParams(
            dimension_semantics=("parallel", "arbitrary"),
            vmem_limit_bytes=48 * 1024 * 1024,
        ),
    )(windows, inv, weights)


def body(raw_rows, valid_counts, taps, templates, masks):
    samples = raw_rows[0]
    counts = valid_counts[0]
    local_stations = samples.shape[0]
    raw_width = samples.shape[2]
    corr_place = lax.axis_index("corr")
    filt_place = lax.axis_index("filt")
    filt_count = lax.axis_size("filt")
    sample_times = corr_place * raw_width + lax.iota(jnp.int32, raw_width)
    live = jnp.where(
        sample_times[None, None, :] < counts[:, None, None], samples, jnp.zeros_like(samples)
    )
    history = from_behind(live[:, :, raw_width - 128 :], "corr", 1)
    corr_count = lax.axis_size("corr")
    ahead = from_behind(live[:, :, :512], "corr", -1)
    extended = jnp.concatenate([history, live, ahead], axis=2).reshape(
        local_stations * 3, raw_width + 640
    )
    decimated = raw_width // DEC
    blocks = decimated // 128 + 1
    frames = jnp.stack(
        [extended[:, 512 * a : 512 * a + 640] for a in range(blocks)], axis=1
    ).reshape(local_stations * 3 * blocks, 640)
    ring = jnp.concatenate(
        [jnp.zeros((65,), taps.dtype), taps[::-1], jnp.zeros((644 - 129,), taps.dtype)]
    )
    bank = jnp.tile(ring, 128)[: 128 * 640].reshape(128, 640)
    filtered = lax.dot_general(
        frames, bank, (((1,), (1,)), ((), ())), preferred_element_type=jnp.float32
    )
    filtered = filtered.astype(jnp.bfloat16).reshape(local_stations * 3, decimated + 128)
    past_end = (corr_place == corr_count - 1) & (lax.iota(jnp.int32, decimated + 128) >= decimated)
    filtered = jnp.where(past_end[None, :], jnp.zeros_like(filtered), filtered)
    per_block = corr_count // filt_count
    block = per_block * decimated
    width = block // corr_count
    span = width + 128
    received = []
    for k in range(filt_count):
        piece = (filt_place + k) % filt_count
        part = lax.dynamic_slice_in_dim(filtered, piece * width, span, 1)
        route = []
        for c in range(corr_count):
            for f in range(filt_count):
                dest = ((c % per_block) * filt_count + (f + k) % filt_count) * filt_count + c // per_block
                route.append((c * filt_count + f, dest))
        received.append(lax.ppermute(part, ("corr", "filt"), route))
    received = jnp.stack(received, axis=0)
    order = (corr_place - lax.iota(jnp.int32, filt_count)) % filt_count
    rows = jnp.take(received, order, axis=0).reshape(filt_count * filtered.shape[0], span)
    energy = window_energy(rows.astype(jnp.float32), width)
    inv = lax.rsqrt(jnp.maximum(energy, 1.0))
    tile = min(TT, width)
    tiles = width // tile
    windows = jnp.stack([rows[:, i * tile : i * tile + tile + 128] for i in range(tiles)], axis=0)

    local_count = templates.shape[0]
    copies = jnp.broadcast_to(templates[None], (corr_count,) + templates.shape)
    templates = lax.all_to_all(copies, "corr", 0, 0, tiled=True).reshape(
        corr_count * local_count, templates.shape[1]
    )
    count = templates.shape[0]
    stations = masks.shape[2]
    shaped = templates.astype(jnp.float32).reshape(count, 3, L)
    norms = jnp.sqrt(jnp.sum(shaped * shaped, axis=2) + 1e-06)
    base = shaped / norms[:, :, None]
    chosen = masks.astype(jnp.float32)
    full = jnp.transpose(base, (0, 2, 1))[:, :, None, :] * jnp.transpose(chosen, (0, 2, 1))[:, None, :, :]
    full = full.astype(jnp.bfloat16).reshape(count, L, stations * 3)
    full = jnp.concatenate([full, jnp.zeros((count, JP - L, stations * 3), full.dtype)], axis=1)
    total_rows = stations * 3
    row_block = 96 if total_rows % 96 == 0 else total_rows
    chunks = total_rows // row_block
    weights = (
        full.reshape(count, JP, chunks, row_block)
        .transpose(0, 2, 1, 3)
        .reshape(count, chunks * JP * row_block)
    )
    stacked = correlate(windows, inv, weights, row_block)
    pieces = [lax.dynamic_slice_in_dim(stacked, corr_place * local_count, local_count, 0)]
    for d in range(1, corr_count):
        target = (corr_place + d) % corr_count
        part = lax.dynamic_slice_in_dim(stacked, target * local_count, local_count, 0)
        route = [(i, (i + d) % corr_count) for i in range(corr_count)]
        pieces.append(lax.ppermute(part, "corr", route))
    pieces = jnp.stack(pieces, axis=0)
    order = (corr_place - lax.iota(jnp.int32, corr_count)) % corr_count
    stacked = jnp.take(pieces, order, axis=0)
    stacked = jnp.transpose(stacked, (1, 0, 2)).reshape(local_count, corr_count * width)
    return stacked[None]


def solution(mesh):
    return jax.shard_map(
        body,
        mesh=mesh,
        in_specs=(
            P(("groups", "pair"), "filt", None, "corr"),
            P(("groups", "pair"), "filt"),
            P(),
            P("corr", None),
            P(),
        ),
        out_specs=P(("groups", "pair"), "corr", "filt"),
        check_vma=False,
    )
```

```python
import functools

import jax
import jax.numpy as jnp
from jax import lax
from jax.experimental import pallas as pl
from jax.experimental.pallas import tpu as pltpu
from jax.sharding import PartitionSpec as P

L = 75
TAPS = 64
DEC = 4
JP = 76
TT = 512
RSUB = 16


def from_behind(block, axis, distance):
    devices = range(lax.axis_size(axis))
    route = [(i - distance, i) for i in devices if i - distance in devices]
    return lax.ppermute(block, axis, route)


def window_energy(rows, width):
    p1 = rows * rows
    p2 = p1[:, :-1] + p1[:, 1:]
    p4 = p2[:, :-2] + p2[:, 2:]
    p8 = p4[:, :-4] + p4[:, 4:]
    p16 = p8[:, :-8] + p8[:, 8:]
    p32 = p16[:, :-16] + p16[:, 16:]
    p64 = p32[:, :-32] + p32[:, 32:]
    return (
        p64[:, :width]
        + p8[:, 64 : 64 + width]
        + p2[:, 72 : 72 + width]
        + p1[:, 74 : 74 + width]
    )


def corr_kernel(f_ref, inv_ref, w_ref, o_ref, s_ref, *, row_block, tile):
    q = pl.program_id(1)
    span = tile + 128

    def fill(sub, carry):
        r0 = pl.multiple_of(sub * RSUB, RSUB)
        seg = f_ref[0, pl.ds(r0, RSUB), :].astype(jnp.float32)
        inv = inv_ref[pl.ds(r0, RSUB), :]
        for j in range(JP):
            moved = seg if j == 0 else pltpu.roll(seg, span - j, 1)
            piece = (moved[:, :tile] * inv).astype(jnp.bfloat16)
            s_ref[pl.ds(pl.multiple_of(j * row_block + r0, RSUB), RSUB), :] = piece
        return carry

    lax.fori_loop(0, row_block // RSUB, fill, 0)
    part = jnp.dot(w_ref[...], s_ref[...], preferred_element_type=jnp.float32)

    @pl.when(q == 0)
    def _():
        o_ref[...] = part

    @pl.when(q > 0)
    def _():
        o_ref[...] += part


def correlate(windows, inv, weights, row_block):
    tiles, rows, span = windows.shape
    count = weights.shape[0]
    width = inv.shape[1]
    tile = width // tiles
    chunks = rows // row_block
    return pl.pallas_call(
        functools.partial(corr_kernel, row_block=row_block, tile=tile),
        grid=(tiles, chunks),
        in_specs=[
            pl.BlockSpec((1, row_block, span), lambda i, q: (i, q, 0)),
            pl.BlockSpec((row_block, tile), lambda i, q: (q, i)),
            pl.BlockSpec((count, JP * row_block), lambda i, q: (0, q)),
        ],
        out_specs=pl.BlockSpec((count, tile), lambda i, q: (0, i)),
        out_shape=jax.ShapeDtypeStruct((count, width), jnp.float32),
        scratch_shapes=[pltpu.VMEM((JP * row_block, tile), jnp.bfloat16)],
        compiler_params=pltpu.CompilerParams(
            dimension_semantics=("parallel", "arbitrary"),
            vmem_limit_bytes=48 * 1024 * 1024,
        ),
    )(windows, inv, weights)


def body(raw_rows, valid_counts, taps, templates, masks):
    samples = raw_rows[0]
    counts = valid_counts[0]
    local_stations = samples.shape[0]
    raw_width = samples.shape[2]
    corr_place = lax.axis_index("corr")
    filt_place = lax.axis_index("filt")
    filt_count = lax.axis_size("filt")
    corr_place = lax.axis_index("corr")
    sample_times = corr_place * raw_width + lax.iota(jnp.int32, raw_width)
    live = jnp.where(
        sample_times[None, None, :] < counts[:, None, None], samples, jnp.zeros_like(samples)
    )
    corr_count = lax.axis_size("corr")
    head = live[:, :, :512].reshape(-1)
    tail = live[:, :, raw_width - 128 :].reshape(-1)
    tail = jnp.concatenate([tail, jnp.zeros((head.shape[0] - tail.shape[0],), tail.dtype)])
    own_templates = templates.reshape(-1)
    peers = lax.iota(jnp.int32, corr_count)
    lead = jnp.where(
        (peers == corr_place - 1)[:, None],
        head[None, :],
        jnp.where((peers == corr_place + 1)[:, None], tail[None, :], jnp.zeros_like(head)[None, :]),
    )
    parcels = jnp.concatenate(
        [lead, jnp.broadcast_to(own_templates[None, :], (corr_count, own_templates.shape[0]))], axis=1
    )
    arrived = lax.all_to_all(parcels, "corr", 0, 0, tiled=True)
    previous = lax.dynamic_index_in_dim(arrived, jnp.maximum(corr_place - 1, 0), 0, keepdims=False)
    following = lax.dynamic_index_in_dim(
        arrived, jnp.minimum(corr_place + 1, corr_count - 1), 0, keepdims=False
    )
    history = previous[: tail.shape[0]][: local_stations * 3 * 128].reshape(local_stations, 3, 128)
    history = jnp.where(corr_place > 0, history, jnp.zeros_like(history))
    ahead = following[: head.shape[0]].reshape(local_stations, 3, 512)
    ahead = jnp.where(corr_place < corr_count - 1, ahead, jnp.zeros_like(ahead))
    gathered_templates = arrived[:, head.shape[0] :].reshape(
        corr_count * templates.shape[0], templates.shape[1]
    )
    extended = jnp.concatenate([history, live, ahead], axis=2).reshape(
        local_stations * 3, raw_width + 640
    )
    decimated = raw_width // DEC
    blocks = decimated // 128 + 1
    frames = jnp.stack(
        [extended[:, 512 * a : 512 * a + 640] for a in range(blocks)], axis=1
    ).reshape(local_stations * 3 * blocks, 640)
    ring = jnp.concatenate(
        [jnp.zeros((65,), taps.dtype), taps[::-1], jnp.zeros((644 - 129,), taps.dtype)]
    )
    bank = jnp.tile(ring, 128)[: 128 * 640].reshape(128, 640)
    filtered = lax.dot_general(
        frames, bank, (((1,), (1,)), ((), ())), preferred_element_type=jnp.float32
    )
    filtered = filtered.astype(jnp.bfloat16).reshape(local_stations * 3, decimated + 128)
    past_end = (corr_place == corr_count - 1) & (lax.iota(jnp.int32, decimated + 128) >= decimated)
    filtered = jnp.where(past_end[None, :], jnp.zeros_like(filtered), filtered)
    per_block = corr_count // filt_count
    block = per_block * decimated
    width = block // corr_count
    span = width + 128
    received = []
    for k in range(filt_count):
        piece = (filt_place + k) % filt_count
        part = lax.dynamic_slice_in_dim(filtered, piece * width, span, 1)
        route = []
        for c in range(corr_count):
            for f in range(filt_count):
                dest = ((c % per_block) * filt_count + (f + k) % filt_count) * filt_count + c // per_block
                route.append((c * filt_count + f, dest))
        received.append(lax.ppermute(part, ("corr", "filt"), route))
    received = jnp.stack(received, axis=0)
    order = (corr_place - lax.iota(jnp.int32, filt_count)) % filt_count
    rows = jnp.take(received, order, axis=0).reshape(filt_count * filtered.shape[0], span)
    energy = window_energy(rows.astype(jnp.float32), width)
    inv = lax.rsqrt(jnp.maximum(energy, 1.0))
    tile = min(TT, width)
    tiles = width // tile
    windows = jnp.stack([rows[:, i * tile : i * tile + tile + 128] for i in range(tiles)], axis=0)

    local_count = templates.shape[0]
    templates = gathered_templates
    count = templates.shape[0]
    stations = masks.shape[2]
    shaped = templates.astype(jnp.float32).reshape(count, 3, L)
    norms = jnp.sqrt(jnp.sum(shaped * shaped, axis=2) + 1e-06)
    base = shaped / norms[:, :, None]
    chosen = masks.astype(jnp.float32)
    full = jnp.transpose(base, (0, 2, 1))[:, :, None, :] * jnp.transpose(chosen, (0, 2, 1))[:, None, :, :]
    full = full.astype(jnp.bfloat16).reshape(count, L, stations * 3)
    full = jnp.concatenate([full, jnp.zeros((count, JP - L, stations * 3), full.dtype)], axis=1)
    total_rows = stations * 3
    row_block = 96 if total_rows % 96 == 0 else total_rows
    chunks = total_rows // row_block
    weights = (
        full.reshape(count, JP, chunks, row_block)
        .transpose(0, 2, 1, 3)
        .reshape(count, chunks * JP * row_block)
    )
    stacked = correlate(windows, inv, weights, row_block)
    pieces = [lax.dynamic_slice_in_dim(stacked, corr_place * local_count, local_count, 0)]
    for d in range(1, corr_count):
        target = (corr_place + d) % corr_count
        part = lax.dynamic_slice_in_dim(stacked, target * local_count, local_count, 0)
        route = [(i, (i + d) % corr_count) for i in range(corr_count)]
        pieces.append(lax.ppermute(part, "corr", route))
    pieces = jnp.stack(pieces, axis=0)
    order = (corr_place - lax.iota(jnp.int32, corr_count)) % corr_count
    stacked = jnp.take(pieces, order, axis=0)
    stacked = jnp.transpose(stacked, (1, 0, 2)).reshape(local_count, corr_count * width)
    return stacked[None]


def solution(mesh):
    return jax.shard_map(
        body,
        mesh=mesh,
        in_specs=(
            P(("groups", "pair"), "filt", None, "corr"),
            P(("groups", "pair"), "filt"),
            P(),
            P("corr", None),
            P(),
        ),
        out_specs=P(("groups", "pair"), "corr", "filt"),
        check_vma=False,
    )
```

```python
import functools

import jax
import jax.numpy as jnp
from jax import lax
from jax.experimental import pallas as pl
from jax.experimental.pallas import tpu as pltpu
from jax.sharding import PartitionSpec as P

L = 75
TAPS = 64
DEC = 4
JP = 76
TT = 512
RSUB = 16


def from_behind(block, axis, distance):
    devices = range(lax.axis_size(axis))
    route = [(i - distance, i) for i in devices if i - distance in devices]
    return lax.ppermute(block, axis, route)


def window_energy(rows, width):
    p1 = rows * rows
    p2 = p1[:, :-1] + p1[:, 1:]
    p4 = p2[:, :-2] + p2[:, 2:]
    p8 = p4[:, :-4] + p4[:, 4:]
    p16 = p8[:, :-8] + p8[:, 8:]
    p32 = p16[:, :-16] + p16[:, 16:]
    p64 = p32[:, :-32] + p32[:, 32:]
    return (
        p64[:, :width]
        + p8[:, 64 : 64 + width]
        + p2[:, 72 : 72 + width]
        + p1[:, 74 : 74 + width]
    )


def corr_kernel(f_ref, inv_ref, w_ref, o_ref, s_ref, *, row_block, tile):
    q = pl.program_id(1)
    span = tile + 128

    def fill(sub, carry):
        r0 = pl.multiple_of(sub * RSUB, RSUB)
        seg = f_ref[0, pl.ds(r0, RSUB), :].astype(jnp.float32)
        inv = inv_ref[pl.ds(r0, RSUB), :]
        for j in range(JP):
            moved = seg if j == 0 else pltpu.roll(seg, span - j, 1)
            piece = (moved[:, :tile] * inv).astype(jnp.bfloat16)
            s_ref[pl.ds(pl.multiple_of(j * row_block + r0, RSUB), RSUB), :] = piece
        return carry

    lax.fori_loop(0, row_block // RSUB, fill, 0)
    part = jnp.dot(w_ref[...], s_ref[...], preferred_element_type=jnp.float32)

    @pl.when(q == 0)
    def _():
        o_ref[...] = part

    @pl.when(q > 0)
    def _():
        o_ref[...] += part


def correlate(windows, inv, weights, row_block):
    tiles, rows, span = windows.shape
    count = weights.shape[0]
    width = inv.shape[1]
    tile = width // tiles
    chunks = rows // row_block
    return pl.pallas_call(
        functools.partial(corr_kernel, row_block=row_block, tile=tile),
        grid=(tiles, chunks),
        in_specs=[
            pl.BlockSpec((1, row_block, span), lambda i, q: (i, q, 0)),
            pl.BlockSpec((row_block, tile), lambda i, q: (q, i)),
            pl.BlockSpec((count, JP * row_block), lambda i, q: (0, q)),
        ],
        out_specs=pl.BlockSpec((count, tile), lambda i, q: (0, i)),
        out_shape=jax.ShapeDtypeStruct((count, width), jnp.float32),
        scratch_shapes=[pltpu.VMEM((JP * row_block, tile), jnp.bfloat16)],
        compiler_params=pltpu.CompilerParams(
            dimension_semantics=("parallel", "arbitrary"),
            vmem_limit_bytes=48 * 1024 * 1024,
        ),
    )(windows, inv, weights)


def body(raw_rows, valid_counts, taps, templates, masks):
    samples = raw_rows[0]
    counts = valid_counts[0]
    local_stations = samples.shape[0]
    raw_width = samples.shape[2]
    corr_place = lax.axis_index("corr")
    filt_place = lax.axis_index("filt")
    filt_count = lax.axis_size("filt")
    sample_times = corr_place * raw_width + lax.iota(jnp.int32, raw_width)
    dense = samples.reshape(local_stations * 3, raw_width)
    row_counts = jnp.repeat(counts, 3)
    live = jnp.where(sample_times[None, :] < row_counts[:, None], dense, jnp.zeros_like(dense))
    history = from_behind(live[:, raw_width - 128 :], "corr", 1)
    corr_count = lax.axis_size("corr")
    ahead = from_behind(live[:, :512], "corr", -1)
    extended = jnp.concatenate([history, live, ahead], axis=1)
    decimated = raw_width // DEC
    blocks = decimated // 128 + 1
    frames = jnp.stack(
        [extended[:, 512 * a : 512 * a + 640] for a in range(blocks)], axis=1
    ).reshape(local_stations * 3 * blocks, 640)
    flip = (lax.iota(jnp.int32, TAPS)[:, None] + lax.iota(jnp.int32, TAPS)[None, :] == TAPS - 1)
    reversed_taps = jnp.dot(
        taps[None, :], flip.astype(taps.dtype), preferred_element_type=jnp.float32
    )[0].astype(taps.dtype)
    ring = jnp.concatenate(
        [jnp.zeros((65,), taps.dtype), reversed_taps, jnp.zeros((644 - 129,), taps.dtype)]
    )
    bank = jnp.tile(ring, 128)[: 128 * 640].reshape(128, 640)
    filtered = lax.dot_general(
        frames, bank, (((1,), (1,)), ((), ())), preferred_element_type=jnp.float32
    )
    filtered = filtered.astype(jnp.bfloat16).reshape(local_stations * 3, decimated + 128)
    past_end = (corr_place == corr_count - 1) & (lax.iota(jnp.int32, decimated + 128) >= decimated)
    filtered = jnp.where(past_end[None, :], jnp.zeros_like(filtered), filtered)
    per_block = corr_count // filt_count
    block = per_block * decimated
    width = block // corr_count
    span = width + 128
    received = []
    for k in range(filt_count):
        piece = (filt_place + k) % filt_count
        part = lax.dynamic_slice_in_dim(filtered, piece * width, span, 1)
        route = []
        for c in range(corr_count):
            for f in range(filt_count):
                dest = ((c % per_block) * filt_count + (f + k) % filt_count) * filt_count + c // per_block
                route.append((c * filt_count + f, dest))
        received.append(lax.ppermute(part, ("corr", "filt"), route))
    rows = jnp.concatenate(received, axis=0)
    energy = window_energy(rows.astype(jnp.float32), width)
    inv = lax.rsqrt(jnp.maximum(energy, 1.0))
    tile = min(TT, width)
    tiles = width // tile
    windows = jnp.stack([rows[:, i * tile : i * tile + tile + 128] for i in range(tiles)], axis=0)

    local_count = templates.shape[0]
    template_width = templates.shape[1]
    lanes = -(-template_width // 128) * 128
    wide = jnp.concatenate(
        [templates, jnp.zeros((local_count, lanes - template_width), templates.dtype)], axis=1
    )
    copies = jnp.broadcast_to(wide[None], (corr_count,) + wide.shape)
    templates = lax.all_to_all(copies, "corr", 0, 0, tiled=True).reshape(
        corr_count * local_count, lanes
    )[:, :template_width]
    count = templates.shape[0]
    stations = masks.shape[2]
    shaped = templates.astype(jnp.float32).reshape(count, 3, L)
    norms = jnp.sqrt(jnp.sum(shaped * shaped, axis=2) + 1e-06)
    base = shaped / norms[:, :, None]
    arrival = (corr_place - lax.iota(jnp.int32, filt_count)) % filt_count
    chosen = jnp.take(masks.reshape(count, 3, filt_count, stations // filt_count), arrival, axis=2)
    chosen = chosen.reshape(count, 3, stations).astype(jnp.float32)
    full = jnp.transpose(base, (0, 2, 1))[:, :, None, :] * jnp.transpose(chosen, (0, 2, 1))[:, None, :, :]
    full = full.astype(jnp.bfloat16).reshape(count, L, stations * 3)
    full = jnp.concatenate([full, jnp.zeros((count, JP - L, stations * 3), full.dtype)], axis=1)
    total_rows = stations * 3
    row_block = 96 if total_rows % 96 == 0 else total_rows
    chunks = total_rows // row_block
    weights = (
        full.reshape(count, JP, chunks, row_block)
        .transpose(0, 2, 1, 3)
        .reshape(count, chunks * JP * row_block)
    )
    stacked = correlate(windows, inv, weights, row_block)
    pieces = [lax.dynamic_slice_in_dim(stacked, corr_place * local_count, local_count, 0)]
    for d in range(1, corr_count):
        target = (corr_place + d) % corr_count
        part = lax.dynamic_slice_in_dim(stacked, target * local_count, local_count, 0)
        route = [(i, (i + d) % corr_count) for i in range(corr_count)]
        pieces.append(lax.ppermute(part, "corr", route))
    stacked = jnp.zeros((local_count, corr_count * width), jnp.float32)
    for d, part in enumerate(pieces):
        place = ((corr_place - d) % corr_count) * width
        stacked = lax.dynamic_update_slice_in_dim(stacked, part, place, 1)
    return stacked[None]


def solution(mesh):
    return jax.shard_map(
        body,
        mesh=mesh,
        in_specs=(
            P(("groups", "pair"), "filt", None, "corr"),
            P(("groups", "pair"), "filt"),
            P(),
            P("corr", None),
            P(),
        ),
        out_specs=P(("groups", "pair"), "corr", "filt"),
        check_vma=False,
    )
```

```python
import functools

import jax
import jax.numpy as jnp
from jax import lax
from jax.experimental import pallas as pl
from jax.experimental.pallas import tpu as pltpu
from jax.sharding import PartitionSpec as P

L = 75
TAPS = 64
DEC = 4
JP = 76
TT = 512
RSUB = 16


def from_behind(block, axis, distance):
    devices = range(lax.axis_size(axis))
    route = [(i - distance, i) for i in devices if i - distance in devices]
    return lax.ppermute(block, axis, route)


def window_energy(rows, width):
    p1 = rows * rows
    p2 = p1[:, :-1] + p1[:, 1:]
    p4 = p2[:, :-2] + p2[:, 2:]
    p8 = p4[:, :-4] + p4[:, 4:]
    p16 = p8[:, :-8] + p8[:, 8:]
    p32 = p16[:, :-16] + p16[:, 16:]
    p64 = p32[:, :-32] + p32[:, 32:]
    return (
        p64[:, :width]
        + p8[:, 64 : 64 + width]
        + p2[:, 72 : 72 + width]
        + p1[:, 74 : 74 + width]
    )


def corr_kernel(f_ref, inv_ref, w_ref, o_ref, s_ref, *, row_block, tile):
    q = pl.program_id(1)
    span = tile + 128

    def fill(sub, carry):
        r0 = pl.multiple_of(sub * RSUB, RSUB)
        seg = f_ref[0, pl.ds(r0, RSUB), :].astype(jnp.float32)
        inv = inv_ref[pl.ds(r0, RSUB), :]
        for j in range(JP):
            moved = seg if j == 0 else pltpu.roll(seg, span - j, 1)
            piece = (moved[:, :tile] * inv).astype(jnp.bfloat16)
            s_ref[pl.ds(pl.multiple_of(j * row_block + r0, RSUB), RSUB), :] = piece
        return carry

    lax.fori_loop(0, row_block // RSUB, fill, 0)
    part = jnp.dot(w_ref[...], s_ref[...], preferred_element_type=jnp.float32)

    @pl.when(q == 0)
    def _():
        o_ref[...] = part

    @pl.when(q > 0)
    def _():
        o_ref[...] += part


def correlate(windows, inv, weights, row_block):
    tiles, rows, span = windows.shape
    count = weights.shape[0]
    width = inv.shape[1]
    tile = width // tiles
    chunks = rows // row_block
    return pl.pallas_call(
        functools.partial(corr_kernel, row_block=row_block, tile=tile),
        grid=(tiles, chunks),
        in_specs=[
            pl.BlockSpec((1, row_block, span), lambda i, q: (i, q, 0)),
            pl.BlockSpec((row_block, tile), lambda i, q: (q, i)),
            pl.BlockSpec((count, JP * row_block), lambda i, q: (0, q)),
        ],
        out_specs=pl.BlockSpec((count, tile), lambda i, q: (0, i)),
        out_shape=jax.ShapeDtypeStruct((count, width), jnp.float32),
        scratch_shapes=[pltpu.VMEM((JP * row_block, tile), jnp.bfloat16)],
        compiler_params=pltpu.CompilerParams(
            dimension_semantics=("parallel", "arbitrary"),
            vmem_limit_bytes=48 * 1024 * 1024,
        ),
    )(windows, inv, weights)


def body(raw_rows, valid_counts, taps, templates, masks):
    samples = raw_rows[0]
    counts = valid_counts[0]
    local_stations = samples.shape[0]
    raw_width = samples.shape[2]
    corr_place = lax.axis_index("corr")
    filt_place = lax.axis_index("filt")
    filt_count = lax.axis_size("filt")
    sample_times = corr_place * raw_width + lax.iota(jnp.int32, raw_width)
    keep = sample_times[None, None, :] < counts[:, None, None]
    zero = jnp.zeros((), samples.dtype)
    own_tail = jnp.where(keep[:, :, raw_width - 128 :], samples[:, :, raw_width - 128 :], zero)
    own_head = jnp.where(keep[:, :, :512], samples[:, :, :512], zero)
    history = from_behind(own_tail, "corr", 1)
    corr_count = lax.axis_size("corr")
    ahead = from_behind(own_head, "corr", -1)
    live = jnp.where(keep, samples, zero)
    extended = jnp.concatenate([history, live, ahead], axis=2)
    decimated = raw_width // DEC
    blocks = decimated // 128 + 1
    frames = jnp.stack(
        [extended[:, :, 512 * a : 512 * a + 640] for a in range(blocks)], axis=2
    ).reshape(local_stations * 3 * blocks, 640)
    flip = (lax.iota(jnp.int32, TAPS)[:, None] + lax.iota(jnp.int32, TAPS)[None, :] == TAPS - 1)
    reversed_taps = jnp.dot(
        taps[None, :], flip.astype(taps.dtype), preferred_element_type=jnp.float32
    )[0].astype(taps.dtype)
    ring = jnp.concatenate(
        [jnp.zeros((65,), taps.dtype), reversed_taps, jnp.zeros((644 - 129,), taps.dtype)]
    )
    bank = jnp.tile(ring, 128)[: 128 * 640].reshape(128, 640)
    filtered = lax.dot_general(
        frames, bank, (((1,), (1,)), ((), ())), preferred_element_type=jnp.float32
    )
    filtered = filtered.astype(jnp.bfloat16).reshape(local_stations * 3, decimated + 128)
    past_end = (corr_place == corr_count - 1) & (lax.iota(jnp.int32, decimated + 128) >= decimated)
    filtered = jnp.where(past_end[None, :], jnp.zeros_like(filtered), filtered)
    per_block = corr_count // filt_count
    block = per_block * decimated
    width = block // corr_count
    span = width + 128
    received = []
    for k in range(filt_count):
        piece = (filt_place + k) % filt_count
        part = lax.dynamic_slice_in_dim(filtered, piece * width, span, 1)
        route = []
        for c in range(corr_count):
            for f in range(filt_count):
                dest = ((c % per_block) * filt_count + (f + k) % filt_count) * filt_count + c // per_block
                route.append((c * filt_count + f, dest))
        received.append(lax.ppermute(part, ("corr", "filt"), route))
    rows = jnp.concatenate(received, axis=0)
    energy = window_energy(rows.astype(jnp.float32), width)
    inv = lax.rsqrt(jnp.maximum(energy, 1.0))
    tile = min(TT, width)
    tiles = width // tile
    windows = jnp.stack([rows[:, i * tile : i * tile + tile + 128] for i in range(tiles)], axis=0)

    local_count = templates.shape[0]
    template_width = templates.shape[1]
    lanes = -(-template_width // 128) * 128
    wide = jnp.concatenate(
        [templates, jnp.zeros((local_count, lanes - template_width), templates.dtype)], axis=1
    )
    copies = jnp.broadcast_to(wide[None], (corr_count,) + wide.shape)
    templates = lax.all_to_all(copies, "corr", 0, 0, tiled=True).reshape(
        corr_count * local_count, lanes
    )[:, :template_width]
    count = templates.shape[0]
    stations = masks.shape[2]
    shaped = templates.astype(jnp.float32).reshape(count, 3, L)
    norms = jnp.sqrt(jnp.sum(shaped * shaped, axis=2) + 1e-06)
    base = shaped / norms[:, :, None]
    arrival = (corr_place - lax.iota(jnp.int32, filt_count)) % filt_count
    blocked = masks.reshape(count, 3, filt_count, stations // filt_count)
    chosen = jnp.zeros_like(blocked)
    for k in range(filt_count):
        for g in range(filt_count):
            chosen = chosen.at[:, :, k].add(jnp.where(arrival[k] == g, blocked[:, :, g], 0))
    chosen = chosen.reshape(count, 3, stations).astype(jnp.float32)
    full = jnp.transpose(base, (0, 2, 1))[:, :, None, :] * jnp.transpose(chosen, (0, 2, 1))[:, None, :, :]
    full = full.astype(jnp.bfloat16).reshape(count, L, stations * 3)
    full = jnp.concatenate([full, jnp.zeros((count, JP - L, stations * 3), full.dtype)], axis=1)
    total_rows = stations * 3
    row_block = 96 if total_rows % 96 == 0 else total_rows
    chunks = total_rows // row_block
    weights = (
        full.reshape(count, JP, chunks, row_block)
        .transpose(0, 2, 1, 3)
        .reshape(count, chunks * JP * row_block)
    )
    stacked = correlate(windows, inv, weights, row_block)
    pieces = [lax.dynamic_slice_in_dim(stacked, corr_place * local_count, local_count, 0)]
    for d in range(1, corr_count):
        target = (corr_place + d) % corr_count
        part = lax.dynamic_slice_in_dim(stacked, target * local_count, local_count, 0)
        route = [(i, (i + d) % corr_count) for i in range(corr_count)]
        pieces.append(lax.ppermute(part, "corr", route))
    stacked = jnp.zeros((local_count, corr_count * width), jnp.float32)
    for d, part in enumerate(pieces):
        place = ((corr_place - d) % corr_count) * width
        stacked = lax.dynamic_update_slice_in_dim(stacked, part, place, 1)
    return stacked[None]


def solution(mesh):
    return jax.shard_map(
        body,
        mesh=mesh,
        in_specs=(
            P(("groups", "pair"), "filt", None, "corr"),
            P(("groups", "pair"), "filt"),
            P(),
            P("corr", None),
            P(),
        ),
        out_specs=P(("groups", "pair"), "corr", "filt"),
        check_vma=False,
    )
```

```python
import functools

import jax
import jax.numpy as jnp
from jax import lax
from jax.experimental import pallas as pl
from jax.experimental.pallas import tpu as pltpu
from jax.sharding import PartitionSpec as P

L = 75
TAPS = 64
DEC = 4
JP = 76
TT = 512
RSUB = 16


def from_behind(block, axis, distance):
    devices = range(lax.axis_size(axis))
    route = [(i - distance, i) for i in devices if i - distance in devices]
    return lax.ppermute(block, axis, route)


def window_energy(rows, width):
    p1 = rows * rows
    p2 = p1[:, :-1] + p1[:, 1:]
    p4 = p2[:, :-2] + p2[:, 2:]
    p8 = p4[:, :-4] + p4[:, 4:]
    p16 = p8[:, :-8] + p8[:, 8:]
    p32 = p16[:, :-16] + p16[:, 16:]
    p64 = p32[:, :-32] + p32[:, 32:]
    return (
        p64[:, :width]
        + p8[:, 64 : 64 + width]
        + p2[:, 72 : 72 + width]
        + p1[:, 74 : 74 + width]
    )


def corr_kernel(f_ref, inv_ref, w_ref, o_ref, s_ref, *, row_block, tile):
    q = pl.program_id(1)
    span = tile + 128

    def fill(sub, carry):
        r0 = pl.multiple_of(sub * RSUB, RSUB)
        seg = f_ref[0, pl.ds(r0, RSUB), :].astype(jnp.float32)
        inv = inv_ref[pl.ds(r0, RSUB), :]
        for j in range(JP):
            moved = seg if j == 0 else pltpu.roll(seg, span - j, 1)
            piece = (moved[:, :tile] * inv).astype(jnp.bfloat16)
            s_ref[pl.ds(pl.multiple_of(j * row_block + r0, RSUB), RSUB), :] = piece
        return carry

    lax.fori_loop(0, row_block // RSUB, fill, 0)
    part = jnp.dot(w_ref[...], s_ref[...], preferred_element_type=jnp.float32)

    @pl.when(q == 0)
    def _():
        o_ref[...] = part

    @pl.when(q > 0)
    def _():
        o_ref[...] += part


def correlate(windows, inv, weights, row_block):
    tiles, rows, span = windows.shape
    count = weights.shape[0]
    width = inv.shape[1]
    tile = width // tiles
    chunks = rows // row_block
    return pl.pallas_call(
        functools.partial(corr_kernel, row_block=row_block, tile=tile),
        grid=(tiles, chunks),
        in_specs=[
            pl.BlockSpec((1, row_block, span), lambda i, q: (i, q, 0)),
            pl.BlockSpec((row_block, tile), lambda i, q: (q, i)),
            pl.BlockSpec((count, JP * row_block), lambda i, q: (0, q)),
        ],
        out_specs=pl.BlockSpec((count, tile), lambda i, q: (0, i)),
        out_shape=jax.ShapeDtypeStruct((count, width), jnp.float32),
        scratch_shapes=[pltpu.VMEM((JP * row_block, tile), jnp.bfloat16)],
        compiler_params=pltpu.CompilerParams(
            dimension_semantics=("parallel", "arbitrary"),
            vmem_limit_bytes=48 * 1024 * 1024,
        ),
    )(windows, inv, weights)


def body(raw_rows, valid_counts, taps, templates, masks):
    samples = raw_rows[0]
    counts = valid_counts[0]
    local_stations = samples.shape[0]
    raw_width = samples.shape[2]
    corr_place = lax.axis_index("corr")
    filt_place = lax.axis_index("filt")
    filt_count = lax.axis_size("filt")
    sample_times = corr_place * raw_width + lax.iota(jnp.int32, raw_width)
    dense = samples.reshape(local_stations * 3, raw_width)
    row_counts = jnp.repeat(counts, 3)
    live = jnp.where(sample_times[None, :] < row_counts[:, None], dense, jnp.zeros_like(dense))
    history = from_behind(live[:, raw_width - 128 :], "corr", 1)
    corr_count = lax.axis_size("corr")
    ahead = from_behind(live[:, :512], "corr", -1)
    extended = jnp.concatenate([history, live, ahead], axis=1)
    decimated = raw_width // DEC
    blocks = decimated // 128 + 1
    frames = jnp.stack(
        [extended[:, 512 * a : 512 * a + 640] for a in range(blocks)], axis=1
    ).reshape(local_stations * 3 * blocks, 640)
    flip = (lax.iota(jnp.int32, TAPS)[:, None] + lax.iota(jnp.int32, TAPS)[None, :] == TAPS - 1)
    reversed_taps = jnp.dot(
        taps[None, :], flip.astype(taps.dtype), preferred_element_type=jnp.float32
    )[0].astype(taps.dtype)
    ring = jnp.concatenate(
        [jnp.zeros((65,), taps.dtype), reversed_taps, jnp.zeros((644 - 129,), taps.dtype)]
    )
    bank = jnp.tile(ring, 128)[: 128 * 640].reshape(128, 640)
    filtered = lax.dot_general(
        frames, bank, (((1,), (1,)), ((), ())), preferred_element_type=jnp.float32
    )
    filtered = filtered.astype(jnp.bfloat16).reshape(local_stations * 3, decimated + 128)
    past_end = (corr_place == corr_count - 1) & (lax.iota(jnp.int32, decimated + 128) >= decimated)
    filtered = jnp.where(past_end[None, :], jnp.zeros_like(filtered), filtered)
    per_block = corr_count // filt_count
    block = per_block * decimated
    width = block // corr_count
    span = width + 128
    received = []
    for k in range(filt_count):
        piece = (filt_place + k) % filt_count
        part = lax.dynamic_slice_in_dim(filtered, piece * width, span, 1)
        route = []
        for c in range(corr_count):
            for f in range(filt_count):
                dest = ((c % per_block) * filt_count + (f + k) % filt_count) * filt_count + c // per_block
                route.append((c * filt_count + f, dest))
        received.append(lax.ppermute(part, ("corr", "filt"), route))
    rows = jnp.concatenate(received, axis=0)
    energy = window_energy(rows.astype(jnp.float32), width)
    inv = lax.rsqrt(jnp.maximum(energy, 1.0))
    tile = min(TT, width)
    tiles = width // tile
    windows = jnp.stack([rows[:, i * tile : i * tile + tile + 128] for i in range(tiles)], axis=0)

    local_count = templates.shape[0]
    template_width = templates.shape[1]
    lanes = -(-template_width // 128) * 128
    wide = jnp.concatenate(
        [templates, jnp.zeros((local_count, lanes - template_width), templates.dtype)], axis=1
    )
    arrived = [wide]
    for d in range(1, corr_count):
        route = [(i, (i + d) % corr_count) for i in range(corr_count)]
        arrived.append(lax.ppermute(wide, "corr", route))
    arrived = jnp.stack(arrived, axis=0)
    order = (corr_place - lax.iota(jnp.int32, corr_count)) % corr_count
    templates = jnp.take(arrived, order, axis=0).reshape(corr_count * local_count, lanes)[
        :, :template_width
    ]
    count = templates.shape[0]
    stations = masks.shape[2]
    shaped = templates.astype(jnp.float32).reshape(count, 3, L)
    norms = jnp.sqrt(jnp.sum(shaped * shaped, axis=2) + 1e-06)
    base = shaped / norms[:, :, None]
    arrival = (corr_place - lax.iota(jnp.int32, filt_count)) % filt_count
    chosen = jnp.take(masks.reshape(count, 3, filt_count, stations // filt_count), arrival, axis=2)
    chosen = chosen.reshape(count, 3, stations).astype(jnp.float32)
    full = jnp.transpose(base, (0, 2, 1))[:, :, None, :] * jnp.transpose(chosen, (0, 2, 1))[:, None, :, :]
    full = full.astype(jnp.bfloat16).reshape(count, L, stations * 3)
    full = jnp.concatenate([full, jnp.zeros((count, JP - L, stations * 3), full.dtype)], axis=1)
    total_rows = stations * 3
    row_block = 96 if total_rows % 96 == 0 else total_rows
    chunks = total_rows // row_block
    weights = (
        full.reshape(count, JP, chunks, row_block)
        .transpose(0, 2, 1, 3)
        .reshape(count, chunks * JP * row_block)
    )
    stacked = correlate(windows, inv, weights, row_block)
    pieces = [lax.dynamic_slice_in_dim(stacked, corr_place * local_count, local_count, 0)]
    for d in range(1, corr_count):
        target = (corr_place + d) % corr_count
        part = lax.dynamic_slice_in_dim(stacked, target * local_count, local_count, 0)
        route = [(i, (i + d) % corr_count) for i in range(corr_count)]
        pieces.append(lax.ppermute(part, "corr", route))
    stacked = jnp.zeros((local_count, corr_count * width), jnp.float32)
    for d, part in enumerate(pieces):
        place = ((corr_place - d) % corr_count) * width
        stacked = lax.dynamic_update_slice_in_dim(stacked, part, place, 1)
    return stacked[None]


def solution(mesh):
    return jax.shard_map(
        body,
        mesh=mesh,
        in_specs=(
            P(("groups", "pair"), "filt", None, "corr"),
            P(("groups", "pair"), "filt"),
            P(),
            P("corr", None),
            P(),
        ),
        out_specs=P(("groups", "pair"), "corr", "filt"),
        check_vma=False,
    )
```

```python
import functools

import jax
import jax.numpy as jnp
from jax import lax
from jax.experimental import pallas as pl
from jax.experimental.pallas import tpu as pltpu
from jax.sharding import PartitionSpec as P

L = 75
TAPS = 64
DEC = 4
JP = 76
TT = 512
RSUB = 16


def from_behind(block, axis, distance):
    devices = range(lax.axis_size(axis))
    route = [(i - distance, i) for i in devices if i - distance in devices]
    return lax.ppermute(block, axis, route)


def window_energy(rows, width):
    p1 = rows * rows
    p2 = p1[:, :-1] + p1[:, 1:]
    p4 = p2[:, :-2] + p2[:, 2:]
    p8 = p4[:, :-4] + p4[:, 4:]
    p16 = p8[:, :-8] + p8[:, 8:]
    p32 = p16[:, :-16] + p16[:, 16:]
    p64 = p32[:, :-32] + p32[:, 32:]
    return (
        p64[:, :width]
        + p8[:, 64 : 64 + width]
        + p2[:, 72 : 72 + width]
        + p1[:, 74 : 74 + width]
    )


def corr_kernel(f_ref, inv_ref, w_ref, o_ref, s_ref, *, row_block, tile):
    q = pl.program_id(1)
    span = tile + 128

    def fill(sub, carry):
        r0 = pl.multiple_of(sub * RSUB, RSUB)
        seg = f_ref[0, pl.ds(r0, RSUB), :].astype(jnp.float32)
        inv = inv_ref[pl.ds(r0, RSUB), :]
        for j in range(JP):
            moved = seg if j == 0 else pltpu.roll(seg, span - j, 1)
            piece = (moved[:, :tile] * inv).astype(jnp.bfloat16)
            s_ref[pl.ds(pl.multiple_of(j * row_block + r0, RSUB), RSUB), :] = piece
        return carry

    lax.fori_loop(0, row_block // RSUB, fill, 0)
    part = jnp.dot(w_ref[...], s_ref[...], preferred_element_type=jnp.float32)

    @pl.when(q == 0)
    def _():
        o_ref[...] = part

    @pl.when(q > 0)
    def _():
        o_ref[...] += part


def correlate(windows, inv, weights, row_block):
    tiles, rows, span = windows.shape
    count = weights.shape[0]
    width = inv.shape[1]
    tile = width // tiles
    chunks = rows // row_block
    return pl.pallas_call(
        functools.partial(corr_kernel, row_block=row_block, tile=tile),
        grid=(tiles, chunks),
        in_specs=[
            pl.BlockSpec((1, row_block, span), lambda i, q: (i, q, 0)),
            pl.BlockSpec((row_block, tile), lambda i, q: (q, i)),
            pl.BlockSpec((count, JP * row_block), lambda i, q: (0, q)),
        ],
        out_specs=pl.BlockSpec((count, tile), lambda i, q: (0, i)),
        out_shape=jax.ShapeDtypeStruct((count, width), jnp.float32),
        scratch_shapes=[pltpu.VMEM((JP * row_block, tile), jnp.bfloat16)],
        compiler_params=pltpu.CompilerParams(
            dimension_semantics=("parallel", "arbitrary"),
            vmem_limit_bytes=48 * 1024 * 1024,
        ),
    )(windows, inv, weights)


def body(raw_rows, valid_counts, taps, templates, masks):
    samples = raw_rows[0]
    counts = valid_counts[0]
    local_stations = samples.shape[0]
    raw_width = samples.shape[2]
    corr_place = lax.axis_index("corr")
    filt_place = lax.axis_index("filt")
    filt_count = lax.axis_size("filt")
    sample_times = corr_place * raw_width + lax.iota(jnp.int32, raw_width)
    dense = samples.reshape(local_stations * 3, raw_width)
    row_counts = jnp.repeat(counts, 3)
    live = jnp.where(sample_times[None, :] < row_counts[:, None], dense, jnp.zeros_like(dense))
    history = from_behind(live[:, raw_width - 128 :], "corr", 1)
    corr_count = lax.axis_size("corr")
    ahead = from_behind(live[:, :512], "corr", -1)
    extended = jnp.concatenate([history, live, ahead], axis=1)
    decimated = raw_width // DEC
    blocks = decimated // 128 + 1
    frames = jnp.stack(
        [extended[:, 512 * a : 512 * a + 640] for a in range(blocks)], axis=1
    ).reshape(local_stations * 3 * blocks, 640)
    flip = (lax.iota(jnp.int32, TAPS)[:, None] + lax.iota(jnp.int32, TAPS)[None, :] == TAPS - 1)
    reversed_taps = jnp.dot(
        taps[None, :], flip.astype(taps.dtype), preferred_element_type=jnp.float32
    )[0].astype(taps.dtype)
    ring = jnp.concatenate(
        [jnp.zeros((65,), taps.dtype), reversed_taps, jnp.zeros((644 - 129,), taps.dtype)]
    )
    bank = jnp.tile(ring, 128)[: 128 * 640].reshape(128, 640)
    filtered = lax.dot_general(
        frames, bank, (((1,), (1,)), ((), ())), preferred_element_type=jnp.float32
    )
    filtered = filtered.astype(jnp.bfloat16).reshape(local_stations * 3, decimated + 128)
    past_end = (corr_place == corr_count - 1) & (lax.iota(jnp.int32, decimated + 128) >= decimated)
    filtered = jnp.where(past_end[None, :], jnp.zeros_like(filtered), filtered)
    per_block = corr_count // filt_count
    block = per_block * decimated
    halves = per_block // 2
    width = halves * decimated
    span = width + 128
    pairs = corr_count // 2
    partner_of = [(i, i ^ 1) for i in range(corr_count)]
    side = corr_place % 2
    received = []
    for k in range(pairs):
        route = []
        for c in range(corr_count):
            for f in range(filt_count):
                number = (c % halves) * filt_count + f
                h = (c % per_block) // halves
                dest = (2 * ((number + k) % pairs) + h) * filt_count + c // per_block
                route.append((c * filt_count + f, dest))
        received.append(lax.ppermute(filtered, ("corr", "filt"), route))
    pair_place = corr_place // 2
    if halves == 1:
        rows = jnp.concatenate(received, axis=0)
        arrival = (pair_place - lax.iota(jnp.int32, filt_count)) % filt_count
    else:
        order = (pair_place - lax.iota(jnp.int32, pairs)) % pairs
        ordered = jnp.take(jnp.stack(received, axis=0), order, axis=0)
        ordered = ordered.reshape(halves, filt_count, filtered.shape[0], decimated + 128)
        heads = jnp.transpose(ordered[:, :, :, :decimated], (1, 2, 0, 3)).reshape(
            filt_count, filtered.shape[0], width
        )
        tail = ordered[halves - 1, :, :, decimated:]
        rows = jnp.concatenate([heads, tail], axis=2).reshape(filt_count * filtered.shape[0], span)
        arrival = lax.iota(jnp.int32, filt_count)
    energy = window_energy(rows.astype(jnp.float32), width)
    inv = lax.rsqrt(jnp.maximum(energy, 1.0))
    tile = min(TT, width)
    tiles = width // tile
    windows = jnp.stack([rows[:, i * tile : i * tile + tile + 128] for i in range(tiles)], axis=0)

    local_count = templates.shape[0]
    template_width = templates.shape[1]
    lanes = -(-template_width // 128) * 128
    wide = jnp.concatenate(
        [templates, jnp.zeros((local_count, lanes - template_width), templates.dtype)], axis=1
    )
    other = lax.ppermute(wide, "corr", partner_of)
    first = jnp.where(side == 0, wide, other)
    second = jnp.where(side == 0, other, wide)
    templates = jnp.concatenate([first, second], axis=0)[:, :template_width]
    count = templates.shape[0]
    stations = masks.shape[2]
    shaped = templates.astype(jnp.float32).reshape(count, 3, L)
    norms = jnp.sqrt(jnp.sum(shaped * shaped, axis=2) + 1e-06)
    base = shaped / norms[:, :, None]
    masks = lax.dynamic_slice_in_dim(masks, pair_place * count, count, 0)
    chosen = jnp.take(masks.reshape(count, 3, filt_count, stations // filt_count), arrival, axis=2)
    chosen = chosen.reshape(count, 3, stations).astype(jnp.float32)
    full = jnp.transpose(base, (0, 2, 1))[:, :, None, :] * jnp.transpose(chosen, (0, 2, 1))[:, None, :, :]
    full = full.astype(jnp.bfloat16).reshape(count, L, stations * 3)
    full = jnp.concatenate([full, jnp.zeros((count, JP - L, stations * 3), full.dtype)], axis=1)
    total_rows = stations * 3
    row_block = 96 if total_rows % 96 == 0 else total_rows
    chunks = total_rows // row_block
    weights = (
        full.reshape(count, JP, chunks, row_block)
        .transpose(0, 2, 1, 3)
        .reshape(count, chunks * JP * row_block)
    )
    stacked = correlate(windows, inv, weights, row_block)
    mine = lax.dynamic_slice_in_dim(stacked, side * local_count, local_count, 0)
    theirs = lax.dynamic_slice_in_dim(stacked, (1 - side) * local_count, local_count, 0)
    back = lax.ppermute(theirs, "corr", partner_of)
    stacked = jnp.where(
        side == 0, jnp.concatenate([mine, back], axis=1), jnp.concatenate([back, mine], axis=1)
    )
    return stacked[None]


def solution(mesh):
    return jax.shard_map(
        body,
        mesh=mesh,
        in_specs=(
            P(("groups", "pair"), "filt", None, "corr"),
            P(("groups", "pair"), "filt"),
            P(),
            P("corr", None),
            P(),
        ),
        out_specs=P(("groups", "pair"), "corr", "filt"),
        check_vma=False,
    )
```

```python
import functools

import jax
import jax.numpy as jnp
from jax import lax
from jax.experimental import pallas as pl
from jax.experimental.pallas import tpu as pltpu
from jax.sharding import PartitionSpec as P

L = 75
TAPS = 64
DEC = 4
JP = 76
TT = 512
RSUB = 16


def from_behind(block, axis, distance):
    devices = range(lax.axis_size(axis))
    route = [(i - distance, i) for i in devices if i - distance in devices]
    return lax.ppermute(block, axis, route)


def window_energy(rows, width):
    p1 = rows * rows
    p2 = p1[:, :-1] + p1[:, 1:]
    p4 = p2[:, :-2] + p2[:, 2:]
    p8 = p4[:, :-4] + p4[:, 4:]
    p16 = p8[:, :-8] + p8[:, 8:]
    p32 = p16[:, :-16] + p16[:, 16:]
    p64 = p32[:, :-32] + p32[:, 32:]
    return (
        p64[:, :width]
        + p8[:, 64 : 64 + width]
        + p2[:, 72 : 72 + width]
        + p1[:, 74 : 74 + width]
    )


def corr_kernel(f_ref, inv_ref, w_ref, o_ref, s_ref, *, row_block, tile):
    q = pl.program_id(1)
    span = tile + 128

    def fill(sub, carry):
        r0 = pl.multiple_of(sub * RSUB, RSUB)
        seg = f_ref[0, pl.ds(r0, RSUB), :].astype(jnp.float32)
        inv = inv_ref[pl.ds(r0, RSUB), :]
        for j in range(JP):
            moved = seg if j == 0 else pltpu.roll(seg, span - j, 1)
            piece = (moved[:, :tile] * inv).astype(jnp.bfloat16)
            s_ref[pl.ds(pl.multiple_of(j * row_block + r0, RSUB), RSUB), :] = piece
        return carry

    lax.fori_loop(0, row_block // RSUB, fill, 0)
    part = jnp.dot(w_ref[...], s_ref[...], preferred_element_type=jnp.float32)

    @pl.when(q == 0)
    def _():
        o_ref[...] = part

    @pl.when(q > 0)
    def _():
        o_ref[...] += part


def correlate(windows, inv, weights, row_block):
    tiles, rows, span = windows.shape
    count = weights.shape[0]
    width = inv.shape[1]
    tile = width // tiles
    chunks = rows // row_block
    return pl.pallas_call(
        functools.partial(corr_kernel, row_block=row_block, tile=tile),
        grid=(tiles, chunks),
        in_specs=[
            pl.BlockSpec((1, row_block, span), lambda i, q: (i, q, 0)),
            pl.BlockSpec((row_block, tile), lambda i, q: (q, i)),
            pl.BlockSpec((count, JP * row_block), lambda i, q: (0, q)),
        ],
        out_specs=pl.BlockSpec((count, tile), lambda i, q: (0, i)),
        out_shape=jax.ShapeDtypeStruct((count, width), jnp.float32),
        scratch_shapes=[pltpu.VMEM((JP * row_block, tile), jnp.bfloat16)],
        compiler_params=pltpu.CompilerParams(
            dimension_semantics=("parallel", "arbitrary"),
            vmem_limit_bytes=48 * 1024 * 1024,
        ),
    )(windows, inv, weights)


def body(raw_rows, valid_counts, taps, templates, masks):
    samples = raw_rows[0]
    counts = valid_counts[0]
    local_stations = samples.shape[0]
    raw_width = samples.shape[2]
    corr_place = lax.axis_index("corr")
    filt_place = lax.axis_index("filt")
    filt_count = lax.axis_size("filt")
    sample_times = corr_place * raw_width + lax.iota(jnp.int32, raw_width)
    dense = samples.reshape(local_stations * 3, raw_width)
    row_counts = jnp.repeat(counts, 3)
    live = jnp.where(sample_times[None, :] < row_counts[:, None], dense, jnp.zeros_like(dense))
    history = from_behind(live[:, raw_width - 128 :], "corr", 1)
    corr_count = lax.axis_size("corr")
    ahead = from_behind(live[:, :512], "corr", -1)
    extended = jnp.concatenate([history, live, ahead], axis=1)
    decimated = raw_width // DEC
    blocks = decimated // 128 + 1
    frames = jnp.stack(
        [extended[:, 512 * a : 512 * a + 640] for a in range(blocks)], axis=1
    ).reshape(local_stations * 3 * blocks, 640)
    flip = (lax.iota(jnp.int32, TAPS)[:, None] + lax.iota(jnp.int32, TAPS)[None, :] == TAPS - 1)
    reversed_taps = jnp.dot(
        taps[None, :], flip.astype(taps.dtype), preferred_element_type=jnp.float32
    )[0].astype(taps.dtype)
    ring = jnp.concatenate(
        [jnp.zeros((65,), taps.dtype), reversed_taps, jnp.zeros((644 - 129,), taps.dtype)]
    )
    bank = jnp.tile(ring, 128)[: 128 * 640].reshape(128, 640)
    filtered = lax.dot_general(
        frames, bank, (((1,), (1,)), ((), ())), preferred_element_type=jnp.float32
    )
    filtered = filtered.astype(jnp.bfloat16).reshape(local_stations * 3, decimated + 128)
    past_end = (corr_place == corr_count - 1) & (lax.iota(jnp.int32, decimated + 128) >= decimated)
    filtered = jnp.where(past_end[None, :], jnp.zeros_like(filtered), filtered)
    per_block = corr_count // filt_count
    block = per_block * decimated
    width = block // corr_count
    span = width + 128
    received = []
    for k in range(filt_count):
        piece = (filt_place + k) % filt_count
        part = lax.dynamic_slice_in_dim(filtered, piece * width, span, 1)
        route = []
        for c in range(corr_count):
            for f in range(filt_count):
                dest = ((c % per_block) * filt_count + (f + k) % filt_count) * filt_count + c // per_block
                route.append((c * filt_count + f, dest))
        received.append(lax.ppermute(part, ("corr", "filt"), route))
    rows = jnp.concatenate(received, axis=0)
    energy = window_energy(rows.astype(jnp.float32), width)
    inv = lax.rsqrt(jnp.maximum(energy, 1.0))
    tile = min(TT, width)
    tiles = width // tile
    windows = jnp.stack([rows[:, i * tile : i * tile + tile + 128] for i in range(tiles)], axis=0)

    local_count = templates.shape[0]
    template_width = templates.shape[1]
    lanes = -(-template_width // 128) * 128
    wide = jnp.concatenate(
        [templates, jnp.zeros((local_count, lanes - template_width), templates.dtype)], axis=1
    )
    copies = jnp.broadcast_to(wide[None], (corr_count,) + wide.shape)
    templates = lax.all_to_all(copies, "corr", 0, 0, tiled=True).reshape(
        corr_count * local_count, lanes
    )[:, :template_width]
    count = templates.shape[0]
    stations = masks.shape[2]
    shaped = templates.astype(jnp.float32).reshape(count, 3, L)
    norms = jnp.sqrt(jnp.sum(shaped * shaped, axis=2) + 1e-06)
    base = shaped / norms[:, :, None]
    arrival = (corr_place - lax.iota(jnp.int32, filt_count)) % filt_count
    chosen = jnp.take(masks.reshape(count, 3, filt_count, stations // filt_count), arrival, axis=2)
    chosen = chosen.reshape(count, 3, stations).astype(jnp.float32)
    total_rows = stations * 3
    row_block = 96 if total_rows % 96 == 0 else total_rows
    chunks = total_rows // row_block
    if chunks == 1:
        padded = jnp.concatenate([base, jnp.zeros((count, 3, JP - L), base.dtype)], axis=2)
        padded = padded.astype(jnp.bfloat16).reshape(count, 3 * JP)
        flat = jnp.transpose(chosen, (0, 1, 2)).reshape(count, total_rows).astype(jnp.bfloat16)
        start_zero = lax.optimization_barrier(jnp.zeros((), jnp.int32))
        column = lax.iota(jnp.int32, JP * total_rows) + start_zero
        lag = column // total_rows
        row = column % total_rows
        source = lax.iota(jnp.int32, 3 * JP)
        pick_base = (
            (source[:, None] % JP == lag[None, :]) & (source[:, None] // JP == row[None, :] % 3)
        ).astype(jnp.bfloat16)
        slot = lax.iota(jnp.int32, total_rows)
        pick_mask = (
            (slot[:, None] // stations == row[None, :] % 3)
            & (slot[:, None] % stations == row[None, :] // 3)
        ).astype(jnp.bfloat16)
        spread = jnp.dot(padded, pick_base, preferred_element_type=jnp.float32)
        gate = jnp.dot(flat, pick_mask, preferred_element_type=jnp.float32)
        weights = (spread * gate).astype(jnp.bfloat16)
    else:
        full = jnp.transpose(base, (0, 2, 1))[:, :, None, :] * jnp.transpose(chosen, (0, 2, 1))[:, None, :, :]
        full = full.astype(jnp.bfloat16).reshape(count, L, stations * 3)
        full = jnp.concatenate([full, jnp.zeros((count, JP - L, stations * 3), full.dtype)], axis=1)
        weights = (
            full.reshape(count, JP, chunks, row_block)
            .transpose(0, 2, 1, 3)
            .reshape(count, chunks * JP * row_block)
        )
    stacked = correlate(windows, inv, weights, row_block)
    pieces = [lax.dynamic_slice_in_dim(stacked, corr_place * local_count, local_count, 0)]
    for d in range(1, corr_count):
        target = (corr_place + d) % corr_count
        part = lax.dynamic_slice_in_dim(stacked, target * local_count, local_count, 0)
        route = [(i, (i + d) % corr_count) for i in range(corr_count)]
        pieces.append(lax.ppermute(part, "corr", route))
    stacked = jnp.zeros((local_count, corr_count * width), jnp.float32)
    for d, part in enumerate(pieces):
        place = ((corr_place - d) % corr_count) * width
        stacked = lax.dynamic_update_slice_in_dim(stacked, part, place, 1)
    return stacked[None]


def solution(mesh):
    return jax.shard_map(
        body,
        mesh=mesh,
        in_specs=(
            P(("groups", "pair"), "filt", None, "corr"),
            P(("groups", "pair"), "filt"),
            P(),
            P("corr", None),
            P(),
        ),
        out_specs=P(("groups", "pair"), "corr", "filt"),
        check_vma=False,
    )
```

```python
import functools

import jax
import jax.numpy as jnp
from jax import lax
from jax.experimental import pallas as pl
from jax.experimental.pallas import tpu as pltpu
from jax.sharding import PartitionSpec as P

L = 75
TAPS = 64
DEC = 4
JP = 76
TT = 512
RSUB = 16


def from_behind(block, axis, distance):
    devices = range(lax.axis_size(axis))
    route = [(i - distance, i) for i in devices if i - distance in devices]
    return lax.ppermute(block, axis, route)


def window_energy(rows, width):
    p1 = rows * rows
    p2 = p1[:, :-1] + p1[:, 1:]
    p4 = p2[:, :-2] + p2[:, 2:]
    p8 = p4[:, :-4] + p4[:, 4:]
    p16 = p8[:, :-8] + p8[:, 8:]
    p32 = p16[:, :-16] + p16[:, 16:]
    p64 = p32[:, :-32] + p32[:, 32:]
    return (
        p64[:, :width]
        + p8[:, 64 : 64 + width]
        + p2[:, 72 : 72 + width]
        + p1[:, 74 : 74 + width]
    )


def corr_kernel(f_ref, inv_ref, w_ref, o_ref, s_ref, *, row_block, tile):
    q = pl.program_id(1)
    span = tile + 128

    def fill(sub, carry):
        r0 = pl.multiple_of(sub * RSUB, RSUB)
        seg = f_ref[0, pl.ds(r0, RSUB), :].astype(jnp.float32)
        inv = inv_ref[pl.ds(r0, RSUB), :]
        for j in range(JP):
            moved = seg if j == 0 else pltpu.roll(seg, span - j, 1)
            piece = (moved[:, :tile] * inv).astype(jnp.bfloat16)
            s_ref[pl.ds(pl.multiple_of(j * row_block + r0, RSUB), RSUB), :] = piece
        return carry

    lax.fori_loop(0, row_block // RSUB, fill, 0)
    part = jnp.dot(w_ref[...], s_ref[...], preferred_element_type=jnp.float32)

    @pl.when(q == 0)
    def _():
        o_ref[...] = part

    @pl.when(q > 0)
    def _():
        o_ref[...] += part


def correlate(windows, inv, weights, row_block):
    tiles, rows, span = windows.shape
    count = weights.shape[0]
    width = inv.shape[1]
    tile = width // tiles
    chunks = rows // row_block
    return pl.pallas_call(
        functools.partial(corr_kernel, row_block=row_block, tile=tile),
        grid=(tiles, chunks),
        in_specs=[
            pl.BlockSpec((1, row_block, span), lambda i, q: (i, q, 0)),
            pl.BlockSpec((row_block, tile), lambda i, q: (q, i)),
            pl.BlockSpec((count, JP * row_block), lambda i, q: (0, q)),
        ],
        out_specs=pl.BlockSpec((count, tile), lambda i, q: (0, i)),
        out_shape=jax.ShapeDtypeStruct((count, width), jnp.float32),
        scratch_shapes=[pltpu.VMEM((JP * row_block, tile), jnp.bfloat16)],
        compiler_params=pltpu.CompilerParams(
            dimension_semantics=("parallel", "arbitrary"),
            vmem_limit_bytes=48 * 1024 * 1024,
        ),
    )(windows, inv, weights)


def body(raw_rows, valid_counts, taps, templates, masks):
    samples = raw_rows[0]
    counts = valid_counts[0]
    local_stations = samples.shape[0]
    raw_width = samples.shape[2]
    corr_place = lax.axis_index("corr")
    filt_place = lax.axis_index("filt")
    filt_count = lax.axis_size("filt")
    sample_times = corr_place * raw_width + lax.iota(jnp.int32, raw_width)
    keep = sample_times[None, None, :] < counts[:, None, None]
    live = jnp.where(keep, samples, jnp.zeros_like(samples)).reshape(local_stations * 3, raw_width)
    history = from_behind(live[:, raw_width - 128 :], "corr", 1)
    corr_count = lax.axis_size("corr")
    ahead = from_behind(live[:, :512], "corr", -1)
    extended = jnp.concatenate([history, live, ahead], axis=1)
    decimated = raw_width // DEC
    blocks = decimated // 128 + 1
    frames = jnp.stack(
        [extended[:, 512 * a : 512 * a + 640] for a in range(blocks)], axis=1
    ).reshape(local_stations * 3 * blocks, 640)
    flip = (lax.iota(jnp.int32, TAPS)[:, None] + lax.iota(jnp.int32, TAPS)[None, :] == TAPS - 1)
    reversed_taps = jnp.dot(
        taps[None, :], flip.astype(taps.dtype), preferred_element_type=jnp.float32
    )[0].astype(taps.dtype)
    ring = jnp.concatenate(
        [jnp.zeros((65,), taps.dtype), reversed_taps, jnp.zeros((644 - 129,), taps.dtype)]
    )
    bank = jnp.tile(ring, 128)[: 128 * 640].reshape(128, 640)
    filtered = lax.dot_general(
        frames, bank, (((1,), (1,)), ((), ())), preferred_element_type=jnp.float32
    )
    filtered = filtered.astype(jnp.bfloat16).reshape(local_stations * 3, decimated + 128)
    past_end = (corr_place == corr_count - 1) & (lax.iota(jnp.int32, decimated + 128) >= decimated)
    filtered = jnp.where(past_end[None, :], jnp.zeros_like(filtered), filtered)
    per_block = corr_count // filt_count
    block = per_block * decimated
    width = block // corr_count
    span = width + 128
    received = []
    for k in range(filt_count):
        piece = (filt_place + k) % filt_count
        part = lax.dynamic_slice_in_dim(filtered, piece * width, span, 1)
        route = []
        for c in range(corr_count):
            for f in range(filt_count):
                dest = ((c % per_block) * filt_count + (f + k) % filt_count) * filt_count + c // per_block
                route.append((c * filt_count + f, dest))
        received.append(lax.ppermute(part, ("corr", "filt"), route))
    rows = jnp.concatenate(received, axis=0)
    energy = window_energy(rows.astype(jnp.float32), width)
    inv = lax.rsqrt(jnp.maximum(energy, 1.0))
    tile = min(TT, width)
    tiles = width // tile
    windows = jnp.stack([rows[:, i * tile : i * tile + tile + 128] for i in range(tiles)], axis=0)

    local_count = templates.shape[0]
    template_width = templates.shape[1]
    lanes = -(-template_width // 128) * 128
    wide = jnp.concatenate(
        [templates, jnp.zeros((local_count, lanes - template_width), templates.dtype)], axis=1
    )
    copies = jnp.broadcast_to(wide[None], (corr_count,) + wide.shape)
    templates = lax.all_to_all(copies, "corr", 0, 0, tiled=True).reshape(
        corr_count * local_count, lanes
    )[:, :template_width]
    count = templates.shape[0]
    stations = masks.shape[2]
    shaped = templates.astype(jnp.float32).reshape(count, 3, L)
    norms = jnp.sqrt(jnp.sum(shaped * shaped, axis=2) + 1e-06)
    base = shaped / norms[:, :, None]
    arrival = (corr_place - lax.iota(jnp.int32, filt_count)) % filt_count
    blocked = masks.reshape(count, 3, filt_count, stations // filt_count)
    if filt_count == 2:
        swapped = jnp.concatenate([blocked[:, :, 1:], blocked[:, :, :1]], axis=2)
        chosen = jnp.where(arrival[0] == 0, blocked, swapped)
    else:
        chosen = jnp.take(blocked, arrival, axis=2)
    chosen = chosen.reshape(count, 3, stations).astype(jnp.float32)
    total_rows = stations * 3
    row_block = 96 if total_rows % 96 == 0 else total_rows
    chunks = total_rows // row_block
    if chunks == 1:
        padded = jnp.concatenate([base, jnp.zeros((count, 3, JP - L), base.dtype)], axis=2)
        padded = padded.astype(jnp.bfloat16).reshape(count, 3 * JP)
        flat = jnp.transpose(chosen, (0, 1, 2)).reshape(count, total_rows).astype(jnp.bfloat16)
        start_zero = lax.optimization_barrier(jnp.zeros((), jnp.int32))
        column = lax.iota(jnp.int32, JP * total_rows) + start_zero
        lag = column // total_rows
        row = column % total_rows
        source = lax.iota(jnp.int32, 3 * JP)
        pick_base = (
            (source[:, None] % JP == lag[None, :]) & (source[:, None] // JP == row[None, :] % 3)
        ).astype(jnp.bfloat16)
        slot = lax.iota(jnp.int32, total_rows)
        pick_mask = (
            (slot[:, None] // stations == row[None, :] % 3)
            & (slot[:, None] % stations == row[None, :] // 3)
        ).astype(jnp.bfloat16)
        spread = jnp.dot(padded, pick_base, preferred_element_type=jnp.float32)
        gate = jnp.dot(flat, pick_mask, preferred_element_type=jnp.float32)
        weights = (spread * gate).astype(jnp.bfloat16)
    else:
        full = jnp.transpose(base, (0, 2, 1))[:, :, None, :] * jnp.transpose(chosen, (0, 2, 1))[:, None, :, :]
        full = full.astype(jnp.bfloat16).reshape(count, L, stations * 3)
        full = jnp.concatenate([full, jnp.zeros((count, JP - L, stations * 3), full.dtype)], axis=1)
        weights = (
            full.reshape(count, JP, chunks, row_block)
            .transpose(0, 2, 1, 3)
            .reshape(count, chunks * JP * row_block)
        )
    stacked = correlate(windows, inv, weights, row_block)
    pieces = [lax.dynamic_slice_in_dim(stacked, corr_place * local_count, local_count, 0)]
    for d in range(1, corr_count):
        target = (corr_place + d) % corr_count
        part = lax.dynamic_slice_in_dim(stacked, target * local_count, local_count, 0)
        route = [(i, (i + d) % corr_count) for i in range(corr_count)]
        pieces.append(lax.ppermute(part, "corr", route))
    stacked = jnp.zeros((local_count, corr_count * width), jnp.float32)
    for d, part in enumerate(pieces):
        place = ((corr_place - d) % corr_count) * width
        stacked = lax.dynamic_update_slice_in_dim(stacked, part, place, 1)
    return stacked[None]


def solution(mesh):
    return jax.shard_map(
        body,
        mesh=mesh,
        in_specs=(
            P(("groups", "pair"), "filt", None, "corr"),
            P(("groups", "pair"), "filt"),
            P(),
            P("corr", None),
            P(),
        ),
        out_specs=P(("groups", "pair"), "corr", "filt"),
        check_vma=False,
    )
```

```python
import functools

import jax
import jax.numpy as jnp
from jax import lax
from jax.experimental import pallas as pl
from jax.experimental.pallas import tpu as pltpu
from jax.sharding import PartitionSpec as P

L = 75
TAPS = 64
DEC = 4
JP = 76
TT = 512
RSUB = 16


def from_behind(block, axis, distance):
    devices = range(lax.axis_size(axis))
    route = [(i - distance, i) for i in devices if i - distance in devices]
    return lax.ppermute(block, axis, route)


def window_energy(rows, width):
    p1 = rows * rows
    p2 = p1[:, :-1] + p1[:, 1:]
    p4 = p2[:, :-2] + p2[:, 2:]
    p8 = p4[:, :-4] + p4[:, 4:]
    p16 = p8[:, :-8] + p8[:, 8:]
    p32 = p16[:, :-16] + p16[:, 16:]
    p64 = p32[:, :-32] + p32[:, 32:]
    return (
        p64[:, :width]
        + p8[:, 64 : 64 + width]
        + p2[:, 72 : 72 + width]
        + p1[:, 74 : 74 + width]
    )


def corr_kernel(f_ref, inv_ref, w_ref, o_ref, s_ref, *, row_block, tile):
    q = pl.program_id(1)
    span = tile + 128

    def fill(sub, carry):
        r0 = pl.multiple_of(sub * RSUB, RSUB)
        seg = f_ref[0, pl.ds(r0, RSUB), :].astype(jnp.float32)
        inv = inv_ref[pl.ds(r0, RSUB), :]
        for j in range(JP):
            moved = seg if j == 0 else pltpu.roll(seg, span - j, 1)
            piece = (moved[:, :tile] * inv).astype(jnp.bfloat16)
            s_ref[pl.ds(pl.multiple_of(j * row_block + r0, RSUB), RSUB), :] = piece
        return carry

    lax.fori_loop(0, row_block // RSUB, fill, 0)
    part = jnp.dot(w_ref[...], s_ref[...], preferred_element_type=jnp.float32)

    @pl.when(q == 0)
    def _():
        o_ref[...] = part

    @pl.when(q > 0)
    def _():
        o_ref[...] += part


def correlate(windows, inv, weights, row_block):
    tiles, rows, span = windows.shape
    count = weights.shape[0]
    width = inv.shape[1]
    tile = width // tiles
    chunks = rows // row_block
    return pl.pallas_call(
        functools.partial(corr_kernel, row_block=row_block, tile=tile),
        grid=(tiles, chunks),
        in_specs=[
            pl.BlockSpec((1, row_block, span), lambda i, q: (i, q, 0)),
            pl.BlockSpec((row_block, tile), lambda i, q: (q, i)),
            pl.BlockSpec((count, JP * row_block), lambda i, q: (0, q)),
        ],
        out_specs=pl.BlockSpec((count, tile), lambda i, q: (0, i)),
        out_shape=jax.ShapeDtypeStruct((count, width), jnp.float32),
        scratch_shapes=[pltpu.VMEM((JP * row_block, tile), jnp.bfloat16)],
        compiler_params=pltpu.CompilerParams(
            dimension_semantics=("parallel", "arbitrary"),
            vmem_limit_bytes=48 * 1024 * 1024,
        ),
    )(windows, inv, weights)


def body(raw_rows, valid_counts, taps, templates, masks):
    samples = raw_rows[0]
    counts = valid_counts[0]
    local_stations = samples.shape[0]
    raw_width = samples.shape[2]
    corr_place = lax.axis_index("corr")
    filt_place = lax.axis_index("filt")
    filt_count = lax.axis_size("filt")
    sample_times = corr_place * raw_width + lax.iota(jnp.int32, raw_width)
    keep = sample_times[None, None, :] < counts[:, None, None]
    live = jnp.where(keep, samples, jnp.zeros_like(samples)).reshape(local_stations * 3, raw_width)
    corr_count = lax.axis_size("corr")
    local_count = templates.shape[0]
    template_width = templates.shape[1]
    lanes = -(-template_width // 512) * 512
    wide = jnp.concatenate(
        [templates, jnp.zeros((local_count, lanes - template_width), templates.dtype)], axis=1
    )
    forward = [(i, (i + 1) % corr_count) for i in range(corr_count)]
    backward = [(i, (i - 1) % corr_count) for i in range(corr_count)]
    tail_rows = live.shape[0]
    sent = jnp.concatenate([live[:, raw_width - 128 :], wide.reshape(-1, 128)], axis=0)
    got = lax.ppermute(sent, "corr", forward)
    history = jnp.where(corr_place > 0, got[:tail_rows], jnp.zeros_like(got[:tail_rows]))
    from_previous = got[tail_rows:].reshape(local_count, lanes)
    sent = jnp.concatenate([live[:, :512], wide.reshape(-1, 512)], axis=0)
    got = lax.ppermute(sent, "corr", backward)
    ahead = jnp.where(corr_place < corr_count - 1, got[:tail_rows], jnp.zeros_like(got[:tail_rows]))
    from_next = got[tail_rows:].reshape(local_count, lanes)
    blocks_by_offset = {0: wide, 1: from_previous, corr_count - 1: from_next}
    for d in range(2, corr_count - 1):
        route = [(i, (i + d) % corr_count) for i in range(corr_count)]
        blocks_by_offset[d] = lax.ppermute(wide, "corr", route)
    by_offset = jnp.stack([blocks_by_offset[d] for d in range(corr_count)], axis=0)
    offsets = (corr_place - lax.iota(jnp.int32, corr_count)) % corr_count
    gathered_templates = jnp.take(by_offset, offsets, axis=0).reshape(
        corr_count * local_count, lanes
    )[:, :template_width]
    extended = jnp.concatenate([history, live, ahead], axis=1)
    decimated = raw_width // DEC
    blocks = decimated // 128 + 1
    frames = jnp.stack(
        [extended[:, 512 * a : 512 * a + 640] for a in range(blocks)], axis=1
    ).reshape(local_stations * 3 * blocks, 640)
    flip = (lax.iota(jnp.int32, TAPS)[:, None] + lax.iota(jnp.int32, TAPS)[None, :] == TAPS - 1)
    reversed_taps = jnp.dot(
        taps[None, :], flip.astype(taps.dtype), preferred_element_type=jnp.float32
    )[0].astype(taps.dtype)
    ring = jnp.concatenate(
        [jnp.zeros((65,), taps.dtype), reversed_taps, jnp.zeros((644 - 129,), taps.dtype)]
    )
    bank = jnp.tile(ring, 128)[: 128 * 640].reshape(128, 640)
    filtered = lax.dot_general(
        frames, bank, (((1,), (1,)), ((), ())), preferred_element_type=jnp.float32
    )
    filtered = filtered.astype(jnp.bfloat16).reshape(local_stations * 3, decimated + 128)
    past_end = (corr_place == corr_count - 1) & (lax.iota(jnp.int32, decimated + 128) >= decimated)
    filtered = jnp.where(past_end[None, :], jnp.zeros_like(filtered), filtered)
    per_block = corr_count // filt_count
    block = per_block * decimated
    width = block // corr_count
    span = width + 128
    received = []
    for k in range(filt_count):
        piece = (filt_place + k) % filt_count
        part = lax.dynamic_slice_in_dim(filtered, piece * width, span, 1)
        route = []
        for c in range(corr_count):
            for f in range(filt_count):
                dest = ((c % per_block) * filt_count + (f + k) % filt_count) * filt_count + c // per_block
                route.append((c * filt_count + f, dest))
        received.append(lax.ppermute(part, ("corr", "filt"), route))
    rows = jnp.concatenate(received, axis=0)
    energy = window_energy(rows.astype(jnp.float32), width)
    inv = lax.rsqrt(jnp.maximum(energy, 1.0))
    tile = min(TT, width)
    tiles = width // tile
    windows = jnp.stack([rows[:, i * tile : i * tile + tile + 128] for i in range(tiles)], axis=0)

    templates = gathered_templates
    count = templates.shape[0]
    stations = masks.shape[2]
    shaped = templates.astype(jnp.float32).reshape(count, 3, L)
    norms = jnp.sqrt(jnp.sum(shaped * shaped, axis=2) + 1e-06)
    base = shaped / norms[:, :, None]
    arrival = (corr_place - lax.iota(jnp.int32, filt_count)) % filt_count
    blocked = masks.reshape(count, 3, filt_count, stations // filt_count)
    if filt_count == 2:
        swapped = jnp.concatenate([blocked[:, :, 1:], blocked[:, :, :1]], axis=2)
        chosen = jnp.where(arrival[0] == 0, blocked, swapped)
    else:
        chosen = jnp.take(blocked, arrival, axis=2)
    chosen = chosen.reshape(count, 3, stations).astype(jnp.float32)
    total_rows = stations * 3
    row_block = 96 if total_rows % 96 == 0 else total_rows
    chunks = total_rows // row_block
    if chunks == 1:
        padded = jnp.concatenate([base, jnp.zeros((count, 3, JP - L), base.dtype)], axis=2)
        padded = padded.astype(jnp.bfloat16).reshape(count, 3 * JP)
        flat = jnp.transpose(chosen, (0, 1, 2)).reshape(count, total_rows).astype(jnp.bfloat16)
        start_zero = lax.optimization_barrier(jnp.zeros((), jnp.int32))
        column = lax.iota(jnp.int32, JP * total_rows) + start_zero
        lag = column // total_rows
        row = column % total_rows
        source = lax.iota(jnp.int32, 3 * JP)
        pick_base = (
            (source[:, None] % JP == lag[None, :]) & (source[:, None] // JP == row[None, :] % 3)
        ).astype(jnp.bfloat16)
        slot = lax.iota(jnp.int32, total_rows)
        pick_mask = (
            (slot[:, None] // stations == row[None, :] % 3)
            & (slot[:, None] % stations == row[None, :] // 3)
        ).astype(jnp.bfloat16)
        spread = jnp.dot(padded, pick_base, preferred_element_type=jnp.float32)
        gate = jnp.dot(flat, pick_mask, preferred_element_type=jnp.float32)
        weights = (spread * gate).astype(jnp.bfloat16)
    else:
        full = jnp.transpose(base, (0, 2, 1))[:, :, None, :] * jnp.transpose(chosen, (0, 2, 1))[:, None, :, :]
        full = full.astype(jnp.bfloat16).reshape(count, L, stations * 3)
        full = jnp.concatenate([full, jnp.zeros((count, JP - L, stations * 3), full.dtype)], axis=1)
        weights = (
            full.reshape(count, JP, chunks, row_block)
            .transpose(0, 2, 1, 3)
            .reshape(count, chunks * JP * row_block)
        )
    stacked = correlate(windows, inv, weights, row_block)
    pieces = [lax.dynamic_slice_in_dim(stacked, corr_place * local_count, local_count, 0)]
    for d in range(1, corr_count):
        target = (corr_place + d) % corr_count
        part = lax.dynamic_slice_in_dim(stacked, target * local_count, local_count, 0)
        route = [(i, (i + d) % corr_count) for i in range(corr_count)]
        pieces.append(lax.ppermute(part, "corr", route))
    stacked = jnp.zeros((local_count, corr_count * width), jnp.float32)
    for d, part in enumerate(pieces):
        place = ((corr_place - d) % corr_count) * width
        stacked = lax.dynamic_update_slice_in_dim(stacked, part, place, 1)
    return stacked[None]


def solution(mesh):
    return jax.shard_map(
        body,
        mesh=mesh,
        in_specs=(
            P(("groups", "pair"), "filt", None, "corr"),
            P(("groups", "pair"), "filt"),
            P(),
            P("corr", None),
            P(),
        ),
        out_specs=P(("groups", "pair"), "corr", "filt"),
        check_vma=False,
    )
```

```python
import functools

import jax
import jax.numpy as jnp
from jax import lax
from jax.experimental import pallas as pl
from jax.experimental.pallas import tpu as pltpu
from jax.sharding import PartitionSpec as P

L = 75
TAPS = 64
DEC = 4
JP = 76
TT = 512
RSUB = 16


def from_behind(block, axis, distance):
    devices = range(lax.axis_size(axis))
    route = [(i - distance, i) for i in devices if i - distance in devices]
    return lax.ppermute(block, axis, route)


def window_energy(rows, width):
    p1 = rows * rows
    p2 = p1[:, :-1] + p1[:, 1:]
    p4 = p2[:, :-2] + p2[:, 2:]
    p8 = p4[:, :-4] + p4[:, 4:]
    p16 = p8[:, :-8] + p8[:, 8:]
    p32 = p16[:, :-16] + p16[:, 16:]
    p64 = p32[:, :-32] + p32[:, 32:]
    return (
        p64[:, :width]
        + p8[:, 64 : 64 + width]
        + p2[:, 72 : 72 + width]
        + p1[:, 74 : 74 + width]
    )


def corr_kernel(f_ref, inv_ref, w_ref, o_ref, s_ref, *, row_block, tile):
    q = pl.program_id(1)
    span = tile + 128

    def fill(sub, carry):
        r0 = pl.multiple_of(sub * RSUB, RSUB)
        seg = f_ref[0, pl.ds(r0, RSUB), :].astype(jnp.float32)
        inv = inv_ref[pl.ds(r0, RSUB), :]
        for j in range(JP):
            moved = seg if j == 0 else pltpu.roll(seg, span - j, 1)
            piece = (moved[:, :tile] * inv).astype(jnp.bfloat16)
            s_ref[pl.ds(pl.multiple_of(j * row_block + r0, RSUB), RSUB), :] = piece
        return carry

    lax.fori_loop(0, row_block // RSUB, fill, 0)
    part = jnp.dot(w_ref[...], s_ref[...], preferred_element_type=jnp.float32)

    @pl.when(q == 0)
    def _():
        o_ref[...] = part

    @pl.when(q > 0)
    def _():
        o_ref[...] += part


def correlate(windows, inv, weights, row_block):
    tiles, rows, span = windows.shape
    count = weights.shape[0]
    width = inv.shape[1]
    tile = width // tiles
    chunks = rows // row_block
    return pl.pallas_call(
        functools.partial(corr_kernel, row_block=row_block, tile=tile),
        grid=(tiles, chunks),
        in_specs=[
            pl.BlockSpec((1, row_block, span), lambda i, q: (i, q, 0)),
            pl.BlockSpec((row_block, tile), lambda i, q: (q, i)),
            pl.BlockSpec((count, JP * row_block), lambda i, q: (0, q)),
        ],
        out_specs=pl.BlockSpec((count, tile), lambda i, q: (0, i)),
        out_shape=jax.ShapeDtypeStruct((count, width), jnp.float32),
        scratch_shapes=[pltpu.VMEM((JP * row_block, tile), jnp.bfloat16)],
        compiler_params=pltpu.CompilerParams(
            dimension_semantics=("parallel", "arbitrary"),
            vmem_limit_bytes=48 * 1024 * 1024,
        ),
    )(windows, inv, weights)


def body(raw_rows, valid_counts, taps, templates, masks):
    samples = raw_rows[0]
    counts = valid_counts[0]
    local_stations = samples.shape[0]
    raw_width = samples.shape[2]
    corr_place = lax.axis_index("corr")
    filt_place = lax.axis_index("filt")
    filt_count = lax.axis_size("filt")
    sample_times = corr_place * raw_width + lax.iota(jnp.int32, raw_width)
    keep = sample_times[None, None, :] < counts[:, None, None]
    live = jnp.where(keep, samples, jnp.zeros_like(samples)).reshape(local_stations * 3, raw_width)
    corr_count = lax.axis_size("corr")
    local_count = templates.shape[0]
    template_width = templates.shape[1]
    lanes = -(-template_width // 256) * 256
    wide = jnp.concatenate(
        [templates, jnp.zeros((local_count, lanes - template_width), templates.dtype)], axis=1
    )
    forward = [(i, (i + 1) % corr_count) for i in range(corr_count)]
    backward = [(i, (i - 1) % corr_count) for i in range(corr_count)]
    tail_rows = live.shape[0]
    sent = jnp.concatenate([live[:, raw_width - 128 :], wide.reshape(-1, 128)], axis=0)
    got = lax.ppermute(sent, "corr", forward)
    history = jnp.where(corr_place > 0, got[:tail_rows], jnp.zeros_like(got[:tail_rows]))
    from_previous = got[tail_rows:].reshape(local_count, lanes)
    sent = jnp.concatenate([live[:, :512], wide.reshape(-1, 512)], axis=0)
    got = lax.ppermute(sent, "corr", backward)
    ahead = jnp.where(corr_place < corr_count - 1, got[:tail_rows], jnp.zeros_like(got[:tail_rows]))
    from_next = got[tail_rows:].reshape(local_count, lanes)
    blocks_by_offset = {0: wide, 1: from_previous, corr_count - 1: from_next}
    for d in range(2, corr_count - 1):
        route = [(i, (i + d) % corr_count) for i in range(corr_count)]
        blocks_by_offset[d] = lax.ppermute(wide, "corr", route)
    by_offset = jnp.stack([blocks_by_offset[d] for d in range(corr_count)], axis=0)
    gathered_templates = jnp.concatenate(
        [
            lax.dynamic_index_in_dim(by_offset, (corr_place - b) % corr_count, 0, keepdims=False)
            for b in range(corr_count)
        ],
        axis=0,
    )[:, :template_width]
    extended = jnp.concatenate([history, live, ahead], axis=1)
    decimated = raw_width // DEC
    blocks = decimated // 128 + 1
    frames = jnp.stack(
        [extended[:, 512 * a : 512 * a + 640] for a in range(blocks)], axis=1
    ).reshape(local_stations * 3 * blocks, 640)
    flip = (lax.iota(jnp.int32, TAPS)[:, None] + lax.iota(jnp.int32, TAPS)[None, :] == TAPS - 1)
    reversed_taps = jnp.dot(
        taps[None, :], flip.astype(taps.dtype), preferred_element_type=jnp.float32
    )[0].astype(taps.dtype)
    ring = jnp.concatenate(
        [jnp.zeros((65,), taps.dtype), reversed_taps, jnp.zeros((644 - 129,), taps.dtype)]
    )
    bank = jnp.tile(ring, 128)[: 128 * 640].reshape(128, 640)
    filtered = lax.dot_general(
        frames, bank, (((1,), (1,)), ((), ())), preferred_element_type=jnp.float32
    )
    filtered = filtered.astype(jnp.bfloat16).reshape(local_stations * 3, decimated + 128)
    past_end = (corr_place == corr_count - 1) & (lax.iota(jnp.int32, decimated + 128) >= decimated)
    filtered = jnp.where(past_end[None, :], jnp.zeros_like(filtered), filtered)
    per_block = corr_count // filt_count
    block = per_block * decimated
    width = block // corr_count
    span = width + 128
    received = []
    for k in range(filt_count):
        piece = (filt_place + k) % filt_count
        part = lax.dynamic_slice_in_dim(filtered, piece * width, span, 1)
        route = []
        for c in range(corr_count):
            for f in range(filt_count):
                dest = ((c % per_block) * filt_count + (f + k) % filt_count) * filt_count + c // per_block
                route.append((c * filt_count + f, dest))
        received.append(lax.ppermute(part, ("corr", "filt"), route))
    rows = jnp.concatenate(received, axis=0)
    energy = window_energy(rows.astype(jnp.float32), width)
    inv = lax.rsqrt(jnp.maximum(energy, 1.0))
    tile = min(TT, width)
    tiles = width // tile
    windows = jnp.stack([rows[:, i * tile : i * tile + tile + 128] for i in range(tiles)], axis=0)

    templates = gathered_templates
    count = templates.shape[0]
    stations = masks.shape[2]
    shaped = templates.astype(jnp.float32).reshape(count, 3, L)
    norms = jnp.sqrt(jnp.sum(shaped * shaped, axis=2) + 1e-06)
    base = shaped / norms[:, :, None]
    arrival = (corr_place - lax.iota(jnp.int32, filt_count)) % filt_count
    blocked = masks.reshape(count, 3, filt_count, stations // filt_count)
    if filt_count == 2:
        swapped = jnp.concatenate([blocked[:, :, 1:], blocked[:, :, :1]], axis=2)
        chosen = jnp.where(arrival[0] == 0, blocked, swapped)
    else:
        chosen = jnp.take(blocked, arrival, axis=2)
    chosen = chosen.reshape(count, 3, stations).astype(jnp.float32)
    total_rows = stations * 3
    row_block = 96 if total_rows % 96 == 0 else total_rows
    chunks = total_rows // row_block
    if chunks == 1:
        padded = jnp.concatenate([base, jnp.zeros((count, 3, JP - L), base.dtype)], axis=2)
        padded = padded.astype(jnp.bfloat16).reshape(count, 3 * JP)
        flat = jnp.transpose(chosen, (0, 1, 2)).reshape(count, total_rows).astype(jnp.bfloat16)
        start_zero = lax.optimization_barrier(jnp.zeros((), jnp.int32))
        column = lax.iota(jnp.int32, JP * total_rows) + start_zero
        lag = column // total_rows
        row = column % total_rows
        source = lax.iota(jnp.int32, 3 * JP)
        pick_base = (
            (source[:, None] % JP == lag[None, :]) & (source[:, None] // JP == row[None, :] % 3)
        ).astype(jnp.bfloat16)
        slot = lax.iota(jnp.int32, total_rows)
        pick_mask = (
            (slot[:, None] // stations == row[None, :] % 3)
            & (slot[:, None] % stations == row[None, :] // 3)
        ).astype(jnp.bfloat16)
        spread = jnp.dot(padded, pick_base, preferred_element_type=jnp.float32)
        gate = jnp.dot(flat, pick_mask, preferred_element_type=jnp.float32)
        weights = (spread * gate).astype(jnp.bfloat16)
    else:
        full = jnp.transpose(base, (0, 2, 1))[:, :, None, :] * jnp.transpose(chosen, (0, 2, 1))[:, None, :, :]
        full = full.astype(jnp.bfloat16).reshape(count, L, stations * 3)
        full = jnp.concatenate([full, jnp.zeros((count, JP - L, stations * 3), full.dtype)], axis=1)
        weights = (
            full.reshape(count, JP, chunks, row_block)
            .transpose(0, 2, 1, 3)
            .reshape(count, chunks * JP * row_block)
        )
    stacked = correlate(windows, inv, weights, row_block)
    pieces = [lax.dynamic_slice_in_dim(stacked, corr_place * local_count, local_count, 0)]
    for d in range(1, corr_count):
        target = (corr_place + d) % corr_count
        part = lax.dynamic_slice_in_dim(stacked, target * local_count, local_count, 0)
        route = [(i, (i + d) % corr_count) for i in range(corr_count)]
        pieces.append(lax.ppermute(part, "corr", route))
    stacked = jnp.zeros((local_count, corr_count * width), jnp.float32)
    for d, part in enumerate(pieces):
        place = ((corr_place - d) % corr_count) * width
        stacked = lax.dynamic_update_slice_in_dim(stacked, part, place, 1)
    return stacked[None]


def solution(mesh):
    return jax.shard_map(
        body,
        mesh=mesh,
        in_specs=(
            P(("groups", "pair"), "filt", None, "corr"),
            P(("groups", "pair"), "filt"),
            P(),
            P("corr", None),
            P(),
        ),
        out_specs=P(("groups", "pair"), "corr", "filt"),
        check_vma=False,
    )
```

```python
import functools

import jax
import jax.numpy as jnp
from jax import lax
from jax.experimental import pallas as pl
from jax.experimental.pallas import tpu as pltpu
from jax.sharding import PartitionSpec as P

L = 75
TAPS = 64
DEC = 4
JP = 76
TT = 512
RSUB = 16


def from_behind(block, axis, distance):
    devices = range(lax.axis_size(axis))
    route = [(i - distance, i) for i in devices if i - distance in devices]
    return lax.ppermute(block, axis, route)


def window_energy(rows, width):
    p1 = rows * rows
    p2 = p1[:, :-1] + p1[:, 1:]
    p4 = p2[:, :-2] + p2[:, 2:]
    p8 = p4[:, :-4] + p4[:, 4:]
    p16 = p8[:, :-8] + p8[:, 8:]
    p32 = p16[:, :-16] + p16[:, 16:]
    p64 = p32[:, :-32] + p32[:, 32:]
    return (
        p64[:, :width]
        + p8[:, 64 : 64 + width]
        + p2[:, 72 : 72 + width]
        + p1[:, 74 : 74 + width]
    )


def corr_kernel(f_ref, inv_ref, w_ref, o_ref, s_ref, *, row_block, tile):
    q = pl.program_id(1)
    span = tile + 128

    def fill(sub, carry):
        r0 = pl.multiple_of(sub * RSUB, RSUB)
        seg = f_ref[0, pl.ds(r0, RSUB), :].astype(jnp.float32)
        inv = inv_ref[pl.ds(r0, RSUB), :]
        for j in range(JP):
            moved = seg if j == 0 else pltpu.roll(seg, span - j, 1)
            piece = (moved[:, :tile] * inv).astype(jnp.bfloat16)
            s_ref[pl.ds(pl.multiple_of(j * row_block + r0, RSUB), RSUB), :] = piece
        return carry

    lax.fori_loop(0, row_block // RSUB, fill, 0)
    part = jnp.dot(w_ref[...], s_ref[...], preferred_element_type=jnp.float32)

    @pl.when(q == 0)
    def _():
        o_ref[...] = part

    @pl.when(q > 0)
    def _():
        o_ref[...] += part


def correlate(windows, inv, weights, row_block):
    tiles, rows, span = windows.shape
    count = weights.shape[0]
    width = inv.shape[1]
    tile = width // tiles
    chunks = rows // row_block
    return pl.pallas_call(
        functools.partial(corr_kernel, row_block=row_block, tile=tile),
        grid=(tiles, chunks),
        in_specs=[
            pl.BlockSpec((1, row_block, span), lambda i, q: (i, q, 0)),
            pl.BlockSpec((row_block, tile), lambda i, q: (q, i)),
            pl.BlockSpec((count, JP * row_block), lambda i, q: (0, q)),
        ],
        out_specs=pl.BlockSpec((count, tile), lambda i, q: (0, i)),
        out_shape=jax.ShapeDtypeStruct((count, width), jnp.float32),
        scratch_shapes=[pltpu.VMEM((JP * row_block, tile), jnp.bfloat16)],
        compiler_params=pltpu.CompilerParams(
            dimension_semantics=("parallel", "arbitrary"),
            vmem_limit_bytes=48 * 1024 * 1024,
        ),
    )(windows, inv, weights)


def body(raw_rows, valid_counts, taps, templates, masks):
    samples = raw_rows[0]
    counts = valid_counts[0]
    local_stations = samples.shape[0]
    raw_width = samples.shape[2]
    corr_place = lax.axis_index("corr")
    filt_place = lax.axis_index("filt")
    filt_count = lax.axis_size("filt")
    sample_times = corr_place * raw_width + lax.iota(jnp.int32, raw_width)
    keep = sample_times[None, None, :] < counts[:, None, None]
    live = jnp.where(keep, samples, jnp.zeros_like(samples)).reshape(local_stations * 3, raw_width)
    corr_count = lax.axis_size("corr")
    local_count = templates.shape[0]
    template_width = templates.shape[1]
    lanes = -(-template_width // 256) * 256
    wide = jnp.concatenate(
        [templates, jnp.zeros((local_count, lanes - template_width), templates.dtype)], axis=1
    )
    forward = [(i, (i + 1) % corr_count) for i in range(corr_count)]
    backward = [(i, (i - 1) % corr_count) for i in range(corr_count)]
    tail_rows = live.shape[0]
    sent = jnp.concatenate([live[:, raw_width - 128 :], wide.reshape(-1, 128)], axis=0)
    got = lax.ppermute(sent, "corr", forward)
    history = jnp.where(corr_place > 0, got[:tail_rows], jnp.zeros_like(got[:tail_rows]))
    from_previous = got[tail_rows:].reshape(local_count, lanes)
    sent = jnp.concatenate([live[:, :512], wide.reshape(-1, 512)], axis=0)
    got = lax.ppermute(sent, "corr", backward)
    ahead = jnp.where(corr_place < corr_count - 1, got[:tail_rows], jnp.zeros_like(got[:tail_rows]))
    from_next = got[tail_rows:].reshape(local_count, lanes)
    blocks_by_offset = {0: wide, 1: from_previous, corr_count - 1: from_next}
    for d in range(2, corr_count - 1):
        route = [(i, (i + d) % corr_count) for i in range(corr_count)]
        blocks_by_offset[d] = lax.ppermute(wide, "corr", route)
    by_offset = jnp.stack([blocks_by_offset[d] for d in range(corr_count)], axis=0)
    gathered_templates = jnp.concatenate(
        [
            lax.dynamic_index_in_dim(by_offset, (corr_place - b) % corr_count, 0, keepdims=False)
            for b in range(corr_count)
        ],
        axis=0,
    )[:, :template_width]
    extended = jnp.concatenate([history, live, ahead], axis=1)
    decimated = raw_width // DEC
    blocks = decimated // 128 + 1
    frames = jnp.stack(
        [extended[:, 512 * a : 512 * a + 640] for a in range(blocks)], axis=1
    ).reshape(local_stations * 3 * blocks, 640)
    flip = (lax.iota(jnp.int32, TAPS)[:, None] + lax.iota(jnp.int32, TAPS)[None, :] == TAPS - 1)
    reversed_taps = jnp.dot(
        taps[None, :], flip.astype(taps.dtype), preferred_element_type=jnp.float32
    )[0].astype(taps.dtype)
    ring = jnp.concatenate(
        [jnp.zeros((65,), taps.dtype), reversed_taps, jnp.zeros((644 - 129,), taps.dtype)]
    )
    bank = jnp.tile(ring, 128)[: 128 * 640].reshape(128, 640)
    filtered = lax.dot_general(
        frames, bank, (((1,), (1,)), ((), ())), preferred_element_type=jnp.float32
    )
    filtered = filtered.astype(jnp.bfloat16).reshape(local_stations * 3, decimated + 128)
    past_end = (corr_place == corr_count - 1) & (lax.iota(jnp.int32, decimated + 128) >= decimated)
    filtered = jnp.where(past_end[None, :], jnp.zeros_like(filtered), filtered)
    per_block = corr_count // filt_count
    block = per_block * decimated
    width = block // corr_count
    span = width + 128
    received = []
    for k in range(filt_count):
        piece = (filt_place + k) % filt_count
        part = lax.dynamic_slice_in_dim(filtered, piece * width, span, 1)
        route = []
        for c in range(corr_count):
            for f in range(filt_count):
                dest = ((c % per_block) * filt_count + (f + k) % filt_count) * filt_count + c // per_block
                route.append((c * filt_count + f, dest))
        received.append(lax.ppermute(part, ("corr", "filt"), route))
    rows = jnp.concatenate(received, axis=0)
    energy = window_energy(rows.astype(jnp.float32), width)
    inv = lax.rsqrt(jnp.maximum(energy, 1.0))
    tile = min(TT, width)
    tiles = width // tile
    windows = jnp.stack([rows[:, i * tile : i * tile + tile + 128] for i in range(tiles)], axis=0)

    templates = gathered_templates
    count = templates.shape[0]
    stations = masks.shape[2]
    shaped = templates.astype(jnp.float32).reshape(count, 3, L)
    norms = jnp.sqrt(jnp.sum(shaped * shaped, axis=2) + 1e-06)
    base = shaped / norms[:, :, None]
    arrival = (corr_place - lax.iota(jnp.int32, filt_count)) % filt_count
    blocked = masks.reshape(count, 3, filt_count, stations // filt_count)
    if filt_count == 2:
        swapped = jnp.concatenate([blocked[:, :, 1:], blocked[:, :, :1]], axis=2)
        chosen = jnp.where(arrival[0] == 0, blocked, swapped)
    else:
        chosen = jnp.take(blocked, arrival, axis=2)
    chosen = chosen.reshape(count, 3, stations).astype(jnp.float32)
    total_rows = stations * 3
    row_block = 96 if total_rows % 96 == 0 else total_rows
    chunks = total_rows // row_block
    if chunks == 1:
        padded = jnp.concatenate([base, jnp.zeros((count, 3, JP - L), base.dtype)], axis=2)
        padded = padded.astype(jnp.bfloat16).reshape(count, 3 * JP)
        flat = jnp.transpose(chosen, (0, 1, 2)).reshape(count, total_rows).astype(jnp.bfloat16)
        start_zero = lax.optimization_barrier(jnp.zeros((), jnp.int32))
        column = lax.iota(jnp.int32, JP * total_rows) + start_zero
        lag = column // total_rows
        row = column % total_rows
        source = lax.iota(jnp.int32, 3 * JP)
        pick_base = (
            (source[:, None] % JP == lag[None, :]) & (source[:, None] // JP == row[None, :] % 3)
        ).astype(jnp.bfloat16)
        slot = lax.iota(jnp.int32, total_rows)
        pick_mask = (
            (slot[:, None] // stations == row[None, :] % 3)
            & (slot[:, None] % stations == row[None, :] // 3)
        ).astype(jnp.bfloat16)
        spread = jnp.dot(padded, pick_base, preferred_element_type=jnp.float32)
        gate = jnp.dot(flat, pick_mask, preferred_element_type=jnp.float32)
        weights = (spread * gate).astype(jnp.bfloat16)
    else:
        full = jnp.transpose(base, (0, 2, 1))[:, :, None, :] * jnp.transpose(chosen, (0, 2, 1))[:, None, :, :]
        full = full.astype(jnp.bfloat16).reshape(count, L, stations * 3)
        full = jnp.concatenate([full, jnp.zeros((count, JP - L, stations * 3), full.dtype)], axis=1)
        weights = (
            full.reshape(count, JP, chunks, row_block)
            .transpose(0, 2, 1, 3)
            .reshape(count, chunks * JP * row_block)
        )
    stacked = correlate(windows, inv, weights, row_block)
    mine = lax.dynamic_slice_in_dim(stacked, corr_place * local_count, local_count, 0)
    result = jnp.zeros((local_count, corr_count * width), jnp.float32)
    result = lax.dynamic_update_slice_in_dim(result, mine, corr_place * width, 1)
    for d in range(1, corr_count):
        partner = corr_place ^ d
        part = lax.dynamic_slice_in_dim(stacked, partner * local_count, local_count, 0)
        route = [(i, i ^ d) for i in range(corr_count)]
        part = lax.ppermute(part, "corr", route)
        result = lax.dynamic_update_slice_in_dim(result, part, partner * width, 1)
    stacked = result
    return stacked[None]


def solution(mesh):
    return jax.shard_map(
        body,
        mesh=mesh,
        in_specs=(
            P(("groups", "pair"), "filt", None, "corr"),
            P(("groups", "pair"), "filt"),
            P(),
            P("corr", None),
            P(),
        ),
        out_specs=P(("groups", "pair"), "corr", "filt"),
        check_vma=False,
    )
```

```python
import functools

import jax
import jax.numpy as jnp
from jax import lax
from jax.experimental import pallas as pl
from jax.experimental.pallas import tpu as pltpu
from jax.sharding import PartitionSpec as P

L = 75
TAPS = 64
DEC = 4
JP = 76
JPI = 80
TT = 512
RSUB = 16


def from_behind(block, axis, distance):
    devices = range(lax.axis_size(axis))
    route = [(i - distance, i) for i in devices if i - distance in devices]
    return lax.ppermute(block, axis, route)


def window_energy(rows, width):
    p1 = rows * rows
    p2 = p1[:, :-1] + p1[:, 1:]
    p4 = p2[:, :-2] + p2[:, 2:]
    p8 = p4[:, :-4] + p4[:, 4:]
    p16 = p8[:, :-8] + p8[:, 8:]
    p32 = p16[:, :-16] + p16[:, 16:]
    p64 = p32[:, :-32] + p32[:, 32:]
    return (
        p64[:, :width]
        + p8[:, 64 : 64 + width]
        + p2[:, 72 : 72 + width]
        + p1[:, 74 : 74 + width]
    )


def corr_kernel(f_ref, inv_ref, w_ref, o_ref, s_ref, *, row_block, tile):
    q = pl.program_id(1)
    span = tile + 128

    def fill(sub, carry):
        r0 = pl.multiple_of(sub * RSUB, RSUB)
        seg = f_ref[0, pl.ds(r0, RSUB), :].astype(jnp.float32)
        inv = inv_ref[pl.ds(r0, RSUB), :]
        for j in range(JP):
            moved = seg if j == 0 else pltpu.roll(seg, span - j, 1)
            piece = (moved[:, :tile] * inv).astype(jnp.bfloat16)
            s_ref[pl.ds(pl.multiple_of(j * row_block + r0, RSUB), RSUB), :] = piece
        return carry

    lax.fori_loop(0, row_block // RSUB, fill, 0)
    part = jnp.dot(w_ref[...], s_ref[...], preferred_element_type=jnp.float32)

    @pl.when(q == 0)
    def _():
        o_ref[...] = part

    @pl.when(q > 0)
    def _():
        o_ref[...] += part


def corr_kernel_interleaved(f_ref, inv_ref, w_ref, o_ref, s_ref, *, row_block, tile):
    span = tile + 128
    depth = JPI * RSUB
    part = None
    for sub in range(row_block // RSUB):
        r0 = sub * RSUB
        seg = f_ref[0, r0 : r0 + RSUB, :].astype(jnp.float32)
        inv = inv_ref[r0 : r0 + RSUB, :]
        for j in range(JPI):
            moved = seg if j == 0 else pltpu.roll(seg, span - j, 1)
            piece = (moved[:, :tile] * inv).astype(jnp.bfloat16)
            s_ref[sub * depth + j * RSUB : sub * depth + (j + 1) * RSUB, :] = piece
        step = jnp.dot(
            w_ref[:, sub * depth : (sub + 1) * depth],
            s_ref[sub * depth : (sub + 1) * depth, :],
            preferred_element_type=jnp.float32,
        )
        part = step if part is None else part + step
    o_ref[...] = part


def correlate(windows, inv, weights, row_block, interleaved=False):
    tiles, rows, span = windows.shape
    count = weights.shape[0]
    width = inv.shape[1]
    tile = width // tiles
    chunks = rows // row_block
    lags = JPI if interleaved else JP
    body_fn = corr_kernel_interleaved if interleaved else corr_kernel
    return pl.pallas_call(
        functools.partial(body_fn, row_block=row_block, tile=tile),
        grid=(tiles, chunks),
        in_specs=[
            pl.BlockSpec((1, row_block, span), lambda i, q: (i, q, 0)),
            pl.BlockSpec((row_block, tile), lambda i, q: (q, i)),
            pl.BlockSpec((count, lags * row_block), lambda i, q: (0, q)),
        ],
        out_specs=pl.BlockSpec((count, tile), lambda i, q: (0, i)),
        out_shape=jax.ShapeDtypeStruct((count, width), jnp.float32),
        scratch_shapes=[pltpu.VMEM((lags * row_block, tile), jnp.bfloat16)],
        compiler_params=pltpu.CompilerParams(
            dimension_semantics=("parallel", "arbitrary"),
            vmem_limit_bytes=48 * 1024 * 1024,
        ),
    )(windows, inv, weights)


def body(raw_rows, valid_counts, taps, templates, masks):
    samples = raw_rows[0]
    counts = valid_counts[0]
    local_stations = samples.shape[0]
    raw_width = samples.shape[2]
    corr_place = lax.axis_index("corr")
    filt_place = lax.axis_index("filt")
    filt_count = lax.axis_size("filt")
    sample_times = corr_place * raw_width + lax.iota(jnp.int32, raw_width)
    keep = sample_times[None, None, :] < counts[:, None, None]
    live = jnp.where(keep, samples, jnp.zeros_like(samples)).reshape(local_stations * 3, raw_width)
    corr_count = lax.axis_size("corr")
    local_count = templates.shape[0]
    template_width = templates.shape[1]
    lanes = -(-template_width // 256) * 256
    wide = jnp.concatenate(
        [templates, jnp.zeros((local_count, lanes - template_width), templates.dtype)], axis=1
    )
    forward = [(i, (i + 1) % corr_count) for i in range(corr_count)]
    backward = [(i, (i - 1) % corr_count) for i in range(corr_count)]
    tail_rows = live.shape[0]
    sent = jnp.concatenate([live[:, raw_width - 128 :], wide.reshape(-1, 128)], axis=0)
    got = lax.ppermute(sent, "corr", forward)
    history = jnp.where(corr_place > 0, got[:tail_rows], jnp.zeros_like(got[:tail_rows]))
    from_previous = got[tail_rows:].reshape(local_count, lanes)
    sent = jnp.concatenate([live[:, :512], wide.reshape(-1, 512)], axis=0)
    got = lax.ppermute(sent, "corr", backward)
    ahead = jnp.where(corr_place < corr_count - 1, got[:tail_rows], jnp.zeros_like(got[:tail_rows]))
    from_next = got[tail_rows:].reshape(local_count, lanes)
    blocks_by_offset = {0: wide, 1: from_previous, corr_count - 1: from_next}
    for d in range(2, corr_count - 1):
        route = [(i, (i + d) % corr_count) for i in range(corr_count)]
        blocks_by_offset[d] = lax.ppermute(wide, "corr", route)
    by_offset = jnp.stack([blocks_by_offset[d] for d in range(corr_count)], axis=0)
    gathered_templates = jnp.concatenate(
        [
            lax.dynamic_index_in_dim(by_offset, (corr_place - b) % corr_count, 0, keepdims=False)
            for b in range(corr_count)
        ],
        axis=0,
    )[:, :template_width]
    extended = jnp.concatenate([history, live, ahead], axis=1)
    decimated = raw_width // DEC
    blocks = decimated // 128 + 1
    frames = jnp.stack(
        [extended[:, 512 * a : 512 * a + 640] for a in range(blocks)], axis=1
    ).reshape(local_stations * 3 * blocks, 640)
    flip = (lax.iota(jnp.int32, TAPS)[:, None] + lax.iota(jnp.int32, TAPS)[None, :] == TAPS - 1)
    reversed_taps = jnp.dot(
        taps[None, :], flip.astype(taps.dtype), preferred_element_type=jnp.float32
    )[0].astype(taps.dtype)
    ring = jnp.concatenate(
        [jnp.zeros((65,), taps.dtype), reversed_taps, jnp.zeros((644 - 129,), taps.dtype)]
    )
    bank = jnp.tile(ring, 128)[: 128 * 640].reshape(128, 640)
    filtered = lax.dot_general(
        frames, bank, (((1,), (1,)), ((), ())), preferred_element_type=jnp.float32
    )
    filtered = filtered.astype(jnp.bfloat16).reshape(local_stations * 3, decimated + 128)
    past_end = (corr_place == corr_count - 1) & (lax.iota(jnp.int32, decimated + 128) >= decimated)
    filtered = jnp.where(past_end[None, :], jnp.zeros_like(filtered), filtered)
    per_block = corr_count // filt_count
    block = per_block * decimated
    width = block // corr_count
    span = width + 128
    received = []
    for k in range(filt_count):
        piece = (filt_place + k) % filt_count
        part = lax.dynamic_slice_in_dim(filtered, piece * width, span, 1)
        route = []
        for c in range(corr_count):
            for f in range(filt_count):
                dest = ((c % per_block) * filt_count + (f + k) % filt_count) * filt_count + c // per_block
                route.append((c * filt_count + f, dest))
        received.append(lax.ppermute(part, ("corr", "filt"), route))
    rows = jnp.concatenate(received, axis=0)
    energy = window_energy(rows.astype(jnp.float32), width)
    inv = lax.rsqrt(jnp.maximum(energy, 1.0))
    tile = min(TT, width)
    tiles = width // tile
    windows = jnp.stack([rows[:, i * tile : i * tile + tile + 128] for i in range(tiles)], axis=0)

    templates = gathered_templates
    count = templates.shape[0]
    stations = masks.shape[2]
    shaped = templates.astype(jnp.float32).reshape(count, 3, L)
    norms = jnp.sqrt(jnp.sum(shaped * shaped, axis=2) + 1e-06)
    base = shaped / norms[:, :, None]
    arrival = (corr_place - lax.iota(jnp.int32, filt_count)) % filt_count
    blocked = masks.reshape(count, 3, filt_count, stations // filt_count)
    if filt_count == 2:
        swapped = jnp.concatenate([blocked[:, :, 1:], blocked[:, :, :1]], axis=2)
        chosen = jnp.where(arrival[0] == 0, blocked, swapped)
    else:
        chosen = jnp.take(blocked, arrival, axis=2)
    chosen = chosen.reshape(count, 3, stations).astype(jnp.float32)
    total_rows = stations * 3
    row_block = 96 if total_rows % 96 == 0 else total_rows
    chunks = total_rows // row_block
    if chunks == 1:
        padded = jnp.concatenate([base, jnp.zeros((count, 3, JPI - L), base.dtype)], axis=2)
        padded = padded.astype(jnp.bfloat16).reshape(count, 3 * JPI)
        flat = jnp.transpose(chosen, (0, 1, 2)).reshape(count, total_rows).astype(jnp.bfloat16)
        start_zero = lax.optimization_barrier(jnp.zeros((), jnp.int32))
        column = lax.iota(jnp.int32, JPI * total_rows) + start_zero
        group = column // (JPI * RSUB)
        lag = (column % (JPI * RSUB)) // RSUB
        row = group * RSUB + column % RSUB
        source = lax.iota(jnp.int32, 3 * JPI)
        pick_base = (
            (source[:, None] % JPI == lag[None, :]) & (source[:, None] // JPI == row[None, :] % 3)
        ).astype(jnp.bfloat16)
        slot = lax.iota(jnp.int32, total_rows)
        pick_mask = (
            (slot[:, None] // stations == row[None, :] % 3)
            & (slot[:, None] % stations == row[None, :] // 3)
        ).astype(jnp.bfloat16)
        spread = jnp.dot(padded, pick_base, preferred_element_type=jnp.float32)
        gate = jnp.dot(flat, pick_mask, preferred_element_type=jnp.float32)
        weights = (spread * gate).astype(jnp.bfloat16)
    else:
        full = jnp.transpose(base, (0, 2, 1))[:, :, None, :] * jnp.transpose(chosen, (0, 2, 1))[:, None, :, :]
        full = full.astype(jnp.bfloat16).reshape(count, L, stations * 3)
        full = jnp.concatenate([full, jnp.zeros((count, JP - L, stations * 3), full.dtype)], axis=1)
        weights = (
            full.reshape(count, JP, chunks, row_block)
            .transpose(0, 2, 1, 3)
            .reshape(count, chunks * JP * row_block)
        )
    stacked = correlate(windows, inv, weights, row_block, interleaved=chunks == 1)
    pieces = [lax.dynamic_slice_in_dim(stacked, corr_place * local_count, local_count, 0)]
    for d in range(1, corr_count):
        target = (corr_place + d) % corr_count
        part = lax.dynamic_slice_in_dim(stacked, target * local_count, local_count, 0)
        route = [(i, (i + d) % corr_count) for i in range(corr_count)]
        pieces.append(lax.ppermute(part, "corr", route))
    stacked = jnp.zeros((local_count, corr_count * width), jnp.float32)
    for d, part in enumerate(pieces):
        place = ((corr_place - d) % corr_count) * width
        stacked = lax.dynamic_update_slice_in_dim(stacked, part, place, 1)
    return stacked[None]


def solution(mesh):
    return jax.shard_map(
        body,
        mesh=mesh,
        in_specs=(
            P(("groups", "pair"), "filt", None, "corr"),
            P(("groups", "pair"), "filt"),
            P(),
            P("corr", None),
            P(),
        ),
        out_specs=P(("groups", "pair"), "corr", "filt"),
        check_vma=False,
    )
```

```python
import functools

import jax
import jax.numpy as jnp
from jax import lax
from jax.experimental import pallas as pl
from jax.experimental.pallas import tpu as pltpu
from jax.sharding import PartitionSpec as P

L = 75
TAPS = 64
DEC = 4
JP = 76
JPI = 80
TT = 512
RSUB = 16


def from_behind(block, axis, distance):
    devices = range(lax.axis_size(axis))
    route = [(i - distance, i) for i in devices if i - distance in devices]
    return lax.ppermute(block, axis, route)


def window_energy(rows, width):
    p1 = rows * rows
    p2 = p1[:, :-1] + p1[:, 1:]
    p4 = p2[:, :-2] + p2[:, 2:]
    p8 = p4[:, :-4] + p4[:, 4:]
    p16 = p8[:, :-8] + p8[:, 8:]
    p32 = p16[:, :-16] + p16[:, 16:]
    p64 = p32[:, :-32] + p32[:, 32:]
    return (
        p64[:, :width]
        + p8[:, 64 : 64 + width]
        + p2[:, 72 : 72 + width]
        + p1[:, 74 : 74 + width]
    )


def corr_kernel(f_ref, inv_ref, w_ref, o_ref, s_ref, *, row_block, tile):
    q = pl.program_id(1)
    span = tile + 128

    def fill(sub, carry):
        r0 = pl.multiple_of(sub * RSUB, RSUB)
        seg = f_ref[0, pl.ds(r0, RSUB), :].astype(jnp.float32)
        inv = inv_ref[pl.ds(r0, RSUB), :]
        for j in range(JP):
            moved = seg if j == 0 else pltpu.roll(seg, span - j, 1)
            piece = (moved[:, :tile] * inv).astype(jnp.bfloat16)
            s_ref[pl.ds(pl.multiple_of(j * row_block + r0, RSUB), RSUB), :] = piece
        return carry

    lax.fori_loop(0, row_block // RSUB, fill, 0)
    part = jnp.dot(w_ref[...], s_ref[...], preferred_element_type=jnp.float32)

    @pl.when(q == 0)
    def _():
        o_ref[...] = part

    @pl.when(q > 0)
    def _():
        o_ref[...] += part


def corr_kernel_interleaved(f_ref, inv_ref, w_ref, o_ref, s_ref, *, row_block, tile):
    span = tile + 128
    depth = JPI * RSUB
    part = None
    for sub in range(row_block // RSUB):
        r0 = sub * RSUB
        seg = f_ref[0, r0 : r0 + RSUB, :].astype(jnp.float32)
        inv = inv_ref[r0 : r0 + RSUB, :]
        for j in range(JPI):
            moved = seg if j == 0 else pltpu.roll(seg, span - j, 1)
            piece = (moved[:, :tile] * inv).astype(jnp.bfloat16)
            s_ref[sub * depth + j * RSUB : sub * depth + (j + 1) * RSUB, :] = piece
        step = jnp.dot(
            w_ref[:, sub * depth : (sub + 1) * depth],
            s_ref[sub * depth : (sub + 1) * depth, :],
            preferred_element_type=jnp.float32,
        )
        part = step if part is None else part + step
    o_ref[...] = part


def correlate(windows, inv, weights, row_block, interleaved=False):
    tiles, rows, span = windows.shape
    count = weights.shape[0]
    width = inv.shape[1]
    tile = width // tiles
    chunks = rows // row_block
    lags = JPI if interleaved else JP
    body_fn = corr_kernel_interleaved if interleaved else corr_kernel
    return pl.pallas_call(
        functools.partial(body_fn, row_block=row_block, tile=tile),
        grid=(tiles, chunks),
        in_specs=[
            pl.BlockSpec((1, row_block, span), lambda i, q: (i, q, 0)),
            pl.BlockSpec((row_block, tile), lambda i, q: (q, i)),
            pl.BlockSpec((count, lags * row_block), lambda i, q: (0, q)),
        ],
        out_specs=pl.BlockSpec((count, tile), lambda i, q: (0, i)),
        out_shape=jax.ShapeDtypeStruct((count, width), jnp.float32),
        scratch_shapes=[pltpu.VMEM((lags * row_block, tile), jnp.bfloat16)],
        compiler_params=pltpu.CompilerParams(
            dimension_semantics=("parallel", "arbitrary"),
            vmem_limit_bytes=48 * 1024 * 1024,
        ),
    )(windows, inv, weights)


def body(raw_rows, valid_counts, taps, templates, masks):
    samples = raw_rows[0]
    counts = valid_counts[0]
    local_stations = samples.shape[0]
    raw_width = samples.shape[2]
    corr_place = lax.axis_index("corr")
    filt_place = lax.axis_index("filt")
    filt_count = lax.axis_size("filt")
    sample_times = corr_place * raw_width + lax.iota(jnp.int32, raw_width)
    keep = sample_times[None, None, :] < counts[:, None, None]
    live = jnp.where(keep, samples, jnp.zeros_like(samples)).reshape(local_stations * 3, raw_width)
    corr_count = lax.axis_size("corr")
    local_count = templates.shape[0]
    template_width = templates.shape[1]
    lanes = -(-template_width // 256) * 256
    wide = jnp.concatenate(
        [templates, jnp.zeros((local_count, lanes - template_width), templates.dtype)], axis=1
    )
    forward = [(i, (i + 1) % corr_count) for i in range(corr_count)]
    backward = [(i, (i - 1) % corr_count) for i in range(corr_count)]
    tail_rows = live.shape[0]
    sent = jnp.concatenate([live[:, raw_width - 128 :], wide.reshape(-1, 128)], axis=0)
    got = lax.ppermute(sent, "corr", forward)
    history = jnp.where(corr_place > 0, got[:tail_rows], jnp.zeros_like(got[:tail_rows]))
    from_previous = got[tail_rows:].reshape(local_count, lanes)
    sent = jnp.concatenate([live[:, :512], wide.reshape(-1, 512)], axis=0)
    got = lax.ppermute(sent, "corr", backward)
    ahead = jnp.where(corr_place < corr_count - 1, got[:tail_rows], jnp.zeros_like(got[:tail_rows]))
    from_next = got[tail_rows:].reshape(local_count, lanes)
    blocks_by_offset = {0: wide, 1: from_previous, corr_count - 1: from_next}
    for d in range(2, corr_count - 1):
        route = [(i, (i + d) % corr_count) for i in range(corr_count)]
        blocks_by_offset[d] = lax.ppermute(wide, "corr", route)
    by_offset = jnp.stack([blocks_by_offset[d] for d in range(corr_count)], axis=0)
    gathered_templates = jnp.concatenate(
        [
            lax.dynamic_index_in_dim(by_offset, (corr_place - b) % corr_count, 0, keepdims=False)
            for b in range(corr_count)
        ],
        axis=0,
    )[:, :template_width]
    extended = jnp.concatenate([history, live, ahead], axis=1)
    decimated = raw_width // DEC
    blocks = decimated // 128 + 1
    frames = jnp.stack(
        [extended[:, 512 * a : 512 * a + 640] for a in range(blocks)], axis=1
    ).reshape(local_stations * 3 * blocks, 640)
    flip = (lax.iota(jnp.int32, TAPS)[:, None] + lax.iota(jnp.int32, TAPS)[None, :] == TAPS - 1)
    reversed_taps = jnp.dot(
        taps[None, :], flip.astype(taps.dtype), preferred_element_type=jnp.float32
    )[0].astype(taps.dtype)
    ring = jnp.concatenate(
        [jnp.zeros((65,), taps.dtype), reversed_taps, jnp.zeros((644 - 129,), taps.dtype)]
    )
    bank = jnp.tile(ring, 128)[: 128 * 640].reshape(128, 640)
    filtered = lax.dot_general(
        frames, bank, (((1,), (1,)), ((), ())), preferred_element_type=jnp.float32
    )
    filtered = filtered.astype(jnp.bfloat16).reshape(local_stations * 3, decimated + 128)
    past_end = (corr_place == corr_count - 1) & (lax.iota(jnp.int32, decimated + 128) >= decimated)
    filtered = jnp.where(past_end[None, :], jnp.zeros_like(filtered), filtered)
    per_block = corr_count // filt_count
    block = per_block * decimated
    width = block // corr_count
    span = width + 128
    received = []
    for k in range(filt_count):
        piece = (filt_place + k) % filt_count
        part = lax.dynamic_slice_in_dim(filtered, piece * width, span, 1)
        route = []
        for c in range(corr_count):
            for f in range(filt_count):
                dest = ((c % per_block) * filt_count + (f + k) % filt_count) * filt_count + c // per_block
                route.append((c * filt_count + f, dest))
        received.append(lax.ppermute(part, ("corr", "filt"), route))
    rows = jnp.concatenate(received, axis=0)
    energy = window_energy(rows.astype(jnp.float32), width)
    inv = lax.rsqrt(jnp.maximum(energy, 1.0))
    tile = min(TT, width)
    tiles = width // tile
    windows = jnp.stack([rows[:, i * tile : i * tile + tile + 128] for i in range(tiles)], axis=0)

    templates = gathered_templates
    count = templates.shape[0]
    stations = masks.shape[2]
    shaped = templates.astype(jnp.float32).reshape(count, 3, L)
    norms = jnp.sqrt(jnp.sum(shaped * shaped, axis=2) + 1e-06)
    base = shaped / norms[:, :, None]
    arrival = (corr_place - lax.iota(jnp.int32, filt_count)) % filt_count
    blocked = masks.reshape(count, 3, filt_count, stations // filt_count)
    if filt_count == 2:
        swapped = jnp.concatenate([blocked[:, :, 1:], blocked[:, :, :1]], axis=2)
        chosen = jnp.where(arrival[0] == 0, blocked, swapped)
    else:
        chosen = jnp.take(blocked, arrival, axis=2)
    chosen = chosen.reshape(count, 3, stations).astype(jnp.float32)
    total_rows = stations * 3
    row_block = 96 if total_rows % 96 == 0 else total_rows
    chunks = total_rows // row_block
    if chunks == 1:
        padded = jnp.concatenate([base, jnp.zeros((count, 3, JPI - L), base.dtype)], axis=2)
        padded = padded.astype(jnp.bfloat16).reshape(count, 3 * JPI)
        flat = jnp.transpose(chosen, (0, 1, 2)).reshape(count, total_rows).astype(jnp.bfloat16)
        start_zero = lax.optimization_barrier(jnp.zeros((), jnp.int32))
        column = lax.iota(jnp.int32, JPI * total_rows) + start_zero
        group = column // (JPI * RSUB)
        lag = (column % (JPI * RSUB)) // RSUB
        row = group * RSUB + column % RSUB
        source = lax.iota(jnp.int32, 3 * JPI)
        pick_base = (
            (source[:, None] % JPI == lag[None, :]) & (source[:, None] // JPI == row[None, :] % 3)
        ).astype(jnp.bfloat16)
        slot = lax.iota(jnp.int32, total_rows)
        pick_mask = (
            (slot[:, None] // stations == row[None, :] % 3)
            & (slot[:, None] % stations == row[None, :] // 3)
        ).astype(jnp.bfloat16)
        spread = jnp.dot(padded, pick_base, preferred_element_type=jnp.float32)
        gate = jnp.dot(flat, pick_mask, preferred_element_type=jnp.float32)
        weights = (spread * gate).astype(jnp.bfloat16)
    else:
        full = jnp.transpose(base, (0, 2, 1))[:, :, None, :] * jnp.transpose(chosen, (0, 2, 1))[:, None, :, :]
        full = full.astype(jnp.bfloat16).reshape(count, L, stations * 3)
        full = jnp.concatenate([full, jnp.zeros((count, JP - L, stations * 3), full.dtype)], axis=1)
        weights = (
            full.reshape(count, JP, chunks, row_block)
            .transpose(0, 2, 1, 3)
            .reshape(count, chunks * JP * row_block)
        )
    stacked = correlate(windows, inv, weights, row_block, interleaved=chunks == 1)
    stacked = lax.all_to_all(
        stacked.reshape(corr_count, local_count, width), "corr", 0, 0, tiled=True
    )
    stacked = jnp.transpose(stacked, (1, 0, 2)).reshape(local_count, corr_count * width)
    return stacked[None]


def solution(mesh):
    return jax.shard_map(
        body,
        mesh=mesh,
        in_specs=(
            P(("groups", "pair"), "filt", None, "corr"),
            P(("groups", "pair"), "filt"),
            P(),
            P("corr", None),
            P(),
        ),
        out_specs=P(("groups", "pair"), "corr", "filt"),
        check_vma=False,
    )
```

```python
import functools

import jax
import jax.numpy as jnp
from jax import lax
from jax.experimental import pallas as pl
from jax.experimental.pallas import tpu as pltpu
from jax.sharding import PartitionSpec as P

L = 75
TAPS = 64
DEC = 4
JP = 76
JPI = 80
TT = 512
RSUB = 16


def from_behind(block, axis, distance):
    devices = range(lax.axis_size(axis))
    route = [(i - distance, i) for i in devices if i - distance in devices]
    return lax.ppermute(block, axis, route)


def window_energy(rows, width):
    p1 = rows * rows
    p2 = p1[:, :-1] + p1[:, 1:]
    p4 = p2[:, :-2] + p2[:, 2:]
    p8 = p4[:, :-4] + p4[:, 4:]
    p16 = p8[:, :-8] + p8[:, 8:]
    p32 = p16[:, :-16] + p16[:, 16:]
    p64 = p32[:, :-32] + p32[:, 32:]
    return (
        p64[:, :width]
        + p8[:, 64 : 64 + width]
        + p2[:, 72 : 72 + width]
        + p1[:, 74 : 74 + width]
    )


def corr_kernel(f_ref, inv_ref, w_ref, o_ref, s_ref, *, row_block, tile):
    q = pl.program_id(1)
    span = tile + 128

    def fill(sub, carry):
        r0 = pl.multiple_of(sub * RSUB, RSUB)
        seg = f_ref[0, pl.ds(r0, RSUB), :].astype(jnp.float32)
        inv = inv_ref[pl.ds(r0, RSUB), :]
        for j in range(JP):
            moved = seg if j == 0 else pltpu.roll(seg, span - j, 1)
            piece = (moved[:, :tile] * inv).astype(jnp.bfloat16)
            s_ref[pl.ds(pl.multiple_of(j * row_block + r0, RSUB), RSUB), :] = piece
        return carry

    lax.fori_loop(0, row_block // RSUB, fill, 0)
    part = jnp.dot(w_ref[...], s_ref[...], preferred_element_type=jnp.float32)

    @pl.when(q == 0)
    def _():
        o_ref[...] = part

    @pl.when(q > 0)
    def _():
        o_ref[...] += part


def corr_kernel_interleaved(f_ref, inv_ref, w_ref, o_ref, s_ref, *, row_block, tile):
    span = tile + 128
    depth = JPI * RSUB
    part = None
    for sub in range(row_block // RSUB):
        r0 = sub * RSUB
        seg = f_ref[0, r0 : r0 + RSUB, :].astype(jnp.float32)
        inv = inv_ref[r0 : r0 + RSUB, :]
        for j in range(JPI):
            moved = seg if j == 0 else pltpu.roll(seg, span - j, 1)
            piece = (moved[:, :tile] * inv).astype(jnp.bfloat16)
            s_ref[sub * depth + j * RSUB : sub * depth + (j + 1) * RSUB, :] = piece
        step = jnp.dot(
            w_ref[:, sub * depth : (sub + 1) * depth],
            s_ref[sub * depth : (sub + 1) * depth, :],
            preferred_element_type=jnp.float32,
        )
        part = step if part is None else part + step
    o_ref[...] = part


def correlate(windows, inv, weights, row_block, interleaved=False):
    tiles, rows, span = windows.shape
    count = weights.shape[0]
    width = inv.shape[1]
    tile = width // tiles
    chunks = rows // row_block
    lags = JPI if interleaved else JP
    body_fn = corr_kernel_interleaved if interleaved else corr_kernel
    return pl.pallas_call(
        functools.partial(body_fn, row_block=row_block, tile=tile),
        grid=(tiles, chunks),
        in_specs=[
            pl.BlockSpec((1, row_block, span), lambda i, q: (i, q, 0)),
            pl.BlockSpec((row_block, tile), lambda i, q: (q, i)),
            pl.BlockSpec((count, lags * row_block), lambda i, q: (0, q)),
        ],
        out_specs=pl.BlockSpec((count, tile), lambda i, q: (0, i)),
        out_shape=jax.ShapeDtypeStruct((count, width), jnp.float32),
        scratch_shapes=[pltpu.VMEM((lags * row_block, tile), jnp.bfloat16)],
        compiler_params=pltpu.CompilerParams(
            dimension_semantics=("parallel", "arbitrary"),
            vmem_limit_bytes=48 * 1024 * 1024,
        ),
    )(windows, inv, weights)


def body(raw_rows, valid_counts, taps, templates, masks):
    samples = raw_rows[0]
    counts = valid_counts[0]
    local_stations = samples.shape[0]
    raw_width = samples.shape[2]
    corr_place = lax.axis_index("corr")
    filt_place = lax.axis_index("filt")
    filt_count = lax.axis_size("filt")
    sample_times = corr_place * raw_width + lax.iota(jnp.int32, raw_width)
    keep = sample_times[None, None, :] < counts[:, None, None]
    live = jnp.where(keep, samples, jnp.zeros_like(samples)).reshape(local_stations * 3, raw_width)
    corr_count = lax.axis_size("corr")
    local_count = templates.shape[0]
    template_width = templates.shape[1]
    lanes = -(-template_width // 256) * 256
    wide = jnp.concatenate(
        [templates, jnp.zeros((local_count, lanes - template_width), templates.dtype)], axis=1
    )
    forward = [(i, (i + 1) % corr_count) for i in range(corr_count)]
    backward = [(i, (i - 1) % corr_count) for i in range(corr_count)]
    tail_rows = live.shape[0]
    sent = jnp.concatenate([live[:, raw_width - 128 :], wide.reshape(-1, 128)], axis=0)
    got = lax.ppermute(sent, "corr", forward)
    history = jnp.where(corr_place > 0, got[:tail_rows], jnp.zeros_like(got[:tail_rows]))
    from_previous = got[tail_rows:].reshape(local_count, lanes)
    sent = jnp.concatenate([live[:, :512], wide.reshape(-1, 512)], axis=0)
    got = lax.ppermute(sent, "corr", backward)
    ahead = jnp.where(corr_place < corr_count - 1, got[:tail_rows], jnp.zeros_like(got[:tail_rows]))
    from_next = got[tail_rows:].reshape(local_count, lanes)
    blocks_by_offset = {0: wide, 1: from_previous, corr_count - 1: from_next}
    for d in range(2, corr_count - 1):
        route = [(i, (i + d) % corr_count) for i in range(corr_count)]
        blocks_by_offset[d] = lax.ppermute(wide, "corr", route)
    by_offset = jnp.stack([blocks_by_offset[d] for d in range(corr_count)], axis=0)
    gathered_templates = jnp.concatenate(
        [
            lax.dynamic_index_in_dim(by_offset, (corr_place - b) % corr_count, 0, keepdims=False)
            for b in range(corr_count)
        ],
        axis=0,
    )[:, :template_width]
    decimated = raw_width // DEC
    blocks = decimated // 128 + 1
    rows_in = live.shape[0]
    flip = (lax.iota(jnp.int32, TAPS)[:, None] + lax.iota(jnp.int32, TAPS)[None, :] == TAPS - 1)
    reversed_taps = jnp.dot(
        taps[None, :], flip.astype(taps.dtype), preferred_element_type=jnp.float32
    )[0].astype(taps.dtype)
    ring = jnp.concatenate(
        [jnp.zeros((65,), taps.dtype), reversed_taps, jnp.zeros((644 - 129,), taps.dtype)]
    )
    bank = jnp.tile(ring, 128)[: 128 * 640].reshape(128, 640)

    def apply_bank(frames):
        return lax.dot_general(
            frames, bank, (((1,), (1,)), ((), ())), preferred_element_type=jnp.float32
        )

    inner = jnp.stack(
        [live[:, 512 * a - 128 : 512 * a + 512] for a in range(1, blocks - 1)], axis=1
    ).reshape(rows_in * (blocks - 2), 640)
    inner = apply_bank(inner).reshape(rows_in, (blocks - 2) * 128)
    first = apply_bank(jnp.concatenate([history, live[:, :512]], axis=1))
    last = apply_bank(jnp.concatenate([live[:, raw_width - 128 :], ahead], axis=1))
    filtered = jnp.concatenate([first, inner, last], axis=1)
    filtered = filtered.astype(jnp.bfloat16).reshape(local_stations * 3, decimated + 128)
    past_end = (corr_place == corr_count - 1) & (lax.iota(jnp.int32, decimated + 128) >= decimated)
    filtered = jnp.where(past_end[None, :], jnp.zeros_like(filtered), filtered)
    per_block = corr_count // filt_count
    block = per_block * decimated
    width = block // corr_count
    span = width + 128
    received = []
    for k in range(filt_count):
        piece = (filt_place + k) % filt_count
        part = lax.dynamic_slice_in_dim(filtered, piece * width, span, 1)
        route = []
        for c in range(corr_count):
            for f in range(filt_count):
                dest = ((c % per_block) * filt_count + (f + k) % filt_count) * filt_count + c // per_block
                route.append((c * filt_count + f, dest))
        received.append(lax.ppermute(part, ("corr", "filt"), route))
    rows = jnp.concatenate(received, axis=0)
    energy = window_energy(rows.astype(jnp.float32), width)
    inv = lax.rsqrt(jnp.maximum(energy, 1.0))
    tile = min(TT, width)
    tiles = width // tile
    windows = jnp.stack([rows[:, i * tile : i * tile + tile + 128] for i in range(tiles)], axis=0)

    templates = gathered_templates
    count = templates.shape[0]
    stations = masks.shape[2]
    shaped = templates.astype(jnp.float32).reshape(count, 3, L)
    norms = jnp.sqrt(jnp.sum(shaped * shaped, axis=2) + 1e-06)
    base = shaped / norms[:, :, None]
    arrival = (corr_place - lax.iota(jnp.int32, filt_count)) % filt_count
    blocked = masks.reshape(count, 3, filt_count, stations // filt_count)
    if filt_count == 2:
        swapped = jnp.concatenate([blocked[:, :, 1:], blocked[:, :, :1]], axis=2)
        chosen = jnp.where(arrival[0] == 0, blocked, swapped)
    else:
        chosen = jnp.take(blocked, arrival, axis=2)
    chosen = chosen.reshape(count, 3, stations).astype(jnp.float32)
    total_rows = stations * 3
    row_block = 96 if total_rows % 96 == 0 else total_rows
    chunks = total_rows // row_block
    if chunks == 1:
        padded = jnp.concatenate([base, jnp.zeros((count, 3, JPI - L), base.dtype)], axis=2)
        padded = padded.astype(jnp.bfloat16).reshape(count, 3 * JPI)
        flat = jnp.transpose(chosen, (0, 1, 2)).reshape(count, total_rows).astype(jnp.bfloat16)
        start_zero = lax.optimization_barrier(jnp.zeros((), jnp.int32))
        column = lax.iota(jnp.int32, JPI * total_rows) + start_zero
        group = column // (JPI * RSUB)
        lag = (column % (JPI * RSUB)) // RSUB
        row = group * RSUB + column % RSUB
        source = lax.iota(jnp.int32, 3 * JPI)
        pick_base = (
            (source[:, None] % JPI == lag[None, :]) & (source[:, None] // JPI == row[None, :] % 3)
        ).astype(jnp.bfloat16)
        slot = lax.iota(jnp.int32, total_rows)
        pick_mask = (
            (slot[:, None] // stations == row[None, :] % 3)
            & (slot[:, None] % stations == row[None, :] // 3)
        ).astype(jnp.bfloat16)
        spread = jnp.dot(padded, pick_base, preferred_element_type=jnp.float32)
        gate = jnp.dot(flat, pick_mask, preferred_element_type=jnp.float32)
        weights = (spread * gate).astype(jnp.bfloat16)
    else:
        full = jnp.transpose(base, (0, 2, 1))[:, :, None, :] * jnp.transpose(chosen, (0, 2, 1))[:, None, :, :]
        full = full.astype(jnp.bfloat16).reshape(count, L, stations * 3)
        full = jnp.concatenate([full, jnp.zeros((count, JP - L, stations * 3), full.dtype)], axis=1)
        weights = (
            full.reshape(count, JP, chunks, row_block)
            .transpose(0, 2, 1, 3)
            .reshape(count, chunks * JP * row_block)
        )
    stacked = correlate(windows, inv, weights, row_block, interleaved=chunks == 1)
    pieces = [lax.dynamic_slice_in_dim(stacked, corr_place * local_count, local_count, 0)]
    for d in range(1, corr_count):
        target = (corr_place + d) % corr_count
        part = lax.dynamic_slice_in_dim(stacked, target * local_count, local_count, 0)
        route = [(i, (i + d) % corr_count) for i in range(corr_count)]
        pieces.append(lax.ppermute(part, "corr", route))
    stacked = jnp.zeros((local_count, corr_count * width), jnp.float32)
    for d, part in enumerate(pieces):
        place = ((corr_place - d) % corr_count) * width
        stacked = lax.dynamic_update_slice_in_dim(stacked, part, place, 1)
    return stacked[None]


def solution(mesh):
    return jax.shard_map(
        body,
        mesh=mesh,
        in_specs=(
            P(("groups", "pair"), "filt", None, "corr"),
            P(("groups", "pair"), "filt"),
            P(),
            P("corr", None),
            P(),
        ),
        out_specs=P(("groups", "pair"), "corr", "filt"),
        check_vma=False,
    )
```

```python
import functools

import jax
import jax.numpy as jnp
from jax import lax
from jax.experimental import pallas as pl
from jax.experimental.pallas import tpu as pltpu
from jax.sharding import PartitionSpec as P

L = 75
TAPS = 64
DEC = 4
JP = 76
JPI = 80
TT = 512
RSUB = 16


def from_behind(block, axis, distance):
    devices = range(lax.axis_size(axis))
    route = [(i - distance, i) for i in devices if i - distance in devices]
    return lax.ppermute(block, axis, route)


def window_energy(rows, width):
    p1 = rows * rows
    p2 = p1[:, :-1] + p1[:, 1:]
    p4 = p2[:, :-2] + p2[:, 2:]
    p8 = p4[:, :-4] + p4[:, 4:]
    p16 = p8[:, :-8] + p8[:, 8:]
    p32 = p16[:, :-16] + p16[:, 16:]
    p64 = p32[:, :-32] + p32[:, 32:]
    return (
        p64[:, :width]
        + p8[:, 64 : 64 + width]
        + p2[:, 72 : 72 + width]
        + p1[:, 74 : 74 + width]
    )


def corr_kernel(f_ref, inv_ref, w_ref, o_ref, s_ref, *, row_block, tile):
    q = pl.program_id(1)
    span = tile + 128

    def fill(sub, carry):
        r0 = pl.multiple_of(sub * RSUB, RSUB)
        seg = f_ref[0, pl.ds(r0, RSUB), :].astype(jnp.float32)
        inv = inv_ref[pl.ds(r0, RSUB), :]
        for j in range(JP):
            moved = seg if j == 0 else pltpu.roll(seg, span - j, 1)
            piece = (moved[:, :tile] * inv).astype(jnp.bfloat16)
            s_ref[pl.ds(pl.multiple_of(j * row_block + r0, RSUB), RSUB), :] = piece
        return carry

    lax.fori_loop(0, row_block // RSUB, fill, 0)
    part = jnp.dot(w_ref[...], s_ref[...], preferred_element_type=jnp.float32)

    @pl.when(q == 0)
    def _():
        o_ref[...] = part

    @pl.when(q > 0)
    def _():
        o_ref[...] += part


def corr_kernel_interleaved(f_ref, inv_ref, w_ref, o_ref, s_ref, *, row_block, tile):
    span = tile + 128
    depth = JPI * RSUB
    part = None
    for sub in range(row_block // RSUB):
        r0 = sub * RSUB
        seg = f_ref[0, r0 : r0 + RSUB, :].astype(jnp.float32)
        inv = inv_ref[r0 : r0 + RSUB, :]
        for j in range(JPI):
            moved = seg if j == 0 else pltpu.roll(seg, span - j, 1)
            piece = (moved[:, :tile] * inv).astype(jnp.bfloat16)
            s_ref[sub * depth + j * RSUB : sub * depth + (j + 1) * RSUB, :] = piece
        step = jnp.dot(
            w_ref[:, sub * depth : (sub + 1) * depth],
            s_ref[sub * depth : (sub + 1) * depth, :],
            preferred_element_type=jnp.float32,
        )
        part = step if part is None else part + step
    o_ref[...] = part


def correlate(windows, inv, weights, row_block, interleaved=False):
    tiles, rows, span = windows.shape
    count = weights.shape[0]
    width = inv.shape[1]
    tile = width // tiles
    chunks = rows // row_block
    lags = JPI if interleaved else JP
    body_fn = corr_kernel_interleaved if interleaved else corr_kernel
    return pl.pallas_call(
        functools.partial(body_fn, row_block=row_block, tile=tile),
        grid=(tiles, chunks),
        in_specs=[
            pl.BlockSpec((1, row_block, span), lambda i, q: (i, q, 0)),
            pl.BlockSpec((row_block, tile), lambda i, q: (q, i)),
            pl.BlockSpec((count, lags * row_block), lambda i, q: (0, q)),
        ],
        out_specs=pl.BlockSpec((count, tile), lambda i, q: (0, i)),
        out_shape=jax.ShapeDtypeStruct((count, width), jnp.float32),
        scratch_shapes=[pltpu.VMEM((lags * row_block, tile), jnp.bfloat16)],
        compiler_params=pltpu.CompilerParams(
            dimension_semantics=("parallel", "arbitrary"),
            vmem_limit_bytes=48 * 1024 * 1024,
        ),
    )(windows, inv, weights)


def body(raw_rows, valid_counts, taps, templates, masks):
    samples = raw_rows[0]
    counts = valid_counts[0]
    local_stations = samples.shape[0]
    raw_width = samples.shape[2]
    corr_place = lax.axis_index("corr")
    filt_place = lax.axis_index("filt")
    filt_count = lax.axis_size("filt")
    sample_times = corr_place * raw_width + lax.iota(jnp.int32, raw_width)
    dense = samples.reshape(local_stations * 3, raw_width)
    limit = jnp.repeat(counts - corr_place * raw_width, 3)
    live = jnp.where(
        lax.iota(jnp.int32, raw_width)[None, :] < limit[:, None], dense, jnp.zeros_like(dense)
    )
    corr_count = lax.axis_size("corr")
    local_count = templates.shape[0]
    template_width = templates.shape[1]
    lanes = -(-template_width // 256) * 256
    wide = jnp.concatenate(
        [templates, jnp.zeros((local_count, lanes - template_width), templates.dtype)], axis=1
    )
    forward = [(i, (i + 1) % corr_count) for i in range(corr_count)]
    backward = [(i, (i - 1) % corr_count) for i in range(corr_count)]
    tail_rows = live.shape[0]
    sent = jnp.concatenate([live[:, raw_width - 128 :], wide.reshape(-1, 128)], axis=0)
    got = lax.ppermute(sent, "corr", forward)
    history = jnp.where(corr_place > 0, got[:tail_rows], jnp.zeros_like(got[:tail_rows]))
    from_previous = got[tail_rows:].reshape(local_count, lanes)
    sent = jnp.concatenate([live[:, :512], wide.reshape(-1, 512)], axis=0)
    got = lax.ppermute(sent, "corr", backward)
    ahead = jnp.where(corr_place < corr_count - 1, got[:tail_rows], jnp.zeros_like(got[:tail_rows]))
    from_next = got[tail_rows:].reshape(local_count, lanes)
    blocks_by_offset = {0: wide, 1: from_previous, corr_count - 1: from_next}
    for d in range(2, corr_count - 1):
        route = [(i, (i + d) % corr_count) for i in range(corr_count)]
        blocks_by_offset[d] = lax.ppermute(wide, "corr", route)
    by_offset = jnp.stack([blocks_by_offset[d] for d in range(corr_count)], axis=0)
    gathered_templates = jnp.concatenate(
        [
            lax.dynamic_index_in_dim(by_offset, (corr_place - b) % corr_count, 0, keepdims=False)
            for b in range(corr_count)
        ],
        axis=0,
    )[:, :template_width]
    decimated = raw_width // DEC
    blocks = decimated // 128 + 1
    rows_in = live.shape[0]
    flip = (lax.iota(jnp.int32, TAPS)[:, None] + lax.iota(jnp.int32, TAPS)[None, :] == TAPS - 1)
    reversed_taps = jnp.dot(
        taps[None, :], flip.astype(taps.dtype), preferred_element_type=jnp.float32
    )[0].astype(taps.dtype)
    ring = jnp.concatenate(
        [jnp.zeros((65,), taps.dtype), reversed_taps, jnp.zeros((644 - 129,), taps.dtype)]
    )
    bank = jnp.tile(ring, 128)[: 128 * 640].reshape(128, 640)

    def apply_bank(frames):
        return lax.dot_general(
            frames, bank, (((1,), (1,)), ((), ())), preferred_element_type=jnp.float32
        )

    inner = jnp.stack(
        [live[:, 512 * a - 128 : 512 * a + 512] for a in range(1, blocks - 1)], axis=1
    ).reshape(rows_in * (blocks - 2), 640)
    inner = apply_bank(inner).reshape(rows_in, (blocks - 2) * 128)
    first = apply_bank(jnp.concatenate([history, live[:, :512]], axis=1))
    last = apply_bank(jnp.concatenate([live[:, raw_width - 128 :], ahead], axis=1))
    filtered = jnp.concatenate([first, inner, last], axis=1)
    filtered = filtered.astype(jnp.bfloat16).reshape(local_stations * 3, decimated + 128)
    past_end = (corr_place == corr_count - 1) & (lax.iota(jnp.int32, decimated + 128) >= decimated)
    filtered = jnp.where(past_end[None, :], jnp.zeros_like(filtered), filtered)
    per_block = corr_count // filt_count
    block = per_block * decimated
    width = block // corr_count
    span = width + 128
    received = []
    for k in range(filt_count):
        piece = (filt_place + k) % filt_count
        part = lax.dynamic_slice_in_dim(filtered, piece * width, span, 1)
        route = []
        for c in range(corr_count):
            for f in range(filt_count):
                dest = ((c % per_block) * filt_count + (f + k) % filt_count) * filt_count + c // per_block
                route.append((c * filt_count + f, dest))
        received.append(lax.ppermute(part, ("corr", "filt"), route))
    rows = jnp.concatenate(received, axis=0)
    energy = window_energy(rows.astype(jnp.float32), width)
    inv = lax.rsqrt(jnp.maximum(energy, 1.0))
    tile = min(TT, width)
    tiles = width // tile
    windows = jnp.stack([rows[:, i * tile : i * tile + tile + 128] for i in range(tiles)], axis=0)

    templates = gathered_templates
    count = templates.shape[0]
    stations = masks.shape[2]
    shaped = templates.astype(jnp.float32).reshape(count, 3, L)
    norms = jnp.sqrt(jnp.sum(shaped * shaped, axis=2) + 1e-06)
    base = shaped / norms[:, :, None]
    arrival = (corr_place - lax.iota(jnp.int32, filt_count)) % filt_count
    blocked = masks.reshape(count, 3, filt_count, stations // filt_count)
    if filt_count == 2:
        swapped = jnp.concatenate([blocked[:, :, 1:], blocked[:, :, :1]], axis=2)
        chosen = jnp.where(arrival[0] == 0, blocked, swapped)
    else:
        chosen = jnp.take(blocked, arrival, axis=2)
    chosen = chosen.reshape(count, 3, stations).astype(jnp.float32)
    total_rows = stations * 3
    row_block = 96 if total_rows % 96 == 0 else total_rows
    chunks = total_rows // row_block
    if chunks == 1:
        padded = jnp.concatenate([base, jnp.zeros((count, 3, JPI - L), base.dtype)], axis=2)
        padded = padded.astype(jnp.bfloat16).reshape(count, 3 * JPI)
        flat = jnp.transpose(chosen, (0, 1, 2)).reshape(count, total_rows).astype(jnp.bfloat16)
        start_zero = lax.optimization_barrier(jnp.zeros((), jnp.int32))
        column = lax.iota(jnp.int32, JPI * total_rows) + start_zero
        group = column // (JPI * RSUB)
        lag = (column % (JPI * RSUB)) // RSUB
        row = group * RSUB + column % RSUB
        source = lax.iota(jnp.int32, 3 * JPI)
        pick_base = (
            (source[:, None] % JPI == lag[None, :]) & (source[:, None] // JPI == row[None, :] % 3)
        ).astype(jnp.bfloat16)
        slot = lax.iota(jnp.int32, total_rows)
        pick_mask = (
            (slot[:, None] // stations == row[None, :] % 3)
            & (slot[:, None] % stations == row[None, :] // 3)
        ).astype(jnp.bfloat16)
        spread = jnp.dot(padded, pick_base, preferred_element_type=jnp.float32)
        gate = jnp.dot(flat, pick_mask, preferred_element_type=jnp.float32)
        weights = (spread * gate).astype(jnp.bfloat16)
    else:
        full = jnp.transpose(base, (0, 2, 1))[:, :, None, :] * jnp.transpose(chosen, (0, 2, 1))[:, None, :, :]
        full = full.astype(jnp.bfloat16).reshape(count, L, stations * 3)
        full = jnp.concatenate([full, jnp.zeros((count, JP - L, stations * 3), full.dtype)], axis=1)
        weights = (
            full.reshape(count, JP, chunks, row_block)
            .transpose(0, 2, 1, 3)
            .reshape(count, chunks * JP * row_block)
        )
    stacked = correlate(windows, inv, weights, row_block, interleaved=chunks == 1)
    pieces = [lax.dynamic_slice_in_dim(stacked, corr_place * local_count, local_count, 0)]
    for d in range(1, corr_count):
        target = (corr_place + d) % corr_count
        part = lax.dynamic_slice_in_dim(stacked, target * local_count, local_count, 0)
        route = [(i, (i + d) % corr_count) for i in range(corr_count)]
        pieces.append(lax.ppermute(part, "corr", route))
    stacked = jnp.zeros((local_count, corr_count * width), jnp.float32)
    for d, part in enumerate(pieces):
        place = ((corr_place - d) % corr_count) * width
        stacked = lax.dynamic_update_slice_in_dim(stacked, part, place, 1)
    return stacked[None]


def solution(mesh):
    return jax.shard_map(
        body,
        mesh=mesh,
        in_specs=(
            P(("groups", "pair"), "filt", None, "corr"),
            P(("groups", "pair"), "filt"),
            P(),
            P("corr", None),
            P(),
        ),
        out_specs=P(("groups", "pair"), "corr", "filt"),
        check_vma=False,
    )
```

```python
import functools

import jax
import jax.numpy as jnp
from jax import lax
from jax.experimental import pallas as pl
from jax.experimental.pallas import tpu as pltpu
from jax.sharding import PartitionSpec as P

L = 75
TAPS = 64
DEC = 4
JP = 76
JPI = 80
TT = 512
RSUB = 16


def from_behind(block, axis, distance):
    devices = range(lax.axis_size(axis))
    route = [(i - distance, i) for i in devices if i - distance in devices]
    return lax.ppermute(block, axis, route)


def window_energy(rows, width):
    p1 = rows * rows
    p2 = p1[:, :-1] + p1[:, 1:]
    p4 = p2[:, :-2] + p2[:, 2:]
    p8 = p4[:, :-4] + p4[:, 4:]
    p16 = p8[:, :-8] + p8[:, 8:]
    p32 = p16[:, :-16] + p16[:, 16:]
    p64 = p32[:, :-32] + p32[:, 32:]
    return (
        p64[:, :width]
        + p8[:, 64 : 64 + width]
        + p2[:, 72 : 72 + width]
        + p1[:, 74 : 74 + width]
    )


def corr_kernel(f_ref, inv_ref, w_ref, o_ref, s_ref, *, row_block, tile):
    q = pl.program_id(1)
    span = tile + 128

    def fill(sub, carry):
        r0 = pl.multiple_of(sub * RSUB, RSUB)
        seg = f_ref[0, pl.ds(r0, RSUB), :].astype(jnp.float32)
        inv = inv_ref[pl.ds(r0, RSUB), :]
        for j in range(JP):
            moved = seg if j == 0 else pltpu.roll(seg, span - j, 1)
            piece = (moved[:, :tile] * inv).astype(jnp.bfloat16)
            s_ref[pl.ds(pl.multiple_of(j * row_block + r0, RSUB), RSUB), :] = piece
        return carry

    lax.fori_loop(0, row_block // RSUB, fill, 0)
    part = jnp.dot(w_ref[...], s_ref[...], preferred_element_type=jnp.float32)

    @pl.when(q == 0)
    def _():
        o_ref[...] = part

    @pl.when(q > 0)
    def _():
        o_ref[...] += part


def corr_kernel_interleaved(f_ref, w_ref, o_ref, s_ref, *, row_block, tile):
    span = tile + 128
    depth = JPI * RSUB
    part = None
    for sub in range(row_block // RSUB):
        r0 = sub * RSUB
        seg = f_ref[0, r0 : r0 + RSUB, :].astype(jnp.float32)

        def ahead(x, k):
            return pltpu.roll(x, span - k, 1)

        p1 = seg * seg
        p2 = p1 + ahead(p1, 1)
        p4 = p2 + ahead(p2, 2)
        p8 = p4 + ahead(p4, 4)
        p16 = p8 + ahead(p8, 8)
        p32 = p16 + ahead(p16, 16)
        p64 = p32 + ahead(p32, 32)
        energy = ((p64 + ahead(p8, 64)) + ahead(p2, 72)) + ahead(p1, 74)
        inv = lax.rsqrt(jnp.maximum(energy[:, :tile], 1.0))
        for j in range(JPI):
            moved = seg if j == 0 else pltpu.roll(seg, span - j, 1)
            piece = (moved[:, :tile] * inv).astype(jnp.bfloat16)
            s_ref[sub * depth + j * RSUB : sub * depth + (j + 1) * RSUB, :] = piece
        step = jnp.dot(
            w_ref[:, sub * depth : (sub + 1) * depth],
            s_ref[sub * depth : (sub + 1) * depth, :],
            preferred_element_type=jnp.float32,
        )
        part = step if part is None else part + step
    o_ref[...] = part


def correlate(windows, inv, weights, row_block, interleaved=False):
    tiles, rows, span = windows.shape
    count = weights.shape[0]
    width = inv.shape[1]
    tile = width // tiles
    chunks = rows // row_block
    lags = JPI if interleaved else JP
    body_fn = corr_kernel_interleaved if interleaved else corr_kernel
    return pl.pallas_call(
        functools.partial(body_fn, row_block=row_block, tile=tile),
        grid=(tiles, chunks),
        in_specs=[pl.BlockSpec((1, row_block, span), lambda i, q: (i, q, 0))]
        + ([] if interleaved else [pl.BlockSpec((row_block, tile), lambda i, q: (q, i))])
        + [pl.BlockSpec((count, lags * row_block), lambda i, q: (0, q))],
        out_specs=pl.BlockSpec((count, tile), lambda i, q: (0, i)),
        out_shape=jax.ShapeDtypeStruct((count, width), jnp.float32),
        scratch_shapes=[pltpu.VMEM((lags * row_block, tile), jnp.bfloat16)],
        compiler_params=pltpu.CompilerParams(
            dimension_semantics=("parallel", "arbitrary"),
            vmem_limit_bytes=48 * 1024 * 1024,
        ),
    )(*((windows, weights) if interleaved else (windows, inv, weights)))


def body(raw_rows, valid_counts, taps, templates, masks):
    samples = raw_rows[0]
    counts = valid_counts[0]
    local_stations = samples.shape[0]
    raw_width = samples.shape[2]
    corr_place = lax.axis_index("corr")
    filt_place = lax.axis_index("filt")
    filt_count = lax.axis_size("filt")
    sample_times = corr_place * raw_width + lax.iota(jnp.int32, raw_width)
    dense = samples.reshape(local_stations * 3, raw_width)
    limit = jnp.repeat(counts - corr_place * raw_width, 3)
    live = jnp.where(
        lax.iota(jnp.int32, raw_width)[None, :] < limit[:, None], dense, jnp.zeros_like(dense)
    )
    corr_count = lax.axis_size("corr")
    local_count = templates.shape[0]
    template_width = templates.shape[1]
    lanes = -(-template_width // 256) * 256
    wide = jnp.concatenate(
        [templates, jnp.zeros((local_count, lanes - template_width), templates.dtype)], axis=1
    )
    forward = [(i, (i + 1) % corr_count) for i in range(corr_count)]
    backward = [(i, (i - 1) % corr_count) for i in range(corr_count)]
    tail_rows = live.shape[0]
    sent = jnp.concatenate([live[:, raw_width - 128 :], wide.reshape(-1, 128)], axis=0)
    got = lax.ppermute(sent, "corr", forward)
    history = jnp.where(corr_place > 0, got[:tail_rows], jnp.zeros_like(got[:tail_rows]))
    from_previous = got[tail_rows:].reshape(local_count, lanes)
    sent = jnp.concatenate([live[:, :512], wide.reshape(-1, 512)], axis=0)
    got = lax.ppermute(sent, "corr", backward)
    ahead = jnp.where(corr_place < corr_count - 1, got[:tail_rows], jnp.zeros_like(got[:tail_rows]))
    from_next = got[tail_rows:].reshape(local_count, lanes)
    blocks_by_offset = {0: wide, 1: from_previous, corr_count - 1: from_next}
    for d in range(2, corr_count - 1):
        route = [(i, (i + d) % corr_count) for i in range(corr_count)]
        blocks_by_offset[d] = lax.ppermute(wide, "corr", route)
    by_offset = jnp.stack([blocks_by_offset[d] for d in range(corr_count)], axis=0)
    gathered_templates = jnp.concatenate(
        [
            lax.dynamic_index_in_dim(by_offset, (corr_place - b) % corr_count, 0, keepdims=False)
            for b in range(corr_count)
        ],
        axis=0,
    )[:, :template_width]
    decimated = raw_width // DEC
    blocks = decimated // 128 + 1
    rows_in = live.shape[0]
    flip = (lax.iota(jnp.int32, TAPS)[:, None] + lax.iota(jnp.int32, TAPS)[None, :] == TAPS - 1)
    reversed_taps = jnp.dot(
        taps[None, :], flip.astype(taps.dtype), preferred_element_type=jnp.float32
    )[0].astype(taps.dtype)
    ring = jnp.concatenate(
        [jnp.zeros((65,), taps.dtype), reversed_taps, jnp.zeros((644 - 129,), taps.dtype)]
    )
    bank = jnp.tile(ring, 128)[: 128 * 640].reshape(128, 640)

    def apply_bank(frames):
        return lax.dot_general(
            frames, bank, (((1,), (1,)), ((), ())), preferred_element_type=jnp.float32
        )

    inner = jnp.stack(
        [live[:, 512 * a - 128 : 512 * a + 512] for a in range(1, blocks - 1)], axis=1
    ).reshape(rows_in * (blocks - 2), 640)
    inner = apply_bank(inner).reshape(rows_in, (blocks - 2) * 128)
    first = apply_bank(jnp.concatenate([history, live[:, :512]], axis=1))
    last = apply_bank(jnp.concatenate([live[:, raw_width - 128 :], ahead], axis=1))
    filtered = jnp.concatenate([first, inner, last], axis=1)
    filtered = filtered.astype(jnp.bfloat16).reshape(local_stations * 3, decimated + 128)
    past_end = (corr_place == corr_count - 1) & (lax.iota(jnp.int32, decimated + 128) >= decimated)
    filtered = jnp.where(past_end[None, :], jnp.zeros_like(filtered), filtered)
    per_block = corr_count // filt_count
    block = per_block * decimated
    width = block // corr_count
    span = width + 128
    received = []
    for k in range(filt_count):
        piece = (filt_place + k) % filt_count
        part = lax.dynamic_slice_in_dim(filtered, piece * width, span, 1)
        route = []
        for c in range(corr_count):
            for f in range(filt_count):
                dest = ((c % per_block) * filt_count + (f + k) % filt_count) * filt_count + c // per_block
                route.append((c * filt_count + f, dest))
        received.append(lax.ppermute(part, ("corr", "filt"), route))
    rows = jnp.concatenate(received, axis=0)
    energy = window_energy(rows.astype(jnp.float32), width)
    inv = lax.rsqrt(jnp.maximum(energy, 1.0))
    tile = min(TT, width)
    tiles = width // tile
    windows = jnp.stack([rows[:, i * tile : i * tile + tile + 128] for i in range(tiles)], axis=0)

    templates = gathered_templates
    count = templates.shape[0]
    stations = masks.shape[2]
    shaped = templates.astype(jnp.float32).reshape(count, 3, L)
    norms = jnp.sqrt(jnp.sum(shaped * shaped, axis=2) + 1e-06)
    base = shaped / norms[:, :, None]
    arrival = (corr_place - lax.iota(jnp.int32, filt_count)) % filt_count
    blocked = masks.reshape(count, 3, filt_count, stations // filt_count)
    if filt_count == 2:
        swapped = jnp.concatenate([blocked[:, :, 1:], blocked[:, :, :1]], axis=2)
        chosen = jnp.where(arrival[0] == 0, blocked, swapped)
    else:
        chosen = jnp.take(blocked, arrival, axis=2)
    chosen = chosen.reshape(count, 3, stations).astype(jnp.float32)
    total_rows = stations * 3
    row_block = 96 if total_rows % 96 == 0 else total_rows
    chunks = total_rows // row_block
    if chunks == 1:
        padded = jnp.concatenate([base, jnp.zeros((count, 3, JPI - L), base.dtype)], axis=2)
        padded = padded.astype(jnp.bfloat16).reshape(count, 3 * JPI)
        flat = jnp.transpose(chosen, (0, 1, 2)).reshape(count, total_rows).astype(jnp.bfloat16)
        start_zero = lax.optimization_barrier(jnp.zeros((), jnp.int32))
        column = lax.iota(jnp.int32, JPI * total_rows) + start_zero
        group = column // (JPI * RSUB)
        lag = (column % (JPI * RSUB)) // RSUB
        row = group * RSUB + column % RSUB
        source = lax.iota(jnp.int32, 3 * JPI)
        pick_base = (
            (source[:, None] % JPI == lag[None, :]) & (source[:, None] // JPI == row[None, :] % 3)
        ).astype(jnp.bfloat16)
        slot = lax.iota(jnp.int32, total_rows)
        pick_mask = (
            (slot[:, None] // stations == row[None, :] % 3)
            & (slot[:, None] % stations == row[None, :] // 3)
        ).astype(jnp.bfloat16)
        spread = jnp.dot(padded, pick_base, preferred_element_type=jnp.float32)
        gate = jnp.dot(flat, pick_mask, preferred_element_type=jnp.float32)
        weights = (spread * gate).astype(jnp.bfloat16)
    else:
        full = jnp.transpose(base, (0, 2, 1))[:, :, None, :] * jnp.transpose(chosen, (0, 2, 1))[:, None, :, :]
        full = full.astype(jnp.bfloat16).reshape(count, L, stations * 3)
        full = jnp.concatenate([full, jnp.zeros((count, JP - L, stations * 3), full.dtype)], axis=1)
        weights = (
            full.reshape(count, JP, chunks, row_block)
            .transpose(0, 2, 1, 3)
            .reshape(count, chunks * JP * row_block)
        )
    stacked = correlate(windows, inv, weights, row_block, interleaved=chunks == 1)
    pieces = [lax.dynamic_slice_in_dim(stacked, corr_place * local_count, local_count, 0)]
    for d in range(1, corr_count):
        target = (corr_place + d) % corr_count
        part = lax.dynamic_slice_in_dim(stacked, target * local_count, local_count, 0)
        route = [(i, (i + d) % corr_count) for i in range(corr_count)]
        pieces.append(lax.ppermute(part, "corr", route))
    stacked = jnp.zeros((local_count, corr_count * width), jnp.float32)
    for d, part in enumerate(pieces):
        place = ((corr_place - d) % corr_count) * width
        stacked = lax.dynamic_update_slice_in_dim(stacked, part, place, 1)
    return stacked[None]


def solution(mesh):
    return jax.shard_map(
        body,
        mesh=mesh,
        in_specs=(
            P(("groups", "pair"), "filt", None, "corr"),
            P(("groups", "pair"), "filt"),
            P(),
            P("corr", None),
            P(),
        ),
        out_specs=P(("groups", "pair"), "corr", "filt"),
        check_vma=False,
    )
```

```python
import functools

import jax
import jax.numpy as jnp
from jax import lax
from jax.experimental import pallas as pl
from jax.experimental.pallas import tpu as pltpu
from jax.sharding import PartitionSpec as P

L = 75
TAPS = 64
DEC = 4
JP = 76
JPI = 76
TT = 512
RSUB = 32


def from_behind(block, axis, distance):
    devices = range(lax.axis_size(axis))
    route = [(i - distance, i) for i in devices if i - distance in devices]
    return lax.ppermute(block, axis, route)


def window_energy(rows, width):
    p1 = rows * rows
    p2 = p1[:, :-1] + p1[:, 1:]
    p4 = p2[:, :-2] + p2[:, 2:]
    p8 = p4[:, :-4] + p4[:, 4:]
    p16 = p8[:, :-8] + p8[:, 8:]
    p32 = p16[:, :-16] + p16[:, 16:]
    p64 = p32[:, :-32] + p32[:, 32:]
    return (
        p64[:, :width]
        + p8[:, 64 : 64 + width]
        + p2[:, 72 : 72 + width]
        + p1[:, 74 : 74 + width]
    )


def corr_kernel(f_ref, inv_ref, w_ref, o_ref, s_ref, *, row_block, tile):
    q = pl.program_id(1)
    span = tile + 128

    def fill(sub, carry):
        r0 = pl.multiple_of(sub * RSUB, RSUB)
        seg = f_ref[0, pl.ds(r0, RSUB), :].astype(jnp.float32)
        inv = inv_ref[pl.ds(r0, RSUB), :]
        for j in range(JP):
            moved = seg if j == 0 else pltpu.roll(seg, span - j, 1)
            piece = (moved[:, :tile] * inv).astype(jnp.bfloat16)
            s_ref[pl.ds(pl.multiple_of(j * row_block + r0, RSUB), RSUB), :] = piece
        return carry

    lax.fori_loop(0, row_block // RSUB, fill, 0)
    part = jnp.dot(w_ref[...], s_ref[...], preferred_element_type=jnp.float32)

    @pl.when(q == 0)
    def _():
        o_ref[...] = part

    @pl.when(q > 0)
    def _():
        o_ref[...] += part


def corr_kernel_interleaved(f_ref, inv_ref, w_ref, o_ref, s_ref, *, row_block, tile):
    span = tile + 128
    depth = JPI * RSUB
    part = None
    for sub in range(row_block // RSUB):
        r0 = sub * RSUB
        seg = f_ref[0, r0 : r0 + RSUB, :].astype(jnp.float32)
        inv = inv_ref[r0 : r0 + RSUB, :]
        for j in range(JPI):
            moved = seg if j == 0 else pltpu.roll(seg, span - j, 1)
            piece = (moved[:, :tile] * inv).astype(jnp.bfloat16)
            s_ref[sub * depth + j * RSUB : sub * depth + (j + 1) * RSUB, :] = piece
        step = jnp.dot(
            w_ref[:, sub * depth : (sub + 1) * depth],
            s_ref[sub * depth : (sub + 1) * depth, :],
            preferred_element_type=jnp.float32,
        )
        part = step if part is None else part + step
    o_ref[...] = part


def correlate(windows, inv, weights, row_block, interleaved=False):
    tiles, rows, span = windows.shape
    count = weights.shape[0]
    width = inv.shape[1]
    tile = width // tiles
    chunks = rows // row_block
    lags = JPI if interleaved else JP
    body_fn = corr_kernel_interleaved if interleaved else corr_kernel
    return pl.pallas_call(
        functools.partial(body_fn, row_block=row_block, tile=tile),
        grid=(tiles, chunks),
        in_specs=[
            pl.BlockSpec((1, row_block, span), lambda i, q: (i, q, 0)),
            pl.BlockSpec((row_block, tile), lambda i, q: (q, i)),
            pl.BlockSpec((count, lags * row_block), lambda i, q: (0, q)),
        ],
        out_specs=pl.BlockSpec((count, tile), lambda i, q: (0, i)),
        out_shape=jax.ShapeDtypeStruct((count, width), jnp.float32),
        scratch_shapes=[pltpu.VMEM((lags * row_block, tile), jnp.bfloat16)],
        compiler_params=pltpu.CompilerParams(
            dimension_semantics=("parallel", "arbitrary"),
            vmem_limit_bytes=48 * 1024 * 1024,
        ),
    )(windows, inv, weights)


def body(raw_rows, valid_counts, taps, templates, masks):
    samples = raw_rows[0]
    counts = valid_counts[0]
    local_stations = samples.shape[0]
    raw_width = samples.shape[2]
    corr_place = lax.axis_index("corr")
    filt_place = lax.axis_index("filt")
    filt_count = lax.axis_size("filt")
    sample_times = corr_place * raw_width + lax.iota(jnp.int32, raw_width)
    dense = samples.reshape(local_stations * 3, raw_width)
    limit = jnp.repeat(counts - corr_place * raw_width, 3)
    live = jnp.where(
        lax.iota(jnp.int32, raw_width)[None, :] < limit[:, None], dense, jnp.zeros_like(dense)
    )
    corr_count = lax.axis_size("corr")
    local_count = templates.shape[0]
    template_width = templates.shape[1]
    lanes = -(-template_width // 256) * 256
    wide = jnp.concatenate(
        [templates, jnp.zeros((local_count, lanes - template_width), templates.dtype)], axis=1
    )
    forward = [(i, (i + 1) % corr_count) for i in range(corr_count)]
    backward = [(i, (i - 1) % corr_count) for i in range(corr_count)]
    tail_rows = live.shape[0]
    sent = jnp.concatenate([live[:, raw_width - 128 :], wide.reshape(-1, 128)], axis=0)
    got = lax.ppermute(sent, "corr", forward)
    history = jnp.where(corr_place > 0, got[:tail_rows], jnp.zeros_like(got[:tail_rows]))
    from_previous = got[tail_rows:].reshape(local_count, lanes)
    sent = jnp.concatenate([live[:, :512], wide.reshape(-1, 512)], axis=0)
    got = lax.ppermute(sent, "corr", backward)
    ahead = jnp.where(corr_place < corr_count - 1, got[:tail_rows], jnp.zeros_like(got[:tail_rows]))
    from_next = got[tail_rows:].reshape(local_count, lanes)
    blocks_by_offset = {0: wide, 1: from_previous, corr_count - 1: from_next}
    for d in range(2, corr_count - 1):
        route = [(i, (i + d) % corr_count) for i in range(corr_count)]
        blocks_by_offset[d] = lax.ppermute(wide, "corr", route)
    by_offset = jnp.stack([blocks_by_offset[d] for d in range(corr_count)], axis=0)
    gathered_templates = jnp.concatenate(
        [
            lax.dynamic_index_in_dim(by_offset, (corr_place - b) % corr_count, 0, keepdims=False)
            for b in range(corr_count)
        ],
        axis=0,
    )[:, :template_width]
    decimated = raw_width // DEC
    blocks = decimated // 128 + 1
    rows_in = live.shape[0]
    flip = (lax.iota(jnp.int32, TAPS)[:, None] + lax.iota(jnp.int32, TAPS)[None, :] == TAPS - 1)
    reversed_taps = jnp.dot(
        taps[None, :], flip.astype(taps.dtype), preferred_element_type=jnp.float32
    )[0].astype(taps.dtype)
    ring = jnp.concatenate(
        [jnp.zeros((65,), taps.dtype), reversed_taps, jnp.zeros((644 - 129,), taps.dtype)]
    )
    bank = jnp.tile(ring, 128)[: 128 * 640].reshape(128, 640)

    def apply_bank(frames):
        return lax.dot_general(
            frames, bank, (((1,), (1,)), ((), ())), preferred_element_type=jnp.float32
        )

    inner = jnp.stack(
        [live[:, 512 * a - 128 : 512 * a + 512] for a in range(1, blocks - 1)], axis=1
    ).reshape(rows_in * (blocks - 2), 640)
    inner = apply_bank(inner).reshape(rows_in, (blocks - 2) * 128)
    first = apply_bank(jnp.concatenate([history, live[:, :512]], axis=1))
    last = apply_bank(jnp.concatenate([live[:, raw_width - 128 :], ahead], axis=1))
    filtered = jnp.concatenate([first, inner, last], axis=1)
    filtered = filtered.astype(jnp.bfloat16).reshape(local_stations * 3, decimated + 128)
    past_end = (corr_place == corr_count - 1) & (lax.iota(jnp.int32, decimated + 128) >= decimated)
    filtered = jnp.where(past_end[None, :], jnp.zeros_like(filtered), filtered)
    per_block = corr_count // filt_count
    block = per_block * decimated
    width = block // corr_count
    span = width + 128
    received = []
    for k in range(filt_count):
        piece = (filt_place + k) % filt_count
        part = lax.dynamic_slice_in_dim(filtered, piece * width, span, 1)
        route = []
        for c in range(corr_count):
            for f in range(filt_count):
                dest = ((c % per_block) * filt_count + (f + k) % filt_count) * filt_count + c // per_block
                route.append((c * filt_count + f, dest))
        received.append(lax.ppermute(part, ("corr", "filt"), route))
    rows = jnp.concatenate(received, axis=0)
    energy = window_energy(rows.astype(jnp.float32), width)
    inv = lax.rsqrt(jnp.maximum(energy, 1.0))
    tile = min(TT, width)
    tiles = width // tile
    windows = jnp.stack([rows[:, i * tile : i * tile + tile + 128] for i in range(tiles)], axis=0)

    templates = gathered_templates
    count = templates.shape[0]
    stations = masks.shape[2]
    shaped = templates.astype(jnp.float32).reshape(count, 3, L)
    norms = jnp.sqrt(jnp.sum(shaped * shaped, axis=2) + 1e-06)
    base = shaped / norms[:, :, None]
    arrival = (corr_place - lax.iota(jnp.int32, filt_count)) % filt_count
    blocked = masks.reshape(count, 3, filt_count, stations // filt_count)
    if filt_count == 2:
        swapped = jnp.concatenate([blocked[:, :, 1:], blocked[:, :, :1]], axis=2)
        chosen = jnp.where(arrival[0] == 0, blocked, swapped)
    else:
        chosen = jnp.take(blocked, arrival, axis=2)
    chosen = chosen.reshape(count, 3, stations).astype(jnp.float32)
    total_rows = stations * 3
    row_block = 96 if total_rows % 96 == 0 else total_rows
    chunks = total_rows // row_block
    if chunks == 1:
        padded = jnp.concatenate([base, jnp.zeros((count, 3, JPI - L), base.dtype)], axis=2)
        padded = padded.astype(jnp.bfloat16).reshape(count, 3 * JPI)
        flat = jnp.transpose(chosen, (0, 1, 2)).reshape(count, total_rows).astype(jnp.bfloat16)
        start_zero = lax.optimization_barrier(jnp.zeros((), jnp.int32))
        column = lax.iota(jnp.int32, JPI * total_rows) + start_zero
        group = column // (JPI * RSUB)
        lag = (column % (JPI * RSUB)) // RSUB
        row = group * RSUB + column % RSUB
        source = lax.iota(jnp.int32, 3 * JPI)
        pick_base = (
            (source[:, None] % JPI == lag[None, :]) & (source[:, None] // JPI == row[None, :] % 3)
        ).astype(jnp.bfloat16)
        slot = lax.iota(jnp.int32, total_rows)
        pick_mask = (
            (slot[:, None] // stations == row[None, :] % 3)
            & (slot[:, None] % stations == row[None, :] // 3)
        ).astype(jnp.bfloat16)
        spread = jnp.dot(padded, pick_base, preferred_element_type=jnp.float32)
        gate = jnp.dot(flat, pick_mask, preferred_element_type=jnp.float32)
        weights = (spread * gate).astype(jnp.bfloat16)
    else:
        full = jnp.transpose(base, (0, 2, 1))[:, :, None, :] * jnp.transpose(chosen, (0, 2, 1))[:, None, :, :]
        full = full.astype(jnp.bfloat16).reshape(count, L, stations * 3)
        full = jnp.concatenate([full, jnp.zeros((count, JP - L, stations * 3), full.dtype)], axis=1)
        weights = (
            full.reshape(count, JP, chunks, row_block)
            .transpose(0, 2, 1, 3)
            .reshape(count, chunks * JP * row_block)
        )
    stacked = correlate(windows, inv, weights, row_block, interleaved=chunks == 1)
    pieces = [lax.dynamic_slice_in_dim(stacked, corr_place * local_count, local_count, 0)]
    for d in range(1, corr_count):
        target = (corr_place + d) % corr_count
        part = lax.dynamic_slice_in_dim(stacked, target * local_count, local_count, 0)
        route = [(i, (i + d) % corr_count) for i in range(corr_count)]
        pieces.append(lax.ppermute(part, "corr", route))
    stacked = jnp.zeros((local_count, corr_count * width), jnp.float32)
    for d, part in enumerate(pieces):
        place = ((corr_place - d) % corr_count) * width
        stacked = lax.dynamic_update_slice_in_dim(stacked, part, place, 1)
    return stacked[None]


def solution(mesh):
    return jax.shard_map(
        body,
        mesh=mesh,
        in_specs=(
            P(("groups", "pair"), "filt", None, "corr"),
            P(("groups", "pair"), "filt"),
            P(),
            P("corr", None),
            P(),
        ),
        out_specs=P(("groups", "pair"), "corr", "filt"),
        check_vma=False,
    )
```
